32 devices in a mesh: veh: 8 (over z, x), req: 4 (over y, core).
Axes of the slice: x: 2, y: 2, z: 4, core: 2. Of those that a mesh axis runs over, the one named last changes fastest.
Arguments:
- vehicle_emb: bfloat16 [8192, 128], P(('veh', 'req')), may hold values from -40 to 40
- request_emb: bfloat16 [16384, 128], P('req'), may hold values from -8 to 8
- request_feat: bfloat16 [16384, 256], P('req'), may hold values from -6 to 6
- log_supply: float32 [8192], P('veh'), may hold values from -1.2 to 1.2
- log_demand: float32 [16384], P('req'), may hold values from -1.2 to 1.2
Outputs:
- assigned: float32 [8192, 256], P(('veh', 'req'))
The draws below stay inside these ranges and needn't reach their ends.
All inputs are finite; a program needn't handle non-finite values.
Results may differ from the reference program's by a relative error of at most 0.0017.
Values may be sent and summed in bfloat16 or wider, within the bound.
No kernel may reach another device: no remote copies, remote signals or barrier semaphores. Data moves between devices by JAX's collectives and lax.ppermute only.
A program may use at most 64 MiB of HBM per device.

```python
import math
import jax
import jax.numpy as jnp
from jax import lax

E = 128
F = 256
REQ_DEV = 4096
VEHICLES = 8192
REQUESTS = 16384
N_REQ = 4


def shared_embeddings(key):
    base_key = jax.random.fold_in(key, 11)
    key_req, key_veh = jax.random.split(base_key, 2)
    requests = jax.random.normal(key_req, (REQUESTS, E), jnp.float32)
    vehicles = jax.random.normal(key_veh, (VEHICLES, E), jnp.float32)
    return (jnp.clip(vehicles, -40.0, 40.0), jnp.clip(requests, -8.0, 8.0))


def draw_vehicle_emb(key, part):
    return shared_embeddings(key)[0].astype(jnp.bfloat16)


def draw_request_emb(key, part):
    return shared_embeddings(key)[1].astype(jnp.bfloat16)


def steps_of(own_key, shape, shards, smallest, top_value):
    loudness = 1.0
    for dim, parts in shards:
        draws = jax.random.uniform(jax.random.fold_in(jax.random.fold_in(own_key, 6), dim), (parts,), jnp.float32, smallest / len(shards), top_value / len(shards))
        loudness = loudness * jnp.repeat(jnp.exp(draws), shape[dim] // parts).reshape((-1,) + (1,) * (len(shape) - 1 - dim))
    return loudness


def scatter_about(key, dims, spread, bound, pieces=(), kind=jnp.bfloat16):
    factor_of = steps_of(key, dims, pieces, -0.22, 0.18) if pieces else 1.0
    values = jax.random.normal(key, dims, jnp.float32) * spread * factor_of
    return jnp.minimum(jnp.maximum(values, -bound), bound).astype(kind)


def setup_inputs(seed: int = 0) -> dict:
    streams_of = jax.random.split(jax.random.key(seed), 6)
    vehicle_emb = draw_vehicle_emb(jax.random.fold_in(streams_of[5], 71), 0)
    request_emb = draw_request_emb(jax.random.fold_in(streams_of[5], 71), 0)
    request_feat = scatter_about(streams_of[2], (REQUESTS, F), 1.0, 6.0, ((0, 4),))
    log_supply = jnp.clip(jax.random.uniform(streams_of[3], (VEHICLES,), jnp.float32, -1.2, 1.2) * steps_of(streams_of[3], (VEHICLES,), ((0, 8),), -0.4, 0.0), -1.2, 1.2)
    log_demand = jnp.clip(jax.random.uniform(streams_of[4], (REQUESTS,), jnp.float32, -1.2, 1.2) * steps_of(streams_of[4], (REQUESTS,), ((0, 4),), -0.4, 0.0), -1.2, 1.2)
    return dict(vehicle_emb=vehicle_emb, request_emb=request_emb, request_feat=request_feat, log_supply=log_supply, log_demand=log_demand)


def block_scores(vehicle_block, request_emb):
    score_scale = 3.0 / math.sqrt(E)
    return lax.dot_general(vehicle_block, request_emb, (((1,), (1,)), ((), ())), preferred_element_type=jnp.float32) * score_scale

def reference(vehicle_emb, request_emb, request_feat, log_supply, log_demand):
    block_rows = min(1024, VEHICLES)
    block_count = VEHICLES // block_rows
    vehicle_blocks = vehicle_emb.reshape(block_count, block_rows, E)

    def column_lse(shift):
        shift_blocks = shift.reshape(block_count, block_rows)

        def column_step(state_pair, element):
            running, accrued = state_pair
            vehicle_block, shift_block = element
            logits = block_scores(vehicle_block, request_emb) + shift_block[:, None]
            highest = jnp.maximum(running, lax.optimization_barrier(jnp.max(logits, axis=0)))
            accrued = accrued * jnp.exp(running - highest) + lax.optimization_barrier(jnp.sum(jnp.exp(logits - highest[None, :]), axis=0))
            return ((highest, accrued), None)
        start_pair = (jnp.full((REQUESTS,), -1e+30, jnp.float32), jnp.zeros((REQUESTS,), jnp.float32))
        (highest, accrued), unused = lax.scan(column_step, start_pair, (vehicle_blocks, shift_blocks))
        return highest + jnp.log(accrued)

    def row_lse(potential):

        def row_block(vehicle_block):
            logits = block_scores(vehicle_block, request_emb) + potential[None, :]
            highest = lax.optimization_barrier(jnp.max(logits, axis=1))
            return highest + jnp.log(lax.optimization_barrier(jnp.sum(jnp.exp(logits - highest[:, None]), axis=1)))
        return lax.map(row_block, vehicle_blocks).reshape(VEHICLES)
    demand_first = log_demand - column_lse(jnp.zeros((VEHICLES,), jnp.float32))
    supply_pot = log_supply - row_lse(demand_first)
    demand_second = log_demand - column_lse(supply_pot)
    feat_blocks = request_feat.astype(jnp.float32).reshape(N_REQ, REQ_DEV, F)

    def assign_block(vehicle_block):
        logits = block_scores(vehicle_block, request_emb) + demand_second[None, :]
        logits = logits.reshape(block_rows, N_REQ, REQ_DEV)
        block_peak = lax.optimization_barrier(jnp.max(logits, axis=2))
        powers = jnp.exp(logits - block_peak[:, :, None])
        block_mass = lax.optimization_barrier(jnp.sum(powers, axis=2))
        weights = lax.optimization_barrier(powers.astype(jnp.bfloat16)).astype(jnp.float32)
        block_feat = jnp.einsum('bnr,nrf->bnf', weights, feat_blocks, precision=lax.Precision.HIGHEST)
        row_top = lax.optimization_barrier(jnp.max(block_peak, axis=1))
        factor = jnp.exp(block_peak - row_top[:, None])
        numerator = lax.optimization_barrier(jnp.sum(block_feat * factor[:, :, None], axis=1))
        denominator = lax.optimization_barrier(jnp.sum(block_mass * factor, axis=1))
        return numerator / denominator[:, None]
    return lax.map(assign_block, vehicle_blocks).reshape(VEHICLES, F)
```

```python
import math

import jax
import jax.numpy as jnp
from jax import lax
from jax.sharding import PartitionSpec as P


def gather_by_exchange(x, axis):
    count = lax.axis_size(axis)
    spread = jnp.broadcast_to(x[None], (count,) + x.shape)
    return lax.all_to_all(spread, axis, 0, 0, tiled=True)


def merge_lse(parts):
    top = jnp.max(parts, axis=0)
    return top + jnp.log(jnp.sum(jnp.exp(parts - top[None]), axis=0))


def local(vehicle_emb, request_emb, request_feat, log_supply, log_demand):
    own_rows = lax.all_gather(vehicle_emb, "req", axis=0, tiled=True)
    row_count = own_rows.shape[0]
    block_rows = min(256, row_count)
    block_count = row_count // block_rows
    vehicle_blocks = own_rows.reshape(block_count, block_rows, own_rows.shape[1])
    score_scale = 3.0 / math.sqrt(own_rows.shape[1])
    request_count = request_emb.shape[0]

    def block_scores(vehicle_block):
        return (
            lax.dot_general(
                vehicle_block,
                request_emb,
                (((1,), (1,)), ((), ())),
                preferred_element_type=jnp.float32,
            )
            * score_scale
        )

    def column_pot(shift):
        shift_blocks = shift.reshape(block_count, block_rows)

        def column_step(state_pair, element):
            running, accrued = state_pair
            vehicle_block, shift_block = element
            logits = block_scores(vehicle_block) + shift_block[:, None]
            highest = jnp.maximum(running, jnp.max(logits, axis=0))
            accrued = accrued * jnp.exp(running - highest) + jnp.sum(
                jnp.exp(logits - highest[None, :]), axis=0
            )
            return ((highest, accrued), None)

        start_pair = (
            jnp.full((request_count,), -1e30, jnp.float32),
            jnp.zeros((request_count,), jnp.float32),
        )
        (highest, accrued), unused = lax.scan(
            column_step, start_pair, (vehicle_blocks, shift_blocks)
        )
        partial = highest + jnp.log(accrued)
        return log_demand - merge_lse(gather_by_exchange(partial, "veh"))

    demand_first = column_pot(jnp.zeros((row_count,), jnp.float32))

    def row_block(vehicle_block):
        logits = block_scores(vehicle_block) + demand_first[None, :]
        highest = jnp.max(logits, axis=1)
        return highest + jnp.log(jnp.sum(jnp.exp(logits - highest[:, None]), axis=1))

    partial = lax.map(row_block, vehicle_blocks).reshape(row_count)
    parts = lax.all_gather(partial, "req", axis=0, tiled=False)
    supply_pot = log_supply - merge_lse(parts)
    demand_second = column_pot(supply_pot)

    def assign_block(vehicle_block):
        logits = block_scores(vehicle_block) + demand_second[None, :]
        block_peak = jnp.max(logits, axis=1)
        powers = jnp.exp(logits - block_peak[:, None])
        block_mass = jnp.sum(powers, axis=1)
        weights = powers.astype(jnp.bfloat16)
        block_feat = jnp.dot(weights, request_feat, preferred_element_type=jnp.float32)
        return (block_peak, block_mass, block_feat)

    peaks, masses, features = lax.map(assign_block, vehicle_blocks)
    peaks = peaks.reshape(row_count)
    masses = masses.reshape(row_count)
    features = features.reshape(row_count, request_feat.shape[1])
    summit = lax.pmax(peaks, "req")
    factor = jnp.exp(peaks - summit)
    own_feat, own_mass = (
        lax.psum_scatter(features * factor[:, None], "req", scatter_dimension=0, tiled=True),
        lax.psum_scatter(masses * factor, "req", scatter_dimension=0, tiled=True),
    )
    result = own_feat / own_mass[:, None]
    return result


def solution(mesh):
    in_specs = (P(("veh", "req"), None), P("req", None), P("req", None), P("veh"), P("req"))
    out_specs = P(("veh", "req"), None)
    return jax.shard_map(local, mesh=mesh, in_specs=in_specs, out_specs=out_specs, check_vma=False)
```

```python
import functools
import math

import jax
import jax.numpy as jnp
from jax import lax
from jax.experimental import pallas as pl
from jax.sharding import PartitionSpec as P


def gather_by_exchange(x, axis):
    count = lax.axis_size(axis)
    spread = jnp.broadcast_to(x[None], (count,) + x.shape)
    return lax.all_to_all(spread, axis, 0, 0, tiled=True)


def merge_lse(parts):
    top = jnp.max(parts, axis=0)
    return top + jnp.log(jnp.sum(jnp.exp(parts - top[None]), axis=0))


def lse_kernel(a_ref, shift_ref, b_ref, out_ref, *, scale):
    scores = lax.dot_general(
        a_ref[...], b_ref[...], (((1,), (1,)), ((), ())), preferred_element_type=jnp.float32
    )
    logits = scores * scale + shift_ref[...]
    top = jnp.max(logits, axis=0, keepdims=True)
    total = jnp.sum(jnp.exp(logits - top), axis=0, keepdims=True)
    out_ref[...] = top + jnp.log(total)


def lse_over_rows(a, shift, b, scale, tile):
    rows, width = a.shape
    cols = b.shape[0]
    tile = min(tile, cols)
    return pl.pallas_call(
        functools.partial(lse_kernel, scale=scale),
        out_shape=jax.ShapeDtypeStruct((1, cols), jnp.float32),
        grid=(cols // tile,),
        in_specs=[
            pl.BlockSpec((rows, width), lambda j: (0, 0)),
            pl.BlockSpec((rows, 1), lambda j: (0, 0)),
            pl.BlockSpec((tile, width), lambda j: (j, 0)),
        ],
        out_specs=pl.BlockSpec((1, tile), lambda j: (0, j)),
        cost_estimate=pl.CostEstimate(
            flops=2 * rows * cols * width + 5 * rows * cols,
            transcendentals=rows * cols,
            bytes_accessed=2 * (rows + cols) * width + 4 * (rows + cols),
        ),
    )(a, shift.reshape(rows, 1), b)[0]


def assign_kernel(v_ref, r_ref, d_ref, f_ref, peak_ref, mass_ref, feat_ref, *, scale):
    scores = lax.dot_general(
        v_ref[...], r_ref[...], (((1,), (1,)), ((), ())), preferred_element_type=jnp.float32
    )
    logits = scores * scale + d_ref[...]
    top = jnp.max(logits, axis=1, keepdims=True)
    powers = jnp.exp(logits - top)
    peak_ref[...] = top
    mass_ref[...] = jnp.sum(powers, axis=1, keepdims=True)
    feat_ref[...] = jnp.dot(
        powers.astype(jnp.bfloat16), f_ref[...], preferred_element_type=jnp.float32
    )


def assign_rows(v, r, d, f, scale, tile):
    rows, width = v.shape
    cols, feat = f.shape
    tile = min(tile, rows)
    return pl.pallas_call(
        functools.partial(assign_kernel, scale=scale),
        out_shape=(
            jax.ShapeDtypeStruct((rows, 1), jnp.float32),
            jax.ShapeDtypeStruct((rows, 1), jnp.float32),
            jax.ShapeDtypeStruct((rows, feat), jnp.float32),
        ),
        grid=(rows // tile,),
        in_specs=[
            pl.BlockSpec((tile, width), lambda i: (i, 0)),
            pl.BlockSpec((cols, width), lambda i: (0, 0)),
            pl.BlockSpec((1, cols), lambda i: (0, 0)),
            pl.BlockSpec((cols, feat), lambda i: (0, 0)),
        ],
        out_specs=(
            pl.BlockSpec((tile, 1), lambda i: (i, 0)),
            pl.BlockSpec((tile, 1), lambda i: (i, 0)),
            pl.BlockSpec((tile, feat), lambda i: (i, 0)),
        ),
        cost_estimate=pl.CostEstimate(
            flops=2 * rows * cols * (width + feat) + 5 * rows * cols,
            transcendentals=rows * cols,
            bytes_accessed=2 * (rows + cols) * width + 2 * cols * feat + 4 * rows * (feat + 2),
        ),
    )(v, r, d.reshape(1, cols), f)


def local(vehicle_emb, request_emb, request_feat, log_supply, log_demand):
    own_rows = lax.all_gather(vehicle_emb, "req", axis=0, tiled=True)
    row_count = own_rows.shape[0]
    scale = 3.0 / math.sqrt(own_rows.shape[1])

    def column_pot(shift):
        partial = lse_over_rows(own_rows, shift, request_emb, scale, 512)
        return log_demand - merge_lse(gather_by_exchange(partial, "veh"))

    demand_first = column_pot(jnp.zeros((row_count,), jnp.float32))
    partial = lse_over_rows(request_emb, demand_first, own_rows, scale, 256)
    parts = lax.all_gather(partial, "req", axis=0, tiled=False)
    supply_pot = log_supply - merge_lse(parts)
    demand_second = column_pot(supply_pot)

    peaks, masses, features = assign_rows(
        own_rows, request_emb, demand_second, request_feat, scale, 128
    )
    peaks = peaks[:, 0]
    masses = masses[:, 0]
    summit = lax.pmax(peaks, "req")
    factor = jnp.exp(peaks - summit)
    own_feat, own_mass = (
        lax.psum_scatter(features * factor[:, None], "req", scatter_dimension=0, tiled=True),
        lax.psum_scatter(masses * factor, "req", scatter_dimension=0, tiled=True),
    )
    return own_feat / own_mass[:, None]


def solution(mesh):
    in_specs = (P(("veh", "req"), None), P("req", None), P("req", None), P("veh"), P("req"))
    out_specs = P(("veh", "req"), None)
    return jax.shard_map(local, mesh=mesh, in_specs=in_specs, out_specs=out_specs, check_vma=False)
```

```python
import functools
import math

import jax
import jax.numpy as jnp
from jax import lax
from jax.experimental import pallas as pl
from jax.sharding import PartitionSpec as P


def gather_by_exchange(x, axis):
    count = lax.axis_size(axis)
    spread = jnp.broadcast_to(x[None], (count,) + x.shape)
    return lax.all_to_all(spread, axis, 0, 0, tiled=True)


def merge_lse(parts):
    top = jnp.max(parts, axis=0)
    return top + jnp.log(jnp.sum(jnp.exp(parts - top[None]), axis=0))


def lse_kernel(a_ref, shift_ref, b_ref, out_ref, *, scale):
    scores = lax.dot_general(
        a_ref[...], b_ref[...], (((1,), (1,)), ((), ())), preferred_element_type=jnp.float32
    )
    logits = scores * scale + shift_ref[...]
    top = jnp.max(logits, axis=0, keepdims=True)
    total = jnp.sum(jnp.exp(logits - top), axis=0, keepdims=True)
    out_ref[...] = top + jnp.log(total)


def lse_over_rows(a, shift, b, scale, tile):
    rows, width = a.shape
    cols = b.shape[0]
    tile = min(tile, cols)
    return pl.pallas_call(
        functools.partial(lse_kernel, scale=scale),
        out_shape=jax.ShapeDtypeStruct((1, cols), jnp.float32),
        grid=(cols // tile,),
        in_specs=[
            pl.BlockSpec((rows, width), lambda j: (0, 0)),
            pl.BlockSpec((rows, 1), lambda j: (0, 0)),
            pl.BlockSpec((tile, width), lambda j: (j, 0)),
        ],
        out_specs=pl.BlockSpec((1, tile), lambda j: (0, j)),
        cost_estimate=pl.CostEstimate(
            flops=2 * rows * cols * width + 5 * rows * cols,
            transcendentals=rows * cols,
            bytes_accessed=2 * (rows + cols) * width + 4 * (rows + cols),
        ),
    )(a, shift.reshape(rows, 1), b)[0]


def assign_kernel(v_ref, r_ref, d_ref, f_ref, out_ref, *, scale):
    scores = lax.dot_general(
        v_ref[...], r_ref[...], (((1,), (1,)), ((), ())), preferred_element_type=jnp.float32
    )
    logits = scores * scale + d_ref[...]
    top = jnp.max(logits, axis=1, keepdims=True)
    powers = jnp.exp(logits - top)
    mass = jnp.sum(powers, axis=1, keepdims=True)
    feat = f_ref.shape[1]
    out_ref[:, :feat] = jnp.dot(
        powers.astype(jnp.bfloat16), f_ref[...], preferred_element_type=jnp.float32
    )
    lane = lax.broadcasted_iota(jnp.int32, (top.shape[0], 128), 1)
    out_ref[:, feat:] = jnp.where(lane == 0, mass, jnp.where(lane == 1, top, 0.0))


def assign_rows(v, r, d, f, scale, tile):
    rows, width = v.shape
    cols, feat = f.shape
    tile = min(tile, rows)
    return pl.pallas_call(
        functools.partial(assign_kernel, scale=scale),
        out_shape=jax.ShapeDtypeStruct((rows, feat + 128), jnp.float32),
        grid=(rows // tile,),
        in_specs=[
            pl.BlockSpec((tile, width), lambda i: (i, 0)),
            pl.BlockSpec((cols, width), lambda i: (0, 0)),
            pl.BlockSpec((1, cols), lambda i: (0, 0)),
            pl.BlockSpec((cols, feat), lambda i: (0, 0)),
        ],
        out_specs=pl.BlockSpec((tile, feat + 128), lambda i: (i, 0)),
        cost_estimate=pl.CostEstimate(
            flops=2 * rows * cols * (width + feat) + 5 * rows * cols,
            transcendentals=rows * cols,
            bytes_accessed=2 * (rows + cols) * width + 2 * cols * feat + 4 * rows * (feat + 2),
        ),
    )(v, r, d.reshape(1, cols), f)


def local(vehicle_emb, request_emb, request_feat, log_supply, log_demand):
    own_rows = lax.all_gather(vehicle_emb, "req", axis=0, tiled=True)
    row_count = own_rows.shape[0]
    scale = 3.0 / math.sqrt(own_rows.shape[1])

    def column_pot(shift):
        partial = lse_over_rows(own_rows, shift, request_emb, scale, 512)
        return log_demand - merge_lse(gather_by_exchange(partial, "veh"))

    demand_first = column_pot(jnp.zeros((row_count,), jnp.float32))
    partial = lse_over_rows(request_emb, demand_first, own_rows, scale, 256)
    parts = lax.all_gather(partial, "req", axis=0, tiled=False)
    supply_pot = log_supply - merge_lse(parts)
    demand_second = column_pot(supply_pot)

    packed = assign_rows(own_rows, request_emb, demand_second, request_feat, scale, 128)
    owners = lax.axis_size("req")
    feat = request_feat.shape[1]
    packed = packed.reshape(owners, row_count // owners, feat + 128)
    arrived = lax.all_to_all(packed, "req", 0, 0, tiled=True)
    peaks = arrived[:, :, feat + 1]
    masses = arrived[:, :, feat]
    factor = jnp.exp(peaks - jnp.max(peaks, axis=0, keepdims=True))
    numerator = jnp.sum(arrived[:, :, :feat] * factor[:, :, None], axis=0)
    denominator = jnp.sum(masses * factor, axis=0)
    return numerator / denominator[:, None]


def solution(mesh):
    in_specs = (P(("veh", "req"), None), P("req", None), P("req", None), P("veh"), P("req"))
    out_specs = P(("veh", "req"), None)
    return jax.shard_map(local, mesh=mesh, in_specs=in_specs, out_specs=out_specs, check_vma=False)
```

```python
import functools
import math

import jax
import jax.numpy as jnp
from jax import lax
from jax.experimental import pallas as pl
from jax.experimental.pallas import tpu as pltpu
from jax.sharding import PartitionSpec as P


def gather_by_exchange(x, axis):
    count = lax.axis_size(axis)
    spread = jnp.broadcast_to(x[None], (count,) + x.shape)
    return lax.all_to_all(spread, axis, 0, 0, tiled=True)


def merge_lse(parts):
    top = jnp.max(parts, axis=0)
    return top + jnp.log(jnp.sum(jnp.exp(parts - top[None]), axis=0))


def lse_kernel(a_ref, shift_ref, b_ref, out_ref, *, scale):
    scores = lax.dot_general(
        a_ref[...], b_ref[...], (((1,), (1,)), ((), ())), preferred_element_type=jnp.float32
    )
    logits = scores * scale + shift_ref[...]
    top = jnp.max(logits, axis=0, keepdims=True)
    total = jnp.sum(jnp.exp(logits - top), axis=0, keepdims=True)
    out_ref[...] = top + jnp.log(total)


def lse_over_rows(a, shift, b, scale, tile):
    rows, width = a.shape
    cols = b.shape[0]
    tile = min(tile, cols)
    return pl.pallas_call(
        functools.partial(lse_kernel, scale=scale),
        out_shape=jax.ShapeDtypeStruct((1, cols), jnp.float32),
        grid=(cols // tile,),
        in_specs=[
            pl.BlockSpec((rows, width), lambda j: (0, 0)),
            pl.BlockSpec((rows, 1), lambda j: (0, 0)),
            pl.BlockSpec((tile, width), lambda j: (j, 0)),
        ],
        out_specs=pl.BlockSpec((1, tile), lambda j: (0, j)),
        cost_estimate=pl.CostEstimate(
            flops=2 * rows * cols * width + 5 * rows * cols,
            transcendentals=rows * cols,
            bytes_accessed=2 * (rows + cols) * width + 4 * (rows + cols),
        ),
    )(a, shift.reshape(rows, 1), b)[0]


def assign_kernel(rot_ref, v_ref, r_ref, d_ref, f_ref, out_ref, *, scale):
    scores = lax.dot_general(
        v_ref[...], r_ref[...], (((1,), (1,)), ((), ())), preferred_element_type=jnp.float32
    )
    logits = scores * scale + d_ref[...]
    top = jnp.max(logits, axis=1, keepdims=True)
    powers = jnp.exp(logits - top)
    mass = jnp.sum(powers, axis=1, keepdims=True)
    feat = f_ref.shape[1]
    block_feat = jnp.dot(
        powers.astype(jnp.bfloat16), f_ref[...], preferred_element_type=jnp.float32
    )
    out_ref[:feat, :] = block_feat.T
    lane = lax.broadcasted_iota(jnp.int32, (top.shape[0], 128), 1)
    extra = jnp.where(lane == 0, mass, jnp.where(lane == 1, top, 0.0))
    out_ref[feat:, :] = extra.T[:8, :]


def assign_rows(v, r, d, f, scale, tile, rotation):
    rows, width = v.shape
    cols, feat = f.shape
    tile = min(tile, rows)
    tiles = rows // tile
    grid_spec = pltpu.PrefetchScalarGridSpec(
        num_scalar_prefetch=1,
        grid=(tiles,),
        in_specs=[
            pl.BlockSpec((tile, width), lambda i, rot: ((i + rot[0]) % tiles, 0)),
            pl.BlockSpec((cols, width), lambda i, rot: (0, 0)),
            pl.BlockSpec((1, cols), lambda i, rot: (0, 0)),
            pl.BlockSpec((cols, feat), lambda i, rot: (0, 0)),
        ],
        out_specs=pl.BlockSpec((feat + 8, tile), lambda i, rot: (0, i)),
    )
    return pl.pallas_call(
        functools.partial(assign_kernel, scale=scale),
        out_shape=jax.ShapeDtypeStruct((feat + 8, rows), jnp.float32),
        grid_spec=grid_spec,
        cost_estimate=pl.CostEstimate(
            flops=2 * rows * cols * (width + feat) + 5 * rows * cols,
            transcendentals=rows * cols,
            bytes_accessed=2 * (rows + cols) * width + 2 * cols * feat + 4 * rows * (feat + 8),
        ),
    )(rotation, v, r, d.reshape(1, cols), f)


def local(vehicle_emb, request_emb, request_feat, log_supply, log_demand):
    placed = lax.dynamic_update_slice_in_dim(
        jnp.zeros((lax.axis_size("req") * vehicle_emb.shape[0], vehicle_emb.shape[1]), vehicle_emb.dtype),
        vehicle_emb,
        lax.axis_index("req") * vehicle_emb.shape[0],
        axis=0,
    )
    own_rows = lax.psum(placed, "req")
    row_count = own_rows.shape[0]
    scale = 3.0 / math.sqrt(own_rows.shape[1])

    def column_pot(shift):
        partial = lse_over_rows(own_rows, shift, request_emb, scale, 512)
        return log_demand - merge_lse(gather_by_exchange(partial, "veh"))

    demand_first = column_pot(jnp.zeros((row_count,), jnp.float32))
    partial = lse_over_rows(request_emb, demand_first, own_rows, scale, 256)
    parts = lax.all_gather(partial, "req", axis=0, tiled=False)
    supply_pot = log_supply - merge_lse(parts)
    demand_second = column_pot(supply_pot)

    owners = lax.axis_size("req")
    chunk = row_count // owners
    tile = min(128, chunk)
    me = lax.axis_index("req")
    rotation = jnp.reshape(me * (chunk // tile), (1,)).astype(jnp.int32)
    packed = assign_rows(own_rows, request_emb, demand_second, request_feat, scale, tile, rotation)
    feat = request_feat.shape[1]
    pieces = [packed[:, :chunk]]
    for step in range(1, owners):
        pieces.append(
            lax.ppermute(
                packed[:, step * chunk : (step + 1) * chunk],
                "req",
                [(i, (i + step) % owners) for i in range(owners)],
            )
        )
    arrived = jnp.stack(pieces)
    peaks = arrived[:, feat + 1, :]
    masses = arrived[:, feat, :]
    factor = jnp.exp(peaks - jnp.max(peaks, axis=0, keepdims=True))
    numerator = jnp.sum(arrived[:, :feat, :] * factor[:, None, :], axis=0)
    denominator = jnp.sum(masses * factor, axis=0)
    return (numerator / denominator[None, :]).T


def solution(mesh):
    in_specs = (P(("veh", "req"), None), P("req", None), P("req", None), P("veh"), P("req"))
    out_specs = P(("veh", "req"), None)
    return jax.shard_map(local, mesh=mesh, in_specs=in_specs, out_specs=out_specs, check_vma=False)
```

```python
import functools
import math

import jax
import jax.numpy as jnp
from jax import lax
from jax.experimental import pallas as pl
from jax.experimental.pallas import tpu as pltpu
from jax.sharding import PartitionSpec as P


def gather_by_exchange(x, axis):
    count = lax.axis_size(axis)
    spread = jnp.broadcast_to(x[None], (count,) + x.shape)
    return lax.all_to_all(spread, axis, 0, 0, tiled=True)


def merge_lse(parts):
    top = jnp.max(parts, axis=0)
    return top + jnp.log(jnp.sum(jnp.exp(parts - top[None]), axis=0))


def lse_kernel(a_ref, shift_ref, b_ref, out_ref, *, scale):
    scores = lax.dot_general(
        a_ref[...], b_ref[...], (((1,), (1,)), ((), ())), preferred_element_type=jnp.float32
    )
    logits = scores * scale + shift_ref[...]
    top = jnp.max(logits, axis=0, keepdims=True)
    total = jnp.sum(jnp.exp(logits - top), axis=0, keepdims=True)
    out_ref[...] = top + jnp.log(total)


def lse_over_rows(a, shift, b, scale, tile):
    rows, width = a.shape
    cols = b.shape[0]
    tile = min(tile, cols)
    return pl.pallas_call(
        functools.partial(lse_kernel, scale=scale),
        out_shape=jax.ShapeDtypeStruct((1, cols), jnp.float32),
        grid=(cols // tile,),
        in_specs=[
            pl.BlockSpec((rows, width), lambda j: (0, 0)),
            pl.BlockSpec((rows, 1), lambda j: (0, 0)),
            pl.BlockSpec((tile, width), lambda j: (j, 0)),
        ],
        out_specs=pl.BlockSpec((1, tile), lambda j: (0, j)),
        cost_estimate=pl.CostEstimate(
            flops=2 * rows * cols * width + 5 * rows * cols,
            transcendentals=rows * cols,
            bytes_accessed=2 * (rows + cols) * width + 4 * (rows + cols),
        ),
    )(a, shift.reshape(rows, 1), b)[0]


def assign_kernel(rot_ref, v_ref, r_ref, d_ref, f_ref, out_ref, *, scale):
    scores = lax.dot_general(
        v_ref[...], r_ref[...], (((1,), (1,)), ((), ())), preferred_element_type=jnp.float32
    )
    logits = scores * scale + d_ref[...]
    top = jnp.max(logits, axis=1, keepdims=True)
    powers = jnp.exp(logits - top)
    mass = jnp.sum(powers, axis=1, keepdims=True)
    feat = f_ref.shape[1]
    block_feat = jnp.dot(
        powers.astype(jnp.bfloat16), f_ref[...], preferred_element_type=jnp.float32
    )
    out_ref[:feat, :] = block_feat.T
    lane = lax.broadcasted_iota(jnp.int32, (top.shape[0], 128), 1)
    extra = jnp.where(lane == 0, mass, jnp.where(lane == 1, top, 0.0))
    out_ref[feat:, :] = extra.T[:8, :]


def assign_rows(v, r, d, f, scale, tile, rotation):
    rows, width = v.shape
    cols, feat = f.shape
    tile = min(tile, rows)
    tiles = rows // tile
    grid_spec = pltpu.PrefetchScalarGridSpec(
        num_scalar_prefetch=1,
        grid=(tiles,),
        in_specs=[
            pl.BlockSpec((tile, width), lambda i, rot: ((i + rot[0]) % tiles, 0)),
            pl.BlockSpec((cols, width), lambda i, rot: (0, 0)),
            pl.BlockSpec((1, cols), lambda i, rot: (0, 0)),
            pl.BlockSpec((cols, feat), lambda i, rot: (0, 0)),
        ],
        out_specs=pl.BlockSpec((feat + 8, tile), lambda i, rot: (0, i)),
    )
    return pl.pallas_call(
        functools.partial(assign_kernel, scale=scale),
        out_shape=jax.ShapeDtypeStruct((feat + 8, rows), jnp.float32),
        grid_spec=grid_spec,
        cost_estimate=pl.CostEstimate(
            flops=2 * rows * cols * (width + feat) + 5 * rows * cols,
            transcendentals=rows * cols,
            bytes_accessed=2 * (rows + cols) * width + 2 * cols * feat + 4 * rows * (feat + 8),
        ),
    )(rotation, v, r, d.reshape(1, cols), f)


def local(vehicle_emb, request_emb, request_feat, log_supply, log_demand):
    own_rows = lax.all_gather(vehicle_emb, "req", axis=0, tiled=True)
    row_count = own_rows.shape[0]
    scale = 3.0 / math.sqrt(own_rows.shape[1])

    def column_pot(shift):
        partial = lse_over_rows(own_rows, shift, request_emb, scale, 512)
        return log_demand - merge_lse(gather_by_exchange(partial, "veh"))

    demand_first = column_pot(jnp.zeros((row_count,), jnp.float32))
    partial = lse_over_rows(request_emb, demand_first, own_rows, scale, 256)
    parts = lax.all_gather(partial, "req", axis=0, tiled=False)
    supply_pot = log_supply - merge_lse(parts)
    demand_second = column_pot(supply_pot)

    owners = lax.axis_size("req")
    chunk = row_count // owners
    tile = min(128, chunk)
    me = lax.axis_index("req")
    rotation = jnp.reshape(me * (chunk // tile), (1,)).astype(jnp.int32)
    packed = assign_rows(own_rows, request_emb, demand_second, request_feat, scale, tile, rotation)
    feat = request_feat.shape[1]
    pieces = [packed[:, :chunk]]
    for step in range(1, owners):
        pieces.append(
            lax.ppermute(
                packed[:, step * chunk : (step + 1) * chunk],
                "req",
                [(i, (i + step) % owners) for i in range(owners)],
            )
        )
    arrived = jnp.stack(pieces)
    peaks = arrived[:, feat + 1, :]
    masses = arrived[:, feat, :]
    factor = jnp.exp(peaks - jnp.max(peaks, axis=0, keepdims=True))
    numerator = jnp.sum(arrived[:, :feat, :] * factor[:, None, :], axis=0)
    denominator = jnp.sum(masses * factor, axis=0)
    return (numerator / denominator[None, :]).T


def solution(mesh):
    in_specs = (P(("veh", "req"), None), P("req", None), P("req", None), P("veh"), P("req"))
    out_specs = P(("veh", "req"), None)
    return jax.shard_map(local, mesh=mesh, in_specs=in_specs, out_specs=out_specs, check_vma=False)
```

```python
import functools
import math

import jax
import jax.numpy as jnp
from jax import lax
from jax.experimental import pallas as pl
from jax.experimental.pallas import tpu as pltpu
from jax.sharding import PartitionSpec as P


def gather_by_exchange(x, axis):
    count = lax.axis_size(axis)
    spread = jnp.broadcast_to(x[None], (count,) + x.shape)
    return lax.all_to_all(spread, axis, 0, 0, tiled=True)


def merge_lse(parts):
    top = jnp.max(parts, axis=0)
    return top + jnp.log(jnp.sum(jnp.exp(parts - top[None]), axis=0))


def lse_kernel(a_ref, shift_ref, b_ref, out_ref, *, scale):
    scores = lax.dot_general(
        a_ref[...], b_ref[...], (((1,), (1,)), ((), ())), preferred_element_type=jnp.float32
    )
    logits = scores * scale + shift_ref[...]
    top = jnp.max(logits, axis=0, keepdims=True)
    total = jnp.sum(jnp.exp(logits - top), axis=0, keepdims=True)
    out_ref[...] = top + jnp.log(total)


def lse_over_rows(a, shift, b, scale, tile):
    rows, width = a.shape
    cols = b.shape[0]
    tile = min(tile, cols)
    return pl.pallas_call(
        functools.partial(lse_kernel, scale=scale),
        out_shape=jax.ShapeDtypeStruct((1, cols), jnp.float32),
        grid=(cols // tile,),
        in_specs=[
            pl.BlockSpec((rows, width), lambda j: (0, 0)),
            pl.BlockSpec((rows, 1), lambda j: (0, 0)),
            pl.BlockSpec((tile, width), lambda j: (j, 0)),
        ],
        out_specs=pl.BlockSpec((1, tile), lambda j: (0, j)),
        cost_estimate=pl.CostEstimate(
            flops=2 * rows * cols * width + 5 * rows * cols,
            transcendentals=rows * cols,
            bytes_accessed=2 * (rows + cols) * width + 4 * (rows + cols),
        ),
    )(a, shift.reshape(rows, 1), b)[0]


def assign_kernel(rot_ref, v_ref, r_ref, d_ref, f_ref, out_ref, *, scale):
    scores = lax.dot_general(
        v_ref[...], r_ref[...], (((1,), (1,)), ((), ())), preferred_element_type=jnp.float32
    )
    logits = scores * scale + d_ref[...]
    top = jnp.max(logits, axis=1, keepdims=True)
    powers = jnp.exp(logits - top)
    mass = jnp.sum(powers, axis=1, keepdims=True)
    feat = f_ref.shape[1]
    block_feat = jnp.dot(
        powers.astype(jnp.bfloat16), f_ref[...], preferred_element_type=jnp.float32
    )
    out_ref[:feat, :] = block_feat.T
    lane = lax.broadcasted_iota(jnp.int32, (top.shape[0], 128), 1)
    extra = jnp.where(lane == 0, mass, jnp.where(lane == 1, top, 0.0))
    out_ref[feat:, :] = extra.T[:8, :]


def assign_rows(v, r, d, f, scale, tile, rotation):
    rows, width = v.shape
    cols, feat = f.shape
    tile = min(tile, rows)
    tiles = rows // tile
    grid_spec = pltpu.PrefetchScalarGridSpec(
        num_scalar_prefetch=1,
        grid=(tiles,),
        in_specs=[
            pl.BlockSpec((tile, width), lambda i, rot: ((i + rot[0]) % tiles, 0)),
            pl.BlockSpec((cols, width), lambda i, rot: (0, 0)),
            pl.BlockSpec((1, cols), lambda i, rot: (0, 0)),
            pl.BlockSpec((cols, feat), lambda i, rot: (0, 0)),
        ],
        out_specs=pl.BlockSpec((feat + 8, tile), lambda i, rot: (0, i)),
    )
    return pl.pallas_call(
        functools.partial(assign_kernel, scale=scale),
        out_shape=jax.ShapeDtypeStruct((feat + 8, rows), jnp.float32),
        grid_spec=grid_spec,
        cost_estimate=pl.CostEstimate(
            flops=2 * rows * cols * (width + feat) + 5 * rows * cols,
            transcendentals=rows * cols,
            bytes_accessed=2 * (rows + cols) * width + 2 * cols * feat + 4 * rows * (feat + 8),
        ),
    )(rotation, v, r, d.reshape(1, cols), f)


def local(vehicle_emb, request_emb, request_feat, log_supply, log_demand):
    own_rows = lax.all_gather(vehicle_emb, "req", axis=0, tiled=True)
    row_count = own_rows.shape[0]
    scale = 3.0 / math.sqrt(own_rows.shape[1])

    def column_pot(shift):
        partial = lse_over_rows(own_rows, shift, request_emb, scale, 2048)
        return log_demand - merge_lse(gather_by_exchange(partial, "veh"))

    demand_first = column_pot(jnp.zeros((row_count,), jnp.float32))
    partial = lse_over_rows(request_emb, demand_first, own_rows, scale, 1024)
    parts = lax.all_gather(partial, "req", axis=0, tiled=False)
    supply_pot = log_supply - merge_lse(parts)
    demand_second = column_pot(supply_pot)

    owners = lax.axis_size("req")
    chunk = row_count // owners
    tile = min(256, chunk)
    me = lax.axis_index("req")
    rotation = jnp.reshape(me * (chunk // tile), (1,)).astype(jnp.int32)
    packed = assign_rows(own_rows, request_emb, demand_second, request_feat, scale, tile, rotation)
    feat = request_feat.shape[1]
    pieces = [packed[:, :chunk]]
    for step in range(1, owners):
        pieces.append(
            lax.ppermute(
                packed[:, step * chunk : (step + 1) * chunk],
                "req",
                [(i, (i + step) % owners) for i in range(owners)],
            )
        )
    arrived = jnp.stack(pieces)
    peaks = arrived[:, feat + 1, :]
    masses = arrived[:, feat, :]
    factor = jnp.exp(peaks - jnp.max(peaks, axis=0, keepdims=True))
    numerator = jnp.sum(arrived[:, :feat, :] * factor[:, None, :], axis=0)
    denominator = jnp.sum(masses * factor, axis=0)
    return (numerator / denominator[None, :]).T


def solution(mesh):
    in_specs = (P(("veh", "req"), None), P("req", None), P("req", None), P("veh"), P("req"))
    out_specs = P(("veh", "req"), None)
    return jax.shard_map(local, mesh=mesh, in_specs=in_specs, out_specs=out_specs, check_vma=False)
```

```python
import functools
import math

import jax
import jax.numpy as jnp
from jax import lax
from jax.experimental import pallas as pl
from jax.experimental.pallas import tpu as pltpu
from jax.sharding import PartitionSpec as P


def merged_lse(parts):
    top = jnp.max(parts, axis=0, keepdims=True)
    return top + jnp.log(jnp.sum(jnp.exp(parts - top), axis=0, keepdims=True))


def lse_kernel(*refs, scale, shifted, copies):
    if shifted:
        a_ref, parts_ref, base_ref, b_ref, out_ref, column_ref = refs

        @pl.when(pl.program_id(0) == 0)
        def _():
            row = base_ref[...] - merged_lse(parts_ref[...])
            wide = jnp.broadcast_to(row, (128, row.shape[1]))
            column_ref[...] = jnp.transpose(wide)[:, :1]

    else:
        a_ref, b_ref, out_ref = refs
    scores = lax.dot_general(
        a_ref[...], b_ref[...], (((1,), (1,)), ((), ())), preferred_element_type=jnp.float32
    )
    logits = scores * scale
    if shifted:
        logits = logits + column_ref[...]
    top = jnp.max(logits, axis=0, keepdims=True)
    total = jnp.sum(jnp.exp(logits - top), axis=0, keepdims=True)
    result = top + jnp.log(total)
    out_ref[...] = jnp.broadcast_to(result, (copies, result.shape[1]))


def lse_over_rows(a, b, scale, tile, copies, parts=None, base=None):
    rows, width = a.shape
    cols = b.shape[0]
    tile = min(tile, cols)
    shifted = parts is not None
    in_specs = [pl.BlockSpec((rows, width), lambda j: (0, 0))]
    operands = [a]
    scratch = []
    if shifted:
        in_specs += [
            pl.BlockSpec(parts.shape, lambda j: (0, 0)),
            pl.BlockSpec((1, rows), lambda j: (0, 0)),
        ]
        operands += [parts, base.reshape(1, rows)]
        scratch = [pltpu.VMEM((rows, 1), jnp.float32)]
    in_specs.append(pl.BlockSpec((tile, width), lambda j: (j, 0)))
    operands.append(b)
    return pl.pallas_call(
        functools.partial(lse_kernel, scale=scale, shifted=shifted, copies=copies),
        out_shape=jax.ShapeDtypeStruct((copies, cols), jnp.float32),
        grid=(cols // tile,),
        in_specs=in_specs,
        out_specs=pl.BlockSpec((copies, tile), lambda j: (0, j)),
        scratch_shapes=scratch,
        cost_estimate=pl.CostEstimate(
            flops=2 * rows * cols * width + 5 * rows * cols,
            transcendentals=rows * cols,
            bytes_accessed=2 * (rows + cols) * width + 4 * (rows + copies * cols),
        ),
    )(*operands)


def assign_kernel(rot_ref, v_ref, r_ref, parts_ref, base_ref, f_ref, out_ref, *, scale):
    demand = base_ref[...] - merged_lse(parts_ref[...])
    scores = lax.dot_general(
        v_ref[...], r_ref[...], (((1,), (1,)), ((), ())), preferred_element_type=jnp.float32
    )
    logits = scores * scale + demand
    top = jnp.max(logits, axis=1, keepdims=True)
    powers = jnp.exp(logits - top)
    mass = jnp.sum(powers, axis=1, keepdims=True)
    feat = f_ref.shape[1]
    block_feat = jnp.dot(
        powers.astype(jnp.bfloat16), f_ref[...], preferred_element_type=jnp.float32
    )
    out_ref[:feat, :] = block_feat.T
    lane = lax.broadcasted_iota(jnp.int32, (top.shape[0], 128), 1)
    extra = jnp.where(lane == 0, mass, jnp.where(lane == 1, top, 0.0))
    out_ref[feat:, :] = extra.T[:8, :]


def assign_rows(v, r, parts, base, f, scale, tile, owners, rotation):
    rows, width = v.shape
    cols, feat = f.shape
    chunk = rows // owners
    tiles = rows // tile
    per_chunk = chunk // tile
    grid_spec = pltpu.PrefetchScalarGridSpec(
        num_scalar_prefetch=1,
        grid=(tiles,),
        in_specs=[
            pl.BlockSpec((tile, width), lambda i, rot: ((i + rot[0]) % tiles, 0)),
            pl.BlockSpec((cols, width), lambda i, rot: (0, 0)),
            pl.BlockSpec(parts.shape, lambda i, rot: (0, 0)),
            pl.BlockSpec((1, cols), lambda i, rot: (0, 0)),
            pl.BlockSpec((cols, feat), lambda i, rot: (0, 0)),
        ],
        out_specs=pl.BlockSpec(
            (None, feat + 8, tile), lambda i, rot: (i // per_chunk, 0, i % per_chunk)
        ),
    )
    return pl.pallas_call(
        functools.partial(assign_kernel, scale=scale),
        out_shape=jax.ShapeDtypeStruct((owners, feat + 8, chunk), jnp.float32),
        grid_spec=grid_spec,
        cost_estimate=pl.CostEstimate(
            flops=2 * rows * cols * (width + feat) + 5 * rows * cols,
            transcendentals=rows * cols,
            bytes_accessed=2 * (rows + cols) * width + 2 * cols * feat + 4 * rows * (feat + 8),
        ),
    )(rotation, v, r, parts, base.reshape(1, cols), f)


def local(vehicle_emb, request_emb, request_feat, log_supply, log_demand):
    own_rows = lax.all_gather(vehicle_emb, "req", axis=0, tiled=True)
    row_count = own_rows.shape[0]
    scale = 3.0 / math.sqrt(own_rows.shape[1])
    spread = lax.axis_size("veh")

    def exchange(block):
        return lax.all_to_all(block, "veh", 0, 0, tiled=True)

    first = exchange(lse_over_rows(own_rows, request_emb, scale, 2048, spread))
    partial = lse_over_rows(request_emb, own_rows, scale, 1024, 1, first, log_demand)
    row_parts = lax.all_gather(partial[0], "req", axis=0, tiled=False)
    second = exchange(
        lse_over_rows(own_rows, request_emb, scale, 2048, spread, row_parts, log_supply)
    )

    owners = lax.axis_size("req")
    chunk = row_count // owners
    tile = min(256, chunk)
    me = lax.axis_index("req")
    rotation = jnp.reshape(me * (chunk // tile), (1,)).astype(jnp.int32)
    packed = assign_rows(
        own_rows, request_emb, second, log_demand, request_feat, scale, tile, owners, rotation
    )
    feat = request_feat.shape[1]
    pieces = [packed[0]]
    for step in range(1, owners):
        pieces.append(
            lax.ppermute(packed[step], "req", [(i, (i + step) % owners) for i in range(owners)])
        )
    arrived = jnp.stack(pieces)
    peaks = arrived[:, feat + 1, :]
    masses = arrived[:, feat, :]
    factor = jnp.exp(peaks - jnp.max(peaks, axis=0, keepdims=True))
    numerator = jnp.sum(arrived[:, :feat, :] * factor[:, None, :], axis=0)
    denominator = jnp.sum(masses * factor, axis=0)
    return (numerator / denominator[None, :]).T


def solution(mesh):
    in_specs = (P(("veh", "req"), None), P("req", None), P("req", None), P("veh"), P("req"))
    out_specs = P(("veh", "req"), None)
    return jax.shard_map(local, mesh=mesh, in_specs=in_specs, out_specs=out_specs, check_vma=False)
```

```python
import functools
import math

import jax
import jax.numpy as jnp
from jax import lax
from jax.experimental import pallas as pl
from jax.experimental.pallas import tpu as pltpu
from jax.sharding import PartitionSpec as P


def merged_lse(parts):
    top = jnp.max(parts, axis=0)
    return top + jnp.log(jnp.sum(jnp.exp(parts - top[None]), axis=0))


def lse_kernel(*refs, scale, shifted, copies):
    if shifted:
        a_ref, parts_ref, base_ref, b_ref, out_ref, column_ref = refs

        @pl.when(pl.program_id(0) == 0)
        def _():
            row = base_ref[...] - merged_lse(parts_ref[...])
            wide = jnp.broadcast_to(row, (128, row.shape[1]))
            column_ref[...] = jnp.transpose(wide)[:, :1]

    else:
        a_ref, b_ref, out_ref = refs
    scores = lax.dot_general(
        a_ref[...], b_ref[...], (((1,), (1,)), ((), ())), preferred_element_type=jnp.float32
    )
    logits = scores * scale
    if shifted:
        logits = logits + column_ref[...]
    top = jnp.max(logits, axis=0, keepdims=True)
    total = jnp.sum(jnp.exp(logits - top), axis=0, keepdims=True)
    result = top + jnp.log(total)
    out_ref[...] = jnp.broadcast_to(result[None], (copies,) + result.shape)


def lse_over_rows(a, b, scale, tile, copies, parts=None, base=None):
    rows, width = a.shape
    cols = b.shape[0]
    tile = min(tile, cols)
    shifted = parts is not None
    in_specs = [pl.BlockSpec((rows, width), lambda j: (0, 0))]
    operands = [a]
    scratch = []
    if shifted:
        in_specs += [
            pl.BlockSpec(parts.shape, lambda j: (0, 0, 0)),
            pl.BlockSpec((1, rows), lambda j: (0, 0)),
        ]
        operands += [parts, base.reshape(1, rows)]
        scratch = [pltpu.VMEM((rows, 1), jnp.float32)]
    in_specs.append(pl.BlockSpec((tile, width), lambda j: (j, 0)))
    operands.append(b)
    return pl.pallas_call(
        functools.partial(lse_kernel, scale=scale, shifted=shifted, copies=copies),
        out_shape=jax.ShapeDtypeStruct((copies, 1, cols), jnp.float32),
        grid=(cols // tile,),
        in_specs=in_specs,
        out_specs=pl.BlockSpec((copies, 1, tile), lambda j: (0, 0, j)),
        scratch_shapes=scratch,
        cost_estimate=pl.CostEstimate(
            flops=2 * rows * cols * width + 5 * rows * cols,
            transcendentals=rows * cols,
            bytes_accessed=2 * (rows + cols) * width + 4 * (rows + copies * cols),
        ),
    )(*operands)


def assign_kernel(rot_ref, v_ref, r_ref, parts_ref, base_ref, f_ref, out_ref, *, scale):
    demand = base_ref[...] - merged_lse(parts_ref[...])
    scores = lax.dot_general(
        v_ref[...], r_ref[...], (((1,), (1,)), ((), ())), preferred_element_type=jnp.float32
    )
    logits = scores * scale + demand
    top = jnp.max(logits, axis=1, keepdims=True)
    powers = jnp.exp(logits - top)
    mass = jnp.sum(powers, axis=1, keepdims=True)
    feat = f_ref.shape[1]
    block_feat = jnp.dot(
        powers.astype(jnp.bfloat16), f_ref[...], preferred_element_type=jnp.float32
    )
    out_ref[:feat, :] = block_feat.T
    lane = lax.broadcasted_iota(jnp.int32, (top.shape[0], 128), 1)
    extra = jnp.where(lane == 0, mass, jnp.where(lane == 1, top, 0.0))
    out_ref[feat:, :] = extra.T[:8, :]


def assign_chunk(v, r, parts, base, f, scale, chunk, index):
    rows, width = v.shape
    cols, feat = f.shape
    grid_spec = pltpu.PrefetchScalarGridSpec(
        num_scalar_prefetch=1,
        grid=(1,),
        in_specs=[
            pl.BlockSpec((chunk, width), lambda i, at: (at[0], 0)),
            pl.BlockSpec((cols, width), lambda i, at: (0, 0)),
            pl.BlockSpec(parts.shape, lambda i, at: (0, 0, 0)),
            pl.BlockSpec((1, cols), lambda i, at: (0, 0)),
            pl.BlockSpec((cols, feat), lambda i, at: (0, 0)),
        ],
        out_specs=pl.BlockSpec((feat + 8, chunk), lambda i, at: (0, 0)),
    )
    return pl.pallas_call(
        functools.partial(assign_kernel, scale=scale),
        out_shape=jax.ShapeDtypeStruct((feat + 8, chunk), jnp.float32),
        grid_spec=grid_spec,
        cost_estimate=pl.CostEstimate(
            flops=2 * chunk * cols * (width + feat) + 5 * chunk * cols,
            transcendentals=chunk * cols,
            bytes_accessed=2 * (chunk + cols) * width + 2 * cols * feat + 4 * chunk * (feat + 8),
        ),
    )(index, v, r, parts, base.reshape(1, cols), f)


def local(vehicle_emb, request_emb, request_feat, log_supply, log_demand):
    own_rows = lax.all_gather(vehicle_emb, "req", axis=0, tiled=True)
    row_count = own_rows.shape[0]
    scale = 3.0 / math.sqrt(own_rows.shape[1])
    spread = lax.axis_size("veh")

    def exchange(block):
        return lax.all_to_all(block, "veh", 0, 0, tiled=True)

    first = exchange(lse_over_rows(own_rows, request_emb, scale, 2048, spread))
    partial = lse_over_rows(request_emb, own_rows, scale, 1024, 1, first, log_demand)
    row_parts = lax.all_gather(partial[0], "req", axis=0, tiled=False)
    second = exchange(
        lse_over_rows(own_rows, request_emb, scale, 2048, spread, row_parts, log_supply)
    )

    owners = lax.axis_size("req")
    chunk = row_count // owners
    me = lax.axis_index("req")
    feat = request_feat.shape[1]
    pieces = []
    for step in list(range(1, owners)) + [0]:
        index = jnp.reshape((me + step) % owners, (1,)).astype(jnp.int32)
        piece = assign_chunk(
            own_rows, request_emb, second, log_demand, request_feat, scale, chunk, index
        )
        if step:
            piece = lax.ppermute(piece, "req", [(i, (i + step) % owners) for i in range(owners)])
        pieces.append(piece)
    arrived = jnp.stack(pieces)
    peaks = arrived[:, feat + 1, :]
    masses = arrived[:, feat, :]
    factor = jnp.exp(peaks - jnp.max(peaks, axis=0, keepdims=True))
    numerator = jnp.sum(arrived[:, :feat, :] * factor[:, None, :], axis=0)
    denominator = jnp.sum(masses * factor, axis=0)
    return (numerator / denominator[None, :]).T


def solution(mesh):
    in_specs = (P(("veh", "req"), None), P("req", None), P("req", None), P("veh"), P("req"))
    out_specs = P(("veh", "req"), None)
    return jax.shard_map(local, mesh=mesh, in_specs=in_specs, out_specs=out_specs, check_vma=False)
```

```python
import functools
import math

import jax
import jax.numpy as jnp
from jax import lax
from jax.experimental import pallas as pl
from jax.experimental.pallas import tpu as pltpu
from jax.sharding import PartitionSpec as P


def merged_lse(parts):
    top = jnp.max(parts, axis=0)
    return top + jnp.log(jnp.sum(jnp.exp(parts - top[None]), axis=0))


def lse_kernel(*refs, scale, shifted, copies):
    if shifted:
        a_ref, parts_ref, base_ref, b_ref, out_ref, column_ref = refs

        @pl.when(pl.program_id(0) == 0)
        def _():
            row = base_ref[...] - merged_lse(parts_ref[...])
            wide = jnp.broadcast_to(row, (128, row.shape[1]))
            column_ref[...] = jnp.transpose(wide)[:, :1]

    else:
        a_ref, b_ref, out_ref = refs
    scores = lax.dot_general(
        a_ref[...], b_ref[...], (((1,), (1,)), ((), ())), preferred_element_type=jnp.float32
    )
    logits = scores * scale
    if shifted:
        logits = logits + column_ref[...]
    top = jnp.max(logits, axis=0, keepdims=True)
    total = jnp.sum(jnp.exp(logits - top), axis=0, keepdims=True)
    result = top + jnp.log(total)
    out_ref[...] = jnp.broadcast_to(result[None], (copies,) + result.shape)


def lse_over_rows(a, b, scale, tile, copies, parts=None, base=None):
    rows, width = a.shape
    cols = b.shape[0]
    tile = min(tile, cols)
    shifted = parts is not None
    in_specs = [pl.BlockSpec((rows, width), lambda j: (0, 0))]
    operands = [a]
    scratch = []
    if shifted:
        in_specs += [
            pl.BlockSpec(parts.shape, lambda j: (0, 0, 0)),
            pl.BlockSpec((1, rows), lambda j: (0, 0)),
        ]
        operands += [parts, base.reshape(1, rows)]
        scratch = [pltpu.VMEM((rows, 1), jnp.float32)]
    in_specs.append(pl.BlockSpec((tile, width), lambda j: (j, 0)))
    operands.append(b)
    return pl.pallas_call(
        functools.partial(lse_kernel, scale=scale, shifted=shifted, copies=copies),
        out_shape=jax.ShapeDtypeStruct((copies, 1, cols), jnp.float32),
        grid=(cols // tile,),
        in_specs=in_specs,
        out_specs=pl.BlockSpec((copies, 1, tile), lambda j: (0, 0, j)),
        scratch_shapes=scratch,
        cost_estimate=pl.CostEstimate(
            flops=2 * rows * cols * width + 5 * rows * cols,
            transcendentals=rows * cols,
            bytes_accessed=2 * (rows + cols) * width + 4 * (rows + copies * cols),
        ),
    )(*operands)


def assign_kernel(
    rot_ref, v_ref, r_ref, parts_ref, base_ref, f_hbm, out_ref, f_ref, sem, *, scale
):
    fetch = pltpu.make_async_copy(f_hbm, f_ref, sem)
    fetch.start()
    demand = base_ref[...] - merged_lse(parts_ref[...])
    scores = lax.dot_general(
        v_ref[...], r_ref[...], (((1,), (1,)), ((), ())), preferred_element_type=jnp.float32
    )
    logits = scores * scale + demand
    top = jnp.max(logits, axis=1, keepdims=True)
    powers = jnp.exp(logits - top)
    mass = jnp.sum(powers, axis=1, keepdims=True)
    feat = f_ref.shape[1]
    fetch.wait()
    block_feat = jnp.dot(
        powers.astype(jnp.bfloat16), f_ref[...], preferred_element_type=jnp.float32
    )
    out_ref[:feat, :] = block_feat.T
    lane = lax.broadcasted_iota(jnp.int32, (top.shape[0], 128), 1)
    extra = jnp.where(lane == 0, mass, jnp.where(lane == 1, top, 0.0))
    out_ref[feat:, :] = extra.T[:8, :]


def assign_chunk(v, r, parts, base, f, scale, chunk, index):
    rows, width = v.shape
    cols, feat = f.shape
    grid_spec = pltpu.PrefetchScalarGridSpec(
        num_scalar_prefetch=1,
        grid=(1,),
        in_specs=[
            pl.BlockSpec((chunk, width), lambda i, at: (at[0], 0)),
            pl.BlockSpec((cols, width), lambda i, at: (0, 0)),
            pl.BlockSpec(parts.shape, lambda i, at: (0, 0, 0)),
            pl.BlockSpec((1, cols), lambda i, at: (0, 0)),
            pl.BlockSpec(memory_space=pl.ANY),
        ],
        out_specs=pl.BlockSpec((feat + 8, chunk), lambda i, at: (0, 0)),
        scratch_shapes=[pltpu.VMEM((cols, feat), f.dtype), pltpu.SemaphoreType.DMA(())],
    )
    return pl.pallas_call(
        functools.partial(assign_kernel, scale=scale),
        out_shape=jax.ShapeDtypeStruct((feat + 8, chunk), jnp.float32),
        grid_spec=grid_spec,
        cost_estimate=pl.CostEstimate(
            flops=2 * chunk * cols * (width + feat) + 5 * chunk * cols,
            transcendentals=chunk * cols,
            bytes_accessed=2 * (chunk + cols) * width + 2 * cols * feat + 4 * chunk * (feat + 8),
        ),
    )(index, v, r, parts, base.reshape(1, cols), f)


def local(vehicle_emb, request_emb, request_feat, log_supply, log_demand):
    own_rows = lax.all_gather(vehicle_emb, "req", axis=0, tiled=True)
    row_count = own_rows.shape[0]
    scale = 3.0 / math.sqrt(own_rows.shape[1])
    spread = lax.axis_size("veh")

    def exchange(block):
        return lax.all_to_all(block, "veh", 0, 0, tiled=True)

    first = exchange(lse_over_rows(own_rows, request_emb, scale, 2048, spread))
    partial = lse_over_rows(request_emb, own_rows, scale, 1024, 1, first, log_demand)
    row_parts = lax.all_gather(partial[0], "req", axis=0, tiled=False)
    second = exchange(
        lse_over_rows(own_rows, request_emb, scale, 2048, spread, row_parts, log_supply)
    )

    owners = lax.axis_size("req")
    chunk = row_count // owners
    me = lax.axis_index("req")
    feat = request_feat.shape[1]
    pieces = []
    for step in list(range(1, owners)) + [0]:
        index = jnp.reshape((me + step) % owners, (1,)).astype(jnp.int32)
        piece = assign_chunk(
            own_rows, request_emb, second, log_demand, request_feat, scale, chunk, index
        )
        if step:
            piece = lax.ppermute(piece, "req", [(i, (i + step) % owners) for i in range(owners)])
        pieces.append(piece)
    arrived = jnp.stack(pieces)
    peaks = arrived[:, feat + 1, :]
    masses = arrived[:, feat, :]
    factor = jnp.exp(peaks - jnp.max(peaks, axis=0, keepdims=True))
    numerator = jnp.sum(arrived[:, :feat, :] * factor[:, None, :], axis=0)
    denominator = jnp.sum(masses * factor, axis=0)
    return (numerator / denominator[None, :]).T


def solution(mesh):
    in_specs = (P(("veh", "req"), None), P("req", None), P("req", None), P("veh"), P("req"))
    out_specs = P(("veh", "req"), None)
    return jax.shard_map(local, mesh=mesh, in_specs=in_specs, out_specs=out_specs, check_vma=False)
```

```python
import functools
import math

import jax
import jax.numpy as jnp
from jax import lax
from jax.experimental import pallas as pl
from jax.experimental.pallas import tpu as pltpu
from jax.sharding import PartitionSpec as P


def merged_lse(parts):
    top = jnp.max(parts, axis=0)
    return top + jnp.log(jnp.sum(jnp.exp(parts - top[None]), axis=0))


def lse_kernel(*refs, scale, shifted, copies):
    if shifted:
        a_ref, parts_ref, base_ref, b_ref, out_ref, column_ref = refs

        @pl.when(pl.program_id(0) == 0)
        def _():
            row = base_ref[...] - merged_lse(parts_ref[...])
            wide = jnp.broadcast_to(row, (128, row.shape[1]))
            column_ref[...] = jnp.transpose(wide)[:, :1]

    else:
        a_ref, b_ref, out_ref = refs
    scores = lax.dot_general(
        a_ref[...], b_ref[...], (((1,), (1,)), ((), ())), preferred_element_type=jnp.float32
    )
    logits = scores * scale
    if shifted:
        logits = logits + column_ref[...]
    top = jnp.max(logits, axis=0, keepdims=True)
    total = jnp.sum(jnp.exp(logits - top), axis=0, keepdims=True)
    result = top + jnp.log(total)
    out_ref[...] = jnp.broadcast_to(result[None], (copies,) + result.shape)


def lse_over_rows(a, b, scale, tile, copies, parts=None, base=None):
    rows, width = a.shape
    cols = b.shape[0]
    tile = min(tile, cols)
    shifted = parts is not None
    in_specs = [pl.BlockSpec((rows, width), lambda j: (0, 0))]
    operands = [a]
    scratch = []
    if shifted:
        in_specs += [
            pl.BlockSpec(parts.shape, lambda j: (0, 0, 0)),
            pl.BlockSpec((1, rows), lambda j: (0, 0)),
        ]
        operands += [parts, base.reshape(1, rows)]
        scratch = [pltpu.VMEM((rows, 1), jnp.float32)]
    in_specs.append(pl.BlockSpec((tile, width), lambda j: (j, 0)))
    operands.append(b)
    return pl.pallas_call(
        functools.partial(lse_kernel, scale=scale, shifted=shifted, copies=copies),
        out_shape=jax.ShapeDtypeStruct((copies, 1, cols), jnp.float32),
        grid=(cols // tile,),
        in_specs=in_specs,
        out_specs=pl.BlockSpec((copies, 1, tile), lambda j: (0, 0, j)),
        scratch_shapes=scratch,
        cost_estimate=pl.CostEstimate(
            flops=2 * rows * cols * width + 5 * rows * cols,
            transcendentals=rows * cols,
            bytes_accessed=2 * (rows + cols) * width + 4 * (rows + copies * cols),
        ),
    )(*operands)


def assign_kernel(
    rot_ref, v_ref, r_ref, parts_ref, base_ref, f_hbm, out_ref, f_ref, sem, *, scale
):
    fetch = pltpu.make_async_copy(f_hbm, f_ref, sem)
    fetch.start()
    demand = base_ref[...] - merged_lse(parts_ref[...])
    scores = lax.dot_general(
        v_ref[...], r_ref[...], (((1,), (1,)), ((), ())), preferred_element_type=jnp.float32
    )
    logits = scores * scale + demand
    top = jnp.max(logits, axis=1, keepdims=True)
    powers = jnp.exp(logits - top)
    mass = jnp.sum(powers, axis=1, keepdims=True)
    feat = f_ref.shape[1]
    fetch.wait()
    block_feat = jnp.dot(
        powers.astype(jnp.bfloat16), f_ref[...], preferred_element_type=jnp.float32
    )
    out_ref[:feat, :] = block_feat.T
    lane = lax.broadcasted_iota(jnp.int32, (top.shape[0], 128), 1)
    extra = jnp.where(lane == 0, mass, jnp.where(lane == 1, top, 0.0))
    out_ref[feat:, :] = extra.T[:8, :]


def assign_chunk(v, r, parts, base, f, scale, chunk, index):
    rows, width = v.shape
    cols, feat = f.shape
    grid_spec = pltpu.PrefetchScalarGridSpec(
        num_scalar_prefetch=1,
        grid=(1,),
        in_specs=[
            pl.BlockSpec((chunk, width), lambda i, at: (at[0], 0)),
            pl.BlockSpec((cols, width), lambda i, at: (0, 0)),
            pl.BlockSpec(parts.shape, lambda i, at: (0, 0, 0)),
            pl.BlockSpec((1, cols), lambda i, at: (0, 0)),
            pl.BlockSpec(memory_space=pl.ANY),
        ],
        out_specs=pl.BlockSpec((feat + 8, chunk), lambda i, at: (0, 0)),
        scratch_shapes=[pltpu.VMEM((cols, feat), f.dtype), pltpu.SemaphoreType.DMA(())],
    )
    return pl.pallas_call(
        functools.partial(assign_kernel, scale=scale),
        out_shape=jax.ShapeDtypeStruct((feat + 8, chunk), jnp.float32),
        grid_spec=grid_spec,
        compiler_params=pltpu.CompilerParams(vmem_limit_bytes=24 * 1024 * 1024),
        cost_estimate=pl.CostEstimate(
            flops=2 * chunk * cols * (width + feat) + 5 * chunk * cols,
            transcendentals=chunk * cols,
            bytes_accessed=2 * (chunk + cols) * width + 2 * cols * feat + 4 * chunk * (feat + 8),
        ),
    )(index, v, r, parts, base.reshape(1, cols), f)


def local(vehicle_emb, request_emb, request_feat, log_supply, log_demand):
    own_rows = lax.all_gather(vehicle_emb, "req", axis=0, tiled=True)
    row_count = own_rows.shape[0]
    scale = 3.0 / math.sqrt(own_rows.shape[1])
    spread = lax.axis_size("veh")

    def exchange(block):
        return lax.all_to_all(block, "veh", 0, 0, tiled=True)

    first = exchange(lse_over_rows(own_rows, request_emb, scale, 2048, spread))
    partial = lse_over_rows(request_emb, own_rows, scale, 1024, 1, first, log_demand)
    row_parts = lax.all_gather(partial[0], "req", axis=0, tiled=False)
    second = exchange(
        lse_over_rows(own_rows, request_emb, scale, 2048, spread, row_parts, log_supply)
    )

    owners = lax.axis_size("req")
    chunk = row_count // owners
    me = lax.axis_index("req")
    feat = request_feat.shape[1]
    pieces = []
    for step in list(range(1, owners)) + [0]:
        index = jnp.reshape((me + step) % owners, (1,)).astype(jnp.int32)
        piece = assign_chunk(
            own_rows, request_emb, second, log_demand, request_feat, scale, chunk, index
        )
        if step:
            piece = lax.ppermute(piece, "req", [(i, (i + step) % owners) for i in range(owners)])
        pieces.append(piece)
    arrived = jnp.stack(pieces)
    peaks = arrived[:, feat + 1, :]
    masses = arrived[:, feat, :]
    factor = jnp.exp(peaks - jnp.max(peaks, axis=0, keepdims=True))
    numerator = jnp.sum(arrived[:, :feat, :] * factor[:, None, :], axis=0)
    denominator = jnp.sum(masses * factor, axis=0)
    return (numerator / denominator[None, :]).T


def solution(mesh):
    in_specs = (P(("veh", "req"), None), P("req", None), P("req", None), P("veh"), P("req"))
    out_specs = P(("veh", "req"), None)
    return jax.shard_map(local, mesh=mesh, in_specs=in_specs, out_specs=out_specs, check_vma=False)
```

```python
import functools
import math

import jax
import jax.numpy as jnp
from jax import lax
from jax.experimental import pallas as pl
from jax.experimental.pallas import tpu as pltpu
from jax.sharding import PartitionSpec as P


def merged_lse(parts):
    top = jnp.max(parts, axis=0)
    return top + jnp.log(jnp.sum(jnp.exp(parts - top[None]), axis=0))


def lse_kernel(*refs, scale, shifted, copies):
    if shifted:
        a_ref, parts_ref, base_ref, b_ref, out_ref, column_ref = refs

        @pl.when(pl.program_id(0) == 0)
        def _():
            row = base_ref[...] - merged_lse(parts_ref[...])
            wide = jnp.broadcast_to(row, (128, row.shape[1]))
            column_ref[...] = jnp.transpose(wide)[:, :1]

    else:
        a_ref, b_ref, out_ref = refs
    scores = lax.dot_general(
        a_ref[...], b_ref[...], (((1,), (1,)), ((), ())), preferred_element_type=jnp.float32
    )
    logits = scores * scale
    if shifted:
        logits = logits + column_ref[...]
    top = jnp.max(logits, axis=0, keepdims=True)
    total = jnp.sum(jnp.exp(logits - top), axis=0, keepdims=True)
    result = top + jnp.log(total)
    out_ref[...] = jnp.broadcast_to(result[None], (copies,) + result.shape)


def lse_over_rows(a, b, scale, tile, copies, vmem_limit, parts=None, base=None):
    rows, width = a.shape
    cols = b.shape[0]
    tile = min(tile, cols)
    shifted = parts is not None
    in_specs = [pl.BlockSpec((rows, width), lambda j: (0, 0))]
    operands = [a]
    scratch = []
    if shifted:
        in_specs += [
            pl.BlockSpec(parts.shape, lambda j: (0, 0, 0)),
            pl.BlockSpec((1, rows), lambda j: (0, 0)),
        ]
        operands += [parts, base.reshape(1, rows)]
        scratch = [pltpu.VMEM((rows, 1), jnp.float32)]
    in_specs.append(pl.BlockSpec((tile, width), lambda j: (j, 0)))
    operands.append(b)
    return pl.pallas_call(
        functools.partial(lse_kernel, scale=scale, shifted=shifted, copies=copies),
        out_shape=jax.ShapeDtypeStruct((copies, 1, cols), jnp.float32),
        grid=(cols // tile,),
        in_specs=in_specs,
        out_specs=pl.BlockSpec((copies, 1, tile), lambda j: (0, 0, j)),
        scratch_shapes=scratch,
        compiler_params=pltpu.CompilerParams(vmem_limit_bytes=vmem_limit),
        cost_estimate=pl.CostEstimate(
            flops=2 * rows * cols * width + 5 * rows * cols,
            transcendentals=rows * cols,
            bytes_accessed=2 * (rows + cols) * width + 4 * (rows + copies * cols),
        ),
    )(*operands)


def assign_kernel(
    rot_ref, v_ref, r_ref, parts_ref, base_ref, f_hbm, out_ref, f_ref, sem, *, scale
):
    fetch = pltpu.make_async_copy(f_hbm, f_ref, sem)
    fetch.start()
    demand = base_ref[...] - merged_lse(parts_ref[...])
    scores = lax.dot_general(
        v_ref[...], r_ref[...], (((1,), (1,)), ((), ())), preferred_element_type=jnp.float32
    )
    logits = scores * scale + demand
    top = jnp.max(logits, axis=1, keepdims=True)
    powers = jnp.exp(logits - top)
    mass = jnp.sum(powers, axis=1, keepdims=True)
    feat = f_ref.shape[1]
    fetch.wait()
    block_feat = jnp.dot(
        powers.astype(jnp.bfloat16), f_ref[...], preferred_element_type=jnp.float32
    )
    out_ref[:feat, :] = block_feat.T
    lane = lax.broadcasted_iota(jnp.int32, (top.shape[0], 128), 1)
    extra = jnp.where(lane == 0, mass, jnp.where(lane == 1, top, 0.0))
    out_ref[feat:, :] = extra.T[:8, :]


def assign_chunk(v, r, parts, base, f, scale, chunk, index):
    rows, width = v.shape
    cols, feat = f.shape
    grid_spec = pltpu.PrefetchScalarGridSpec(
        num_scalar_prefetch=1,
        grid=(1,),
        in_specs=[
            pl.BlockSpec((chunk, width), lambda i, at: (at[0], 0)),
            pl.BlockSpec((cols, width), lambda i, at: (0, 0)),
            pl.BlockSpec(parts.shape, lambda i, at: (0, 0, 0)),
            pl.BlockSpec((1, cols), lambda i, at: (0, 0)),
            pl.BlockSpec(memory_space=pl.ANY),
        ],
        out_specs=pl.BlockSpec((feat + 8, chunk), lambda i, at: (0, 0)),
        scratch_shapes=[pltpu.VMEM((cols, feat), f.dtype), pltpu.SemaphoreType.DMA(())],
    )
    return pl.pallas_call(
        functools.partial(assign_kernel, scale=scale),
        out_shape=jax.ShapeDtypeStruct((feat + 8, chunk), jnp.float32),
        grid_spec=grid_spec,
        compiler_params=pltpu.CompilerParams(vmem_limit_bytes=24 * 1024 * 1024),
        cost_estimate=pl.CostEstimate(
            flops=2 * chunk * cols * (width + feat) + 5 * chunk * cols,
            transcendentals=chunk * cols,
            bytes_accessed=2 * (chunk + cols) * width + 2 * cols * feat + 4 * chunk * (feat + 8),
        ),
    )(index, v, r, parts, base.reshape(1, cols), f)


def combine_kernel(*refs):
    piece_refs, out_ref = refs[:-1], refs[-1]
    feat = out_ref.shape[1]
    peaks = [ref[feat + 1 : feat + 2, :] for ref in piece_refs]
    top = peaks[0]
    for peak in peaks[1:]:
        top = jnp.maximum(top, peak)
    numerator = None
    denominator = None
    for ref, peak in zip(piece_refs, peaks):
        factor = jnp.exp(peak - top)
        term = ref[:feat, :] * factor
        mass = ref[feat : feat + 1, :] * factor
        numerator = term if numerator is None else numerator + term
        denominator = mass if denominator is None else denominator + mass
    out_ref[...] = (numerator / denominator).T


def combine(pieces, feat):
    chunk = pieces[0].shape[1]
    return pl.pallas_call(
        combine_kernel,
        out_shape=jax.ShapeDtypeStruct((chunk, feat), jnp.float32),
        in_specs=[pl.BlockSpec(piece.shape, lambda: (0, 0)) for piece in pieces],
        out_specs=pl.BlockSpec((chunk, feat), lambda: (0, 0)),
        cost_estimate=pl.CostEstimate(
            flops=3 * len(pieces) * chunk * feat,
            transcendentals=len(pieces) * chunk,
            bytes_accessed=4 * chunk * ((feat + 8) * len(pieces) + feat),
        ),
    )(*pieces)


def local(vehicle_emb, request_emb, request_feat, log_supply, log_demand):
    own_rows = lax.all_gather(vehicle_emb, "req", axis=0, tiled=True)
    row_count = own_rows.shape[0]
    scale = 3.0 / math.sqrt(own_rows.shape[1])
    spread = lax.axis_size("veh")

    def exchange(block):
        return lax.all_to_all(block, "veh", 0, 0, tiled=True)

    first = exchange(lse_over_rows(own_rows, request_emb, scale, 2048, spread, 24 << 20))
    partial = lse_over_rows(request_emb, own_rows, scale, 1024, 1, 48 << 20, first, log_demand)
    row_parts = lax.all_gather(partial[0], "req", axis=0, tiled=False)
    second = exchange(
        lse_over_rows(own_rows, request_emb, scale, 2048, spread, 24 << 20, row_parts, log_supply)
    )

    owners = lax.axis_size("req")
    chunk = row_count // owners
    me = lax.axis_index("req")
    feat = request_feat.shape[1]
    pieces = []
    for step in list(range(1, owners)) + [0]:
        index = jnp.reshape((me + step) % owners, (1,)).astype(jnp.int32)
        piece = assign_chunk(
            own_rows, request_emb, second, log_demand, request_feat, scale, chunk, index
        )
        if step:
            piece = lax.ppermute(piece, "req", [(i, (i + step) % owners) for i in range(owners)])
        pieces.append(piece)
    return combine(pieces, feat)


def solution(mesh):
    in_specs = (P(("veh", "req"), None), P("req", None), P("req", None), P("veh"), P("req"))
    out_specs = P(("veh", "req"), None)
    return jax.shard_map(local, mesh=mesh, in_specs=in_specs, out_specs=out_specs, check_vma=False)
```

```python
import functools
import math

import jax
import jax.numpy as jnp
from jax import lax
from jax.experimental import pallas as pl
from jax.experimental.pallas import tpu as pltpu
from jax.sharding import PartitionSpec as P


def merged_lse(parts):
    top = jnp.max(parts, axis=0)
    return top + jnp.log(jnp.sum(jnp.exp(parts - top[None]), axis=0))


def lse_kernel(*refs, scale, shifted, copies):
    if shifted:
        a_ref, parts_ref, base_ref, b_ref, out_ref, column_ref = refs

        @pl.when(pl.program_id(0) == 0)
        def _():
            row = base_ref[...] - merged_lse(parts_ref[...])
            wide = jnp.broadcast_to(row, (128, row.shape[1]))
            column_ref[...] = jnp.transpose(wide)[:, :1]

    else:
        a_ref, b_ref, out_ref = refs
    scores = lax.dot_general(
        a_ref[...], b_ref[...], (((1,), (1,)), ((), ())), preferred_element_type=jnp.float32
    )
    logits = scores * scale
    if shifted:
        logits = logits + column_ref[...]
    top = jnp.max(logits, axis=0, keepdims=True)
    total = jnp.sum(jnp.exp(logits - top), axis=0, keepdims=True)
    result = top + jnp.log(total)
    out_ref[...] = jnp.broadcast_to(result[None], (copies,) + result.shape)


def lse_over_rows(a, b, scale, tile, copies, vmem_limit, parts=None, base=None):
    rows, width = a.shape
    cols = b.shape[0]
    tile = min(tile, cols)
    shifted = parts is not None
    in_specs = [pl.BlockSpec((rows, width), lambda j: (0, 0))]
    operands = [a]
    scratch = []
    if shifted:
        in_specs += [
            pl.BlockSpec(parts.shape, lambda j: (0, 0, 0)),
            pl.BlockSpec((1, rows), lambda j: (0, 0)),
        ]
        operands += [parts, base.reshape(1, rows)]
        scratch = [pltpu.VMEM((rows, 1), jnp.float32)]
    in_specs.append(pl.BlockSpec((tile, width), lambda j: (j, 0)))
    operands.append(b)
    return pl.pallas_call(
        functools.partial(lse_kernel, scale=scale, shifted=shifted, copies=copies),
        out_shape=jax.ShapeDtypeStruct((copies, 1, cols), jnp.float32),
        grid=(cols // tile,),
        in_specs=in_specs,
        out_specs=pl.BlockSpec((copies, 1, tile), lambda j: (0, 0, j)),
        scratch_shapes=scratch,
        compiler_params=pltpu.CompilerParams(vmem_limit_bytes=vmem_limit),
        cost_estimate=pl.CostEstimate(
            flops=2 * rows * cols * width + 5 * rows * cols,
            transcendentals=rows * cols,
            bytes_accessed=2 * (rows + cols) * width + 4 * (rows + copies * cols),
        ),
    )(*operands)


def assign_kernel(
    rot_ref, v_ref, r_ref, parts_ref, base_ref, f_hbm, out_ref, f_ref, sem, *, scale
):
    fetch = pltpu.make_async_copy(f_hbm, f_ref, sem)
    fetch.start()
    demand = base_ref[...] - merged_lse(parts_ref[...])
    scores = lax.dot_general(
        v_ref[...], r_ref[...], (((1,), (1,)), ((), ())), preferred_element_type=jnp.float32
    )
    logits = scores * scale + demand
    top = jnp.max(logits, axis=1, keepdims=True)
    powers = jnp.exp(logits - top)
    mass = jnp.sum(powers, axis=1, keepdims=True)
    feat = f_ref.shape[1]
    fetch.wait()
    block_feat = jnp.dot(
        powers.astype(jnp.bfloat16), f_ref[...], preferred_element_type=jnp.float32
    )
    out_ref[:feat, :] = block_feat.T
    lane = lax.broadcasted_iota(jnp.int32, (top.shape[0], 128), 1)
    extra = jnp.where(lane == 0, mass, jnp.where(lane == 1, top, 0.0))
    out_ref[feat:, :] = extra.T[:8, :]


def assign_chunk(v, r, parts, base, f, scale, chunk, index):
    rows, width = v.shape
    cols, feat = f.shape
    grid_spec = pltpu.PrefetchScalarGridSpec(
        num_scalar_prefetch=1,
        grid=(1,),
        in_specs=[
            pl.BlockSpec((chunk, width), lambda i, at: (at[0], 0)),
            pl.BlockSpec((cols, width), lambda i, at: (0, 0)),
            pl.BlockSpec(parts.shape, lambda i, at: (0, 0, 0)),
            pl.BlockSpec((1, cols), lambda i, at: (0, 0)),
            pl.BlockSpec(memory_space=pl.ANY),
        ],
        out_specs=pl.BlockSpec((feat + 8, chunk), lambda i, at: (0, 0)),
        scratch_shapes=[pltpu.VMEM((cols, feat), f.dtype), pltpu.SemaphoreType.DMA(())],
    )
    return pl.pallas_call(
        functools.partial(assign_kernel, scale=scale),
        out_shape=jax.ShapeDtypeStruct((feat + 8, chunk), jnp.float32),
        grid_spec=grid_spec,
        compiler_params=pltpu.CompilerParams(vmem_limit_bytes=24 * 1024 * 1024),
        cost_estimate=pl.CostEstimate(
            flops=2 * chunk * cols * (width + feat) + 5 * chunk * cols,
            transcendentals=chunk * cols,
            bytes_accessed=2 * (chunk + cols) * width + 2 * cols * feat + 4 * chunk * (feat + 8),
        ),
    )(index, v, r, parts, base.reshape(1, cols), f)


def combine_kernel(*refs):
    piece_refs, out_ref = refs[:-1], refs[-1]
    feat = out_ref.shape[1]
    peaks = [ref[feat + 1 : feat + 2, :] for ref in piece_refs]
    top = peaks[0]
    for peak in peaks[1:]:
        top = jnp.maximum(top, peak)
    numerator = None
    denominator = None
    for ref, peak in zip(piece_refs, peaks):
        factor = jnp.exp(peak - top)
        term = ref[:feat, :] * factor
        mass = ref[feat : feat + 1, :] * factor
        numerator = term if numerator is None else numerator + term
        denominator = mass if denominator is None else denominator + mass
    out_ref[...] = (numerator / denominator).T


def combine(pieces, feat):
    chunk = pieces[0].shape[1]
    return pl.pallas_call(
        combine_kernel,
        out_shape=jax.ShapeDtypeStruct((chunk, feat), jnp.float32),
        in_specs=[pl.BlockSpec(piece.shape, lambda: (0, 0)) for piece in pieces],
        out_specs=pl.BlockSpec((chunk, feat), lambda: (0, 0)),
        cost_estimate=pl.CostEstimate(
            flops=3 * len(pieces) * chunk * feat,
            transcendentals=len(pieces) * chunk,
            bytes_accessed=4 * chunk * ((feat + 8) * len(pieces) + feat),
        ),
    )(*pieces)


def local(vehicle_emb, request_emb, request_feat, log_supply, log_demand):
    own_rows = lax.all_gather(vehicle_emb, "req", axis=0, tiled=True)
    row_count = own_rows.shape[0]
    scale = 3.0 / math.sqrt(own_rows.shape[1])
    spread = lax.axis_size("veh")

    def exchange(block):
        return lax.all_to_all(block, "veh", 0, 0, tiled=True)

    first = exchange(lse_over_rows(own_rows, request_emb, scale, 4096, spread, 24 << 20))
    partial = lse_over_rows(request_emb, own_rows, scale, 1024, 1, 48 << 20, first, log_demand)
    row_parts = lax.all_gather(partial[0], "req", axis=0, tiled=False)
    second = exchange(
        lse_over_rows(own_rows, request_emb, scale, 4096, spread, 24 << 20, row_parts, log_supply)
    )

    owners = lax.axis_size("req")
    chunk = row_count // owners
    me = lax.axis_index("req")
    feat = request_feat.shape[1]
    pieces = []
    for step in list(range(1, owners)) + [0]:
        index = jnp.reshape((me + step) % owners, (1,)).astype(jnp.int32)
        piece = assign_chunk(
            own_rows, request_emb, second, log_demand, request_feat, scale, chunk, index
        )
        if step:
            piece = lax.ppermute(piece, "req", [(i, (i + step) % owners) for i in range(owners)])
        pieces.append(piece)
    return combine(pieces, feat)


def solution(mesh):
    in_specs = (P(("veh", "req"), None), P("req", None), P("req", None), P("veh"), P("req"))
    out_specs = P(("veh", "req"), None)
    return jax.shard_map(local, mesh=mesh, in_specs=in_specs, out_specs=out_specs, check_vma=False)
```

```python
import functools
import math

import jax
import jax.numpy as jnp
from jax import lax
from jax.experimental import pallas as pl
from jax.experimental.pallas import tpu as pltpu
from jax.sharding import PartitionSpec as P


def merged_lse(parts):
    top = jnp.max(parts, axis=0)
    return top + jnp.log(jnp.sum(jnp.exp(parts - top[None]), axis=0))


def lse_kernel(*refs, scale, shifted, copies):
    if shifted:
        a_ref, parts_ref, base_ref, b_ref, out_ref, column_ref = refs

        @pl.when(pl.program_id(0) == 0)
        def _():
            row = base_ref[...] - merged_lse(parts_ref[...])
            wide = jnp.broadcast_to(row, (128, row.shape[1]))
            column_ref[...] = jnp.transpose(wide)[:, :1]

    else:
        a_ref, b_ref, out_ref = refs
    scores = lax.dot_general(
        a_ref[...], b_ref[...], (((1,), (1,)), ((), ())), preferred_element_type=jnp.float32
    )
    logits = scores * scale
    if shifted:
        logits = logits + column_ref[...]
    top = jnp.max(logits, axis=0, keepdims=True)
    total = jnp.sum(jnp.exp(logits - top), axis=0, keepdims=True)
    result = top + jnp.log(total)
    out_ref[...] = jnp.broadcast_to(result[None], (copies,) + result.shape)


def lse_over_rows(a, b, scale, tile, copies, vmem_limit, parts=None, base=None):
    rows, width = a.shape
    cols = b.shape[0]
    tile = min(tile, cols)
    shifted = parts is not None
    in_specs = [pl.BlockSpec((rows, width), lambda j: (0, 0))]
    operands = [a]
    scratch = []
    if shifted:
        in_specs += [
            pl.BlockSpec(parts.shape, lambda j: (0, 0, 0)),
            pl.BlockSpec((1, rows), lambda j: (0, 0)),
        ]
        operands += [parts, base.reshape(1, rows)]
        scratch = [pltpu.VMEM((rows, 1), jnp.float32)]
    in_specs.append(pl.BlockSpec((tile, width), lambda j: (j, 0)))
    operands.append(b)
    return pl.pallas_call(
        functools.partial(lse_kernel, scale=scale, shifted=shifted, copies=copies),
        out_shape=jax.ShapeDtypeStruct((copies, 1, cols), jnp.float32),
        grid=(cols // tile,),
        in_specs=in_specs,
        out_specs=pl.BlockSpec((copies, 1, tile), lambda j: (0, 0, j)),
        scratch_shapes=scratch,
        compiler_params=pltpu.CompilerParams(vmem_limit_bytes=vmem_limit),
        cost_estimate=pl.CostEstimate(
            flops=2 * rows * cols * width + 5 * rows * cols,
            transcendentals=rows * cols,
            bytes_accessed=2 * (rows + cols) * width + 4 * (rows + copies * cols),
        ),
    )(*operands)


def assign_kernel(
    at_ref, v_ref, r_ref, parts_ref, base_ref, f_hbm, out_ref, f_ref, sem, s_ref, p_ref, stat_ref,
    *, scale, step
):
    fetch = pltpu.make_async_copy(f_hbm, f_ref, sem)
    fetch.start()
    demand = base_ref[...] - merged_lse(parts_ref[...])
    scores = lax.dot_general(
        v_ref[...], r_ref[...], (((1,), (1,)), ((), ())), preferred_element_type=jnp.float32
    )
    s_ref[...] = scores * scale + demand

    def block(k, carry):
        start = pl.multiple_of(k * step, step)
        logits = s_ref[pl.ds(start, step), :]
        top = jnp.max(logits, axis=1, keepdims=True)
        powers = jnp.exp(logits - top)
        mass = jnp.sum(powers, axis=1, keepdims=True)
        p_ref[pl.ds(start, step), :] = powers.astype(jnp.bfloat16)
        lane = lax.broadcasted_iota(jnp.int32, (step, 128), 1)
        stat_ref[pl.ds(start, step), :] = jnp.where(lane == 0, mass, jnp.where(lane == 1, top, 0.0))
        return carry

    lax.fori_loop(0, s_ref.shape[0] // step, block, 0)
    feat = f_ref.shape[1]
    fetch.wait()
    block_feat = jnp.dot(p_ref[...], f_ref[...], preferred_element_type=jnp.float32)
    out_ref[:feat, :] = block_feat.T
    out_ref[feat:, :] = stat_ref[...].T[:8, :]


def assign_chunk(v, r, parts, base, f, scale, chunk, index):
    rows, width = v.shape
    cols, feat = f.shape
    grid_spec = pltpu.PrefetchScalarGridSpec(
        num_scalar_prefetch=1,
        grid=(1,),
        in_specs=[
            pl.BlockSpec((chunk, width), lambda i, at: (at[0], 0)),
            pl.BlockSpec((cols, width), lambda i, at: (0, 0)),
            pl.BlockSpec(parts.shape, lambda i, at: (0, 0, 0)),
            pl.BlockSpec((1, cols), lambda i, at: (0, 0)),
            pl.BlockSpec(memory_space=pl.ANY),
        ],
        out_specs=pl.BlockSpec((feat + 8, chunk), lambda i, at: (0, 0)),
        scratch_shapes=[
            pltpu.VMEM((cols, feat), f.dtype),
            pltpu.SemaphoreType.DMA(()),
            pltpu.VMEM((chunk, cols), jnp.float32),
            pltpu.VMEM((chunk, cols), jnp.bfloat16),
            pltpu.VMEM((chunk, 128), jnp.float32),
        ],
    )
    return pl.pallas_call(
        functools.partial(assign_kernel, scale=scale, step=16),
        out_shape=jax.ShapeDtypeStruct((feat + 8, chunk), jnp.float32),
        grid_spec=grid_spec,
        compiler_params=pltpu.CompilerParams(vmem_limit_bytes=24 * 1024 * 1024),
        cost_estimate=pl.CostEstimate(
            flops=2 * chunk * cols * (width + feat) + 5 * chunk * cols,
            transcendentals=chunk * cols,
            bytes_accessed=2 * (chunk + cols) * width + 2 * cols * feat + 4 * chunk * (feat + 8),
        ),
    )(index, v, r, parts, base.reshape(1, cols), f)


def combine_kernel(*refs):
    piece_refs, out_ref = refs[:-1], refs[-1]
    feat = out_ref.shape[1]
    peaks = [ref[feat + 1 : feat + 2, :] for ref in piece_refs]
    top = peaks[0]
    for peak in peaks[1:]:
        top = jnp.maximum(top, peak)
    numerator = None
    denominator = None
    for ref, peak in zip(piece_refs, peaks):
        factor = jnp.exp(peak - top)
        term = ref[:feat, :] * factor
        mass = ref[feat : feat + 1, :] * factor
        numerator = term if numerator is None else numerator + term
        denominator = mass if denominator is None else denominator + mass
    out_ref[...] = (numerator / denominator).T


def combine(pieces, feat):
    chunk = pieces[0].shape[1]
    return pl.pallas_call(
        combine_kernel,
        out_shape=jax.ShapeDtypeStruct((chunk, feat), jnp.float32),
        in_specs=[pl.BlockSpec(piece.shape, lambda: (0, 0)) for piece in pieces],
        out_specs=pl.BlockSpec((chunk, feat), lambda: (0, 0)),
        cost_estimate=pl.CostEstimate(
            flops=3 * len(pieces) * chunk * feat,
            transcendentals=len(pieces) * chunk,
            bytes_accessed=4 * chunk * ((feat + 8) * len(pieces) + feat),
        ),
    )(*pieces)


def local(vehicle_emb, request_emb, request_feat, log_supply, log_demand):
    own_rows = lax.all_gather(vehicle_emb, "req", axis=0, tiled=True)
    row_count = own_rows.shape[0]
    scale = 3.0 / math.sqrt(own_rows.shape[1])
    spread = lax.axis_size("veh")

    def exchange(block):
        return lax.all_to_all(block, "veh", 0, 0, tiled=True)

    first = exchange(lse_over_rows(own_rows, request_emb, scale, 4096, spread, 24 << 20))
    partial = lse_over_rows(request_emb, own_rows, scale, 1024, 1, 48 << 20, first, log_demand)
    row_parts = lax.all_gather(partial[0], "req", axis=0, tiled=False)
    second = exchange(
        lse_over_rows(own_rows, request_emb, scale, 4096, spread, 24 << 20, row_parts, log_supply)
    )

    owners = lax.axis_size("req")
    chunk = row_count // owners
    me = lax.axis_index("req")
    feat = request_feat.shape[1]
    pieces = []
    for step in list(range(1, owners)) + [0]:
        index = jnp.reshape((me + step) % owners, (1,)).astype(jnp.int32)
        piece = assign_chunk(
            own_rows, request_emb, second, log_demand, request_feat, scale, chunk, index
        )
        if step:
            piece = lax.ppermute(piece, "req", [(i, (i + step) % owners) for i in range(owners)])
        pieces.append(piece)
    return combine(pieces, feat)


def solution(mesh):
    in_specs = (P(("veh", "req"), None), P("req", None), P("req", None), P("veh"), P("req"))
    out_specs = P(("veh", "req"), None)
    return jax.shard_map(local, mesh=mesh, in_specs=in_specs, out_specs=out_specs, check_vma=False)
```

```python
import functools
import math

import jax
import jax.numpy as jnp
from jax import lax
from jax.experimental import pallas as pl
from jax.experimental.pallas import tpu as pltpu
from jax.sharding import PartitionSpec as P


def merged_lse(parts):
    top = jnp.max(parts, axis=0)
    return top + jnp.log(jnp.sum(jnp.exp(parts - top[None]), axis=0))


def lse_kernel(*refs, scale, shifted, copies):
    if shifted:
        a_ref, parts_ref, base_ref, b_ref, out_ref, column_ref = refs

        @pl.when(pl.program_id(0) == 0)
        def _():
            row = base_ref[...] - merged_lse(parts_ref[...])
            wide = jnp.broadcast_to(row, (128, row.shape[1]))
            column_ref[...] = jnp.transpose(wide)[:, :1]

    else:
        a_ref, b_ref, out_ref = refs
    scores = lax.dot_general(
        a_ref[...], b_ref[...], (((1,), (1,)), ((), ())), preferred_element_type=jnp.float32
    )
    logits = scores * scale
    if shifted:
        logits = logits + column_ref[...]
    top = jnp.max(logits, axis=0, keepdims=True)
    total = jnp.sum(jnp.exp(logits - top), axis=0, keepdims=True)
    result = top + jnp.log(total)
    out_ref[...] = jnp.broadcast_to(result[None], (copies,) + result.shape)


def lse_over_rows(a, b, scale, tile, copies, vmem_limit, parts=None, base=None):
    rows, width = a.shape
    cols = b.shape[0]
    tile = min(tile, cols)
    shifted = parts is not None
    in_specs = [pl.BlockSpec((rows, width), lambda j: (0, 0))]
    operands = [a]
    scratch = []
    if shifted:
        in_specs += [
            pl.BlockSpec(parts.shape, lambda j: (0, 0, 0)),
            pl.BlockSpec((1, rows), lambda j: (0, 0)),
        ]
        operands += [parts, base.reshape(1, rows)]
        scratch = [pltpu.VMEM((rows, 1), jnp.float32)]
    in_specs.append(pl.BlockSpec((tile, width), lambda j: (j, 0)))
    operands.append(b)
    return pl.pallas_call(
        functools.partial(lse_kernel, scale=scale, shifted=shifted, copies=copies),
        out_shape=jax.ShapeDtypeStruct((copies, 1, cols), jnp.float32),
        grid=(cols // tile,),
        in_specs=in_specs,
        out_specs=pl.BlockSpec((copies, 1, tile), lambda j: (0, 0, j)),
        scratch_shapes=scratch,
        compiler_params=pltpu.CompilerParams(vmem_limit_bytes=vmem_limit),
        cost_estimate=pl.CostEstimate(
            flops=2 * rows * cols * width + 5 * rows * cols,
            transcendentals=rows * cols,
            bytes_accessed=2 * (rows + cols) * width + 4 * (rows + copies * cols),
        ),
    )(*operands)


def row_kernel(a_ref, parts_ref, base_ref, b_ref, out_ref, *, scale):
    demand = base_ref[...] - merged_lse(parts_ref[...])
    scores = lax.dot_general(
        a_ref[...], b_ref[...], (((1,), (1,)), ((), ())), preferred_element_type=jnp.float32
    )
    logits = scores * scale + demand
    top = jnp.max(logits, axis=1, keepdims=True)
    total = jnp.sum(jnp.exp(logits - top), axis=1, keepdims=True)
    result = top + jnp.log(total)
    wide = jnp.broadcast_to(result, (result.shape[0], 128))
    out_ref[...] = jnp.transpose(wide)[:1, :][None]


def row_lse(a, b, scale, tile, vmem_limit, parts, base):
    rows, width = a.shape
    cols = b.shape[0]
    tile = min(tile, rows)
    return pl.pallas_call(
        functools.partial(row_kernel, scale=scale),
        out_shape=jax.ShapeDtypeStruct((1, 1, rows), jnp.float32),
        grid=(rows // tile,),
        in_specs=[
            pl.BlockSpec((tile, width), lambda i: (i, 0)),
            pl.BlockSpec(parts.shape, lambda i: (0, 0, 0)),
            pl.BlockSpec((1, cols), lambda i: (0, 0)),
            pl.BlockSpec((cols, width), lambda i: (0, 0)),
        ],
        out_specs=pl.BlockSpec((1, 1, tile), lambda i: (0, 0, i)),
        compiler_params=pltpu.CompilerParams(vmem_limit_bytes=vmem_limit),
        cost_estimate=pl.CostEstimate(
            flops=2 * rows * cols * width + 5 * rows * cols,
            transcendentals=rows * cols,
            bytes_accessed=2 * (rows + cols) * width + 4 * (rows + 9 * cols),
        ),
    )(a, parts, base.reshape(1, cols), b)


def assign_kernel(
    rot_ref, v_ref, r_ref, parts_ref, base_ref, f_hbm, out_ref, f_ref, sem, *, scale
):
    fetch = pltpu.make_async_copy(f_hbm, f_ref, sem)
    fetch.start()
    demand = base_ref[...] - merged_lse(parts_ref[...])
    scores = lax.dot_general(
        v_ref[...], r_ref[...], (((1,), (1,)), ((), ())), preferred_element_type=jnp.float32
    )
    logits = scores * scale + demand
    top = jnp.max(logits, axis=1, keepdims=True)
    powers = jnp.exp(logits - top)
    mass = jnp.sum(powers, axis=1, keepdims=True)
    feat = f_ref.shape[1]
    fetch.wait()
    block_feat = jnp.dot(
        powers.astype(jnp.bfloat16), f_ref[...], preferred_element_type=jnp.float32
    )
    out_ref[:feat, :] = block_feat.T
    lane = lax.broadcasted_iota(jnp.int32, (top.shape[0], 128), 1)
    extra = jnp.where(lane == 0, mass, jnp.where(lane == 1, top, 0.0))
    out_ref[feat:, :] = extra.T[:8, :]


def assign_chunk(v, r, parts, base, f, scale, chunk, index):
    rows, width = v.shape
    cols, feat = f.shape
    grid_spec = pltpu.PrefetchScalarGridSpec(
        num_scalar_prefetch=1,
        grid=(1,),
        in_specs=[
            pl.BlockSpec((chunk, width), lambda i, at: (at[0], 0)),
            pl.BlockSpec((cols, width), lambda i, at: (0, 0)),
            pl.BlockSpec(parts.shape, lambda i, at: (0, 0, 0)),
            pl.BlockSpec((1, cols), lambda i, at: (0, 0)),
            pl.BlockSpec(memory_space=pl.ANY),
        ],
        out_specs=pl.BlockSpec((feat + 8, chunk), lambda i, at: (0, 0)),
        scratch_shapes=[pltpu.VMEM((cols, feat), f.dtype), pltpu.SemaphoreType.DMA(())],
    )
    return pl.pallas_call(
        functools.partial(assign_kernel, scale=scale),
        out_shape=jax.ShapeDtypeStruct((feat + 8, chunk), jnp.float32),
        grid_spec=grid_spec,
        compiler_params=pltpu.CompilerParams(vmem_limit_bytes=24 * 1024 * 1024),
        cost_estimate=pl.CostEstimate(
            flops=2 * chunk * cols * (width + feat) + 5 * chunk * cols,
            transcendentals=chunk * cols,
            bytes_accessed=2 * (chunk + cols) * width + 2 * cols * feat + 4 * chunk * (feat + 8),
        ),
    )(index, v, r, parts, base.reshape(1, cols), f)


def combine_kernel(*refs):
    piece_refs, out_ref = refs[:-1], refs[-1]
    feat = out_ref.shape[1]
    peaks = [ref[feat + 1 : feat + 2, :] for ref in piece_refs]
    top = peaks[0]
    for peak in peaks[1:]:
        top = jnp.maximum(top, peak)
    numerator = None
    denominator = None
    for ref, peak in zip(piece_refs, peaks):
        factor = jnp.exp(peak - top)
        term = ref[:feat, :] * factor
        mass = ref[feat : feat + 1, :] * factor
        numerator = term if numerator is None else numerator + term
        denominator = mass if denominator is None else denominator + mass
    out_ref[...] = (numerator / denominator).T


def combine(pieces, feat):
    chunk = pieces[0].shape[1]
    width = min(128, chunk)
    return pl.pallas_call(
        combine_kernel,
        out_shape=jax.ShapeDtypeStruct((chunk, feat), jnp.float32),
        grid=(chunk // width,),
        in_specs=[pl.BlockSpec((feat + 8, width), lambda j: (0, j)) for piece in pieces],
        out_specs=pl.BlockSpec((width, feat), lambda j: (j, 0)),
        cost_estimate=pl.CostEstimate(
            flops=3 * len(pieces) * chunk * feat,
            transcendentals=len(pieces) * chunk,
            bytes_accessed=4 * chunk * ((feat + 8) * len(pieces) + feat),
        ),
    )(*pieces)


def local(vehicle_emb, request_emb, request_feat, log_supply, log_demand):
    own_rows = lax.all_gather(vehicle_emb, "req", axis=0, tiled=True)
    row_count = own_rows.shape[0]
    scale = 3.0 / math.sqrt(own_rows.shape[1])
    spread = lax.axis_size("veh")

    def exchange(block):
        return lax.all_to_all(block, "veh", 0, 0, tiled=True)

    first = exchange(lse_over_rows(own_rows, request_emb, scale, 4096, spread, 24 << 20))
    partial = row_lse(own_rows, request_emb, scale, 1024, 48 << 20, first, log_demand)
    row_parts = lax.all_gather(partial[0], "req", axis=0, tiled=False)
    second = exchange(
        lse_over_rows(own_rows, request_emb, scale, 4096, spread, 24 << 20, row_parts, log_supply)
    )

    owners = lax.axis_size("req")
    chunk = row_count // owners
    me = lax.axis_index("req")
    feat = request_feat.shape[1]
    pieces = []
    for step in list(range(1, owners)) + [0]:
        index = jnp.reshape((me + step) % owners, (1,)).astype(jnp.int32)
        piece = assign_chunk(
            own_rows, request_emb, second, log_demand, request_feat, scale, chunk, index
        )
        if step:
            piece = lax.ppermute(piece, "req", [(i, (i + step) % owners) for i in range(owners)])
        pieces.append(piece)
    return combine(pieces, feat)


def solution(mesh):
    in_specs = (P(("veh", "req"), None), P("req", None), P("req", None), P("veh"), P("req"))
    out_specs = P(("veh", "req"), None)
    return jax.shard_map(local, mesh=mesh, in_specs=in_specs, out_specs=out_specs, check_vma=False)
```

```python
import functools
import math

import jax
import jax.numpy as jnp
from jax import lax
from jax.experimental import pallas as pl
from jax.experimental.pallas import tpu as pltpu
from jax.sharding import PartitionSpec as P


def merged_lse(parts):
    top = jnp.max(parts, axis=0)
    return top + jnp.log(jnp.sum(jnp.exp(parts - top[None]), axis=0))


def lse_kernel(*refs, scale, shifted, copies):
    if shifted:
        a_ref, parts_ref, base_ref, b_ref, out_ref, column_ref = refs

        @pl.when(pl.program_id(0) == 0)
        def _():
            row = base_ref[...] - merged_lse(parts_ref[...])
            wide = jnp.broadcast_to(row, (128, row.shape[1]))
            column_ref[...] = jnp.transpose(wide)[:, :1]

    else:
        a_ref, b_ref, out_ref = refs
    scores = lax.dot_general(
        a_ref[...], b_ref[...], (((1,), (1,)), ((), ())), preferred_element_type=jnp.float32
    )
    logits = scores * scale
    if shifted:
        logits = logits + column_ref[...]
    top = jnp.max(logits, axis=0, keepdims=True)
    total = jnp.sum(jnp.exp(logits - top), axis=0, keepdims=True)
    result = top + jnp.log(total)
    out_ref[...] = jnp.broadcast_to(result[None], (copies,) + result.shape)


def lse_over_rows(a, b, scale, tile, copies, vmem_limit, parts=None, base=None):
    rows, width = a.shape
    cols = b.shape[0]
    tile = min(tile, cols)
    shifted = parts is not None
    in_specs = [pl.BlockSpec((rows, width), lambda j: (0, 0))]
    operands = [a]
    scratch = []
    if shifted:
        in_specs += [
            pl.BlockSpec(parts.shape, lambda j: (0, 0, 0)),
            pl.BlockSpec((1, rows), lambda j: (0, 0)),
        ]
        operands += [parts, base.reshape(1, rows)]
        scratch = [pltpu.VMEM((rows, 1), jnp.float32)]
    in_specs.append(pl.BlockSpec((tile, width), lambda j: (j, 0)))
    operands.append(b)
    return pl.pallas_call(
        functools.partial(lse_kernel, scale=scale, shifted=shifted, copies=copies),
        out_shape=jax.ShapeDtypeStruct((copies, 1, cols), jnp.float32),
        grid=(cols // tile,),
        in_specs=in_specs,
        out_specs=pl.BlockSpec((copies, 1, tile), lambda j: (0, 0, j)),
        scratch_shapes=scratch,
        compiler_params=pltpu.CompilerParams(vmem_limit_bytes=vmem_limit),
        cost_estimate=pl.CostEstimate(
            flops=2 * rows * cols * width + 5 * rows * cols,
            transcendentals=rows * cols,
            bytes_accessed=2 * (rows + cols) * width + 4 * (rows + copies * cols),
        ),
    )(*operands)


def row_kernel(a_ref, parts_ref, base_ref, b_ref, out_ref, *, scale):
    demand = base_ref[...] - merged_lse(parts_ref[...])
    scores = lax.dot_general(
        a_ref[...], b_ref[...], (((1,), (1,)), ((), ())), preferred_element_type=jnp.float32
    )
    logits = scores * scale + demand
    top = jnp.max(logits, axis=1, keepdims=True)
    total = jnp.sum(jnp.exp(logits - top), axis=1, keepdims=True)
    result = top + jnp.log(total)
    wide = jnp.broadcast_to(result, (result.shape[0], 128))
    out_ref[...] = jnp.transpose(wide)[:1, :][None]


def row_lse(a, b, scale, tile, vmem_limit, parts, base):
    rows, width = a.shape
    cols = b.shape[0]
    tile = min(tile, rows)
    return pl.pallas_call(
        functools.partial(row_kernel, scale=scale),
        out_shape=jax.ShapeDtypeStruct((1, 1, rows), jnp.float32),
        grid=(rows // tile,),
        in_specs=[
            pl.BlockSpec((tile, width), lambda i: (i, 0)),
            pl.BlockSpec(parts.shape, lambda i: (0, 0, 0)),
            pl.BlockSpec((1, cols), lambda i: (0, 0)),
            pl.BlockSpec((cols, width), lambda i: (0, 0)),
        ],
        out_specs=pl.BlockSpec((1, 1, tile), lambda i: (0, 0, i)),
        compiler_params=pltpu.CompilerParams(vmem_limit_bytes=vmem_limit),
        cost_estimate=pl.CostEstimate(
            flops=2 * rows * cols * width + 5 * rows * cols,
            transcendentals=rows * cols,
            bytes_accessed=2 * (rows + cols) * width + 4 * (rows + 9 * cols),
        ),
    )(a, parts, base.reshape(1, cols), b)


def assign_kernel(
    rot_ref, v_ref, r_ref, parts_ref, base_ref, f_hbm, out_ref, f_ref, sem, *, scale
):
    fetch = pltpu.make_async_copy(f_hbm, f_ref, sem)
    fetch.start()
    demand = base_ref[...] - merged_lse(parts_ref[...])
    scores = lax.dot_general(
        v_ref[...], r_ref[...], (((1,), (1,)), ((), ())), preferred_element_type=jnp.float32
    )
    logits = scores * scale + demand
    top = jnp.max(logits, axis=1, keepdims=True)
    powers = jnp.exp(logits - top)
    mass = jnp.sum(powers, axis=1, keepdims=True)
    feat = f_ref.shape[1]
    fetch.wait()
    block_feat = jnp.dot(
        powers.astype(jnp.bfloat16), f_ref[...], preferred_element_type=jnp.float32
    )
    out_ref[:feat, :] = block_feat.T
    lane = lax.broadcasted_iota(jnp.int32, (top.shape[0], 128), 1)
    extra = jnp.where(lane == 0, mass, jnp.where(lane == 1, top, 0.0))
    out_ref[feat:, :] = extra.T[:8, :]


def assign_chunk(v, r, parts, base, f, scale, chunk, index):
    rows, width = v.shape
    cols, feat = f.shape
    grid_spec = pltpu.PrefetchScalarGridSpec(
        num_scalar_prefetch=1,
        grid=(1,),
        in_specs=[
            pl.BlockSpec((chunk, width), lambda i, at: (at[0], 0)),
            pl.BlockSpec((cols, width), lambda i, at: (0, 0)),
            pl.BlockSpec(parts.shape, lambda i, at: (0, 0, 0)),
            pl.BlockSpec((1, cols), lambda i, at: (0, 0)),
            pl.BlockSpec(memory_space=pl.ANY),
        ],
        out_specs=pl.BlockSpec((feat + 8, chunk), lambda i, at: (0, 0)),
        scratch_shapes=[pltpu.VMEM((cols, feat), f.dtype), pltpu.SemaphoreType.DMA(())],
    )
    return pl.pallas_call(
        functools.partial(assign_kernel, scale=scale),
        out_shape=jax.ShapeDtypeStruct((feat + 8, chunk), jnp.float32),
        grid_spec=grid_spec,
        compiler_params=pltpu.CompilerParams(vmem_limit_bytes=24 * 1024 * 1024),
        cost_estimate=pl.CostEstimate(
            flops=2 * chunk * cols * (width + feat) + 5 * chunk * cols,
            transcendentals=chunk * cols,
            bytes_accessed=2 * (chunk + cols) * width + 2 * cols * feat + 4 * chunk * (feat + 8),
        ),
    )(index, v, r, parts, base.reshape(1, cols), f)


def combine_kernel(*refs):
    piece_refs, out_ref = refs[:-1], refs[-1]
    feat = out_ref.shape[1]
    peaks = [ref[feat + 1 : feat + 2, :] for ref in piece_refs]
    top = peaks[0]
    for peak in peaks[1:]:
        top = jnp.maximum(top, peak)
    numerator = None
    denominator = None
    for ref, peak in zip(piece_refs, peaks):
        factor = jnp.exp(peak - top)
        term = ref[:feat, :] * factor
        mass = ref[feat : feat + 1, :] * factor
        numerator = term if numerator is None else numerator + term
        denominator = mass if denominator is None else denominator + mass
    out_ref[...] = (numerator / denominator).T


def combine(pieces, feat):
    chunk = pieces[0].shape[1]
    width = min(128, chunk)
    return pl.pallas_call(
        combine_kernel,
        out_shape=jax.ShapeDtypeStruct((chunk, feat), jnp.float32),
        grid=(chunk // width,),
        in_specs=[pl.BlockSpec((feat + 8, width), lambda j: (0, j)) for piece in pieces],
        out_specs=pl.BlockSpec((width, feat), lambda j: (j, 0)),
        cost_estimate=pl.CostEstimate(
            flops=3 * len(pieces) * chunk * feat,
            transcendentals=len(pieces) * chunk,
            bytes_accessed=4 * chunk * ((feat + 8) * len(pieces) + feat),
        ),
    )(*pieces)


def local(vehicle_emb, request_emb, request_feat, log_supply, log_demand):
    own_rows = lax.all_gather(vehicle_emb, "req", axis=0, tiled=True)
    row_count = own_rows.shape[0]
    scale = 3.0 / math.sqrt(own_rows.shape[1])
    spread = lax.axis_size("veh")

    def exchange(block):
        return lax.all_to_all(block, "veh", 0, 0, tiled=True)

    first = exchange(lse_over_rows(own_rows, request_emb, scale, 4096, spread, 24 << 20))
    partial = row_lse(own_rows, request_emb, scale, 512, 48 << 20, first, log_demand)
    row_parts = lax.all_gather(partial[0], "req", axis=0, tiled=False)
    second = exchange(
        lse_over_rows(own_rows, request_emb, scale, 4096, spread, 24 << 20, row_parts, log_supply)
    )

    owners = lax.axis_size("req")
    chunk = row_count // owners
    me = lax.axis_index("req")
    feat = request_feat.shape[1]
    pieces = []
    for step in list(range(1, owners)) + [0]:
        index = jnp.reshape((me + step) % owners, (1,)).astype(jnp.int32)
        piece = assign_chunk(
            own_rows, request_emb, second, log_demand, request_feat, scale, chunk, index
        )
        if step:
            piece = lax.ppermute(piece, "req", [(i, (i + step) % owners) for i in range(owners)])
        pieces.append(piece)
    return combine(pieces, feat)


def solution(mesh):
    in_specs = (P(("veh", "req"), None), P("req", None), P("req", None), P("veh"), P("req"))
    out_specs = P(("veh", "req"), None)
    return jax.shard_map(local, mesh=mesh, in_specs=in_specs, out_specs=out_specs, check_vma=False)
```

```python
import functools
import math

import jax
import jax.numpy as jnp
from jax import lax
from jax.experimental import pallas as pl
from jax.experimental.pallas import tpu as pltpu
from jax.sharding import PartitionSpec as P


def merged_lse(parts):
    top = jnp.max(parts, axis=0)
    return top + jnp.log(jnp.sum(jnp.exp(parts - top[None]), axis=0))


def lse_kernel(*refs, scale, shifted, copies):
    if shifted:
        a_ref, parts_ref, base_ref, b_ref, out_ref, column_ref = refs

        @pl.when(pl.program_id(0) == 0)
        def _():
            row = base_ref[...] - merged_lse(parts_ref[...])
            wide = jnp.broadcast_to(row, (128, row.shape[1]))
            column_ref[...] = jnp.transpose(wide)[:, :1]

    else:
        a_ref, b_ref, out_ref = refs
    scores = lax.dot_general(
        a_ref[...], b_ref[...], (((1,), (1,)), ((), ())), preferred_element_type=jnp.float32
    )
    logits = scores * scale
    if shifted:
        logits = logits + column_ref[...]
    top = jnp.max(logits, axis=0, keepdims=True)
    total = jnp.sum(jnp.exp(logits - top), axis=0, keepdims=True)
    result = top + jnp.log(total)
    out_ref[...] = jnp.broadcast_to(result[None], (copies,) + result.shape)


def lse_over_rows(a, b, scale, tile, copies, vmem_limit, parts=None, base=None):
    rows, width = a.shape
    cols = b.shape[0]
    tile = min(tile, cols)
    shifted = parts is not None
    in_specs = [pl.BlockSpec((rows, width), lambda j: (0, 0))]
    operands = [a]
    scratch = []
    if shifted:
        in_specs += [
            pl.BlockSpec(parts.shape, lambda j: (0, 0, 0)),
            pl.BlockSpec((1, rows), lambda j: (0, 0)),
        ]
        operands += [parts, base.reshape(1, rows)]
        scratch = [pltpu.VMEM((rows, 1), jnp.float32)]
    in_specs.append(pl.BlockSpec((tile, width), lambda j: (j, 0)))
    operands.append(b)
    return pl.pallas_call(
        functools.partial(lse_kernel, scale=scale, shifted=shifted, copies=copies),
        out_shape=jax.ShapeDtypeStruct((copies, 1, cols), jnp.float32),
        grid=(cols // tile,),
        in_specs=in_specs,
        out_specs=pl.BlockSpec((copies, 1, tile), lambda j: (0, 0, j)),
        scratch_shapes=scratch,
        compiler_params=pltpu.CompilerParams(vmem_limit_bytes=vmem_limit),
        cost_estimate=pl.CostEstimate(
            flops=2 * rows * cols * width + 5 * rows * cols,
            transcendentals=rows * cols,
            bytes_accessed=2 * (rows + cols) * width + 4 * (rows + copies * cols),
        ),
    )(*operands)


def row_kernel(a_ref, parts_ref, base_ref, b_ref, out_ref, *, scale):
    demand = base_ref[...] - merged_lse(parts_ref[...])
    scores = lax.dot_general(
        a_ref[...], b_ref[...], (((1,), (1,)), ((), ())), preferred_element_type=jnp.float32
    )
    logits = scores * scale + demand
    top = jnp.max(logits, axis=1, keepdims=True)
    total = jnp.sum(jnp.exp(logits - top), axis=1, keepdims=True)
    result = top + jnp.log(total)
    wide = jnp.broadcast_to(result, (result.shape[0], 128))
    out_ref[...] = jnp.transpose(wide)[:1, :][None]


def row_lse(a, b, scale, tile, vmem_limit, parts, base):
    rows, width = a.shape
    cols = b.shape[0]
    tile = min(tile, rows)
    return pl.pallas_call(
        functools.partial(row_kernel, scale=scale),
        out_shape=jax.ShapeDtypeStruct((1, 1, rows), jnp.float32),
        grid=(rows // tile,),
        in_specs=[
            pl.BlockSpec((tile, width), lambda i: (i, 0)),
            pl.BlockSpec(parts.shape, lambda i: (0, 0, 0)),
            pl.BlockSpec((1, cols), lambda i: (0, 0)),
            pl.BlockSpec((cols, width), lambda i: (0, 0)),
        ],
        out_specs=pl.BlockSpec((1, 1, tile), lambda i: (0, 0, i)),
        compiler_params=pltpu.CompilerParams(vmem_limit_bytes=vmem_limit),
        cost_estimate=pl.CostEstimate(
            flops=2 * rows * cols * width + 5 * rows * cols,
            transcendentals=rows * cols,
            bytes_accessed=2 * (rows + cols) * width + 4 * (rows + 9 * cols),
        ),
    )(a, parts, base.reshape(1, cols), b)


def assign_kernel(
    rot_ref, v_ref, r_ref, parts_ref, base_ref, f_hbm, out_ref, f_ref, sem, *, scale
):
    fetch = pltpu.make_async_copy(f_hbm, f_ref, sem)
    fetch.start()
    demand = base_ref[...] - merged_lse(parts_ref[...])
    scores = lax.dot_general(
        v_ref[...], r_ref[...], (((1,), (1,)), ((), ())), preferred_element_type=jnp.float32
    )
    logits = scores * scale + demand
    top = jnp.max(logits, axis=1, keepdims=True)
    powers = jnp.exp(logits - top)
    mass = jnp.sum(powers, axis=1, keepdims=True)
    feat = f_ref.shape[1]
    fetch.wait()
    block_feat = jnp.dot(
        powers.astype(jnp.bfloat16), f_ref[...], preferred_element_type=jnp.float32
    )
    out_ref[:feat, :] = block_feat.T
    lane = lax.broadcasted_iota(jnp.int32, (top.shape[0], 128), 1)
    extra = jnp.where(lane == 0, mass, jnp.where(lane == 1, top, 0.0))
    out_ref[feat:, :] = extra.T[:8, :]


def assign_chunk(v, r, parts, base, f, scale, chunk, index):
    rows, width = v.shape
    cols, feat = f.shape
    grid_spec = pltpu.PrefetchScalarGridSpec(
        num_scalar_prefetch=1,
        grid=(1,),
        in_specs=[
            pl.BlockSpec((chunk, width), lambda i, at: (at[0], 0)),
            pl.BlockSpec((cols, width), lambda i, at: (0, 0)),
            pl.BlockSpec(parts.shape, lambda i, at: (0, 0, 0)),
            pl.BlockSpec((1, cols), lambda i, at: (0, 0)),
            pl.BlockSpec(memory_space=pl.ANY),
        ],
        out_specs=pl.BlockSpec((feat + 8, chunk), lambda i, at: (0, 0)),
        scratch_shapes=[pltpu.VMEM((cols, feat), f.dtype), pltpu.SemaphoreType.DMA(())],
    )
    return pl.pallas_call(
        functools.partial(assign_kernel, scale=scale),
        out_shape=jax.ShapeDtypeStruct((feat + 8, chunk), jnp.float32),
        grid_spec=grid_spec,
        compiler_params=pltpu.CompilerParams(vmem_limit_bytes=24 * 1024 * 1024),
        cost_estimate=pl.CostEstimate(
            flops=2 * chunk * cols * (width + feat) + 5 * chunk * cols,
            transcendentals=chunk * cols,
            bytes_accessed=2 * (chunk + cols) * width + 2 * cols * feat + 4 * chunk * (feat + 8),
        ),
    )(index, v, r, parts, base.reshape(1, cols), f)


def combine_kernel(*refs):
    piece_refs, out_ref = refs[:-1], refs[-1]
    feat = out_ref.shape[1]
    peaks = [ref[feat + 1 : feat + 2, :] for ref in piece_refs]
    top = peaks[0]
    for peak in peaks[1:]:
        top = jnp.maximum(top, peak)
    numerator = None
    denominator = None
    for ref, peak in zip(piece_refs, peaks):
        factor = jnp.exp(peak - top)
        term = ref[:feat, :] * factor
        mass = ref[feat : feat + 1, :] * factor
        numerator = term if numerator is None else numerator + term
        denominator = mass if denominator is None else denominator + mass
    out_ref[...] = (numerator / denominator).T


def combine(pieces, feat):
    chunk = pieces[0].shape[1]
    width = min(128, chunk)
    return pl.pallas_call(
        combine_kernel,
        out_shape=jax.ShapeDtypeStruct((chunk, feat), jnp.float32),
        grid=(chunk // width,),
        in_specs=[pl.BlockSpec((feat + 8, width), lambda j: (0, j)) for piece in pieces],
        out_specs=pl.BlockSpec((width, feat), lambda j: (j, 0)),
        cost_estimate=pl.CostEstimate(
            flops=3 * len(pieces) * chunk * feat,
            transcendentals=len(pieces) * chunk,
            bytes_accessed=4 * chunk * ((feat + 8) * len(pieces) + feat),
        ),
    )(*pieces)


def local(vehicle_emb, request_emb, request_feat, log_supply, log_demand):
    own_rows = lax.all_gather(vehicle_emb, "req", axis=0, tiled=True)
    row_count = own_rows.shape[0]
    scale = 3.0 / math.sqrt(own_rows.shape[1])
    spread = lax.axis_size("veh")

    def exchange(block):
        return lax.all_to_all(block, "veh", 0, 0, tiled=True)

    first = exchange(lse_over_rows(own_rows, request_emb, scale, 4096, spread, 24 << 20))
    partial = row_lse(own_rows, request_emb, scale, 1024, 48 << 20, first, log_demand)
    row_parts = lax.all_gather(partial[0], "req", axis=0, tiled=False)
    second = exchange(
        lse_over_rows(own_rows, request_emb, scale, 4096, spread, 24 << 20, row_parts, log_supply)
    )

    owners = lax.axis_size("req")
    chunk = row_count // owners
    me = lax.axis_index("req")
    feat = request_feat.shape[1]
    if owners & (owners - 1) == 0:
        order = [(step, lambda i, m=step: i ^ m) for step in list(range(2, owners)) + [1]]
    else:
        order = [(step, lambda i, m=step: (i + m) % owners) for step in range(1, owners)]
    pieces = []
    for step, partner in order + [(0, None)]:
        index = jnp.reshape(partner(me) if step else me, (1,)).astype(jnp.int32)
        piece = assign_chunk(
            own_rows, request_emb, second, log_demand, request_feat, scale, chunk, index
        )
        if step:
            piece = lax.ppermute(piece, "req", [(i, partner(i)) for i in range(owners)])
        pieces.append(piece)
    return combine(pieces, feat)


def solution(mesh):
    in_specs = (P(("veh", "req"), None), P("req", None), P("req", None), P("veh"), P("req"))
    out_specs = P(("veh", "req"), None)
    return jax.shard_map(local, mesh=mesh, in_specs=in_specs, out_specs=out_specs, check_vma=False)
```

```python
import functools
import math

import jax
import jax.numpy as jnp
from jax import lax
from jax.experimental import pallas as pl
from jax.experimental.pallas import tpu as pltpu
from jax.sharding import PartitionSpec as P


def merged_lse(parts):
    top = jnp.max(parts, axis=0)
    return top + jnp.log(jnp.sum(jnp.exp(parts - top[None]), axis=0))


def lse_kernel(*refs, scale, shifted, copies):
    if shifted:
        a_ref, parts_ref, base_ref, b_ref, out_ref, column_ref = refs

        @pl.when(pl.program_id(0) == 0)
        def _():
            row = base_ref[...] - merged_lse(parts_ref[...])
            wide = jnp.broadcast_to(row, (128, row.shape[1]))
            column_ref[...] = jnp.transpose(wide)[:, :1]

    else:
        a_ref, b_ref, out_ref = refs
    scores = lax.dot_general(
        a_ref[...], b_ref[...], (((1,), (1,)), ((), ())), preferred_element_type=jnp.float32
    )
    logits = scores * scale
    if shifted:
        logits = logits + column_ref[...]
    top = jnp.max(logits, axis=0, keepdims=True)
    total = jnp.sum(jnp.exp(logits - top), axis=0, keepdims=True)
    result = top + jnp.log(total)
    out_ref[...] = jnp.broadcast_to(result[None], (copies,) + result.shape)


def lse_over_rows(a, b, scale, tile, copies, vmem_limit, parts=None, base=None):
    rows, width = a.shape
    cols = b.shape[0]
    tile = min(tile, cols)
    shifted = parts is not None
    in_specs = [pl.BlockSpec((rows, width), lambda j: (0, 0))]
    operands = [a]
    scratch = []
    if shifted:
        in_specs += [
            pl.BlockSpec(parts.shape, lambda j: (0, 0, 0)),
            pl.BlockSpec((1, rows), lambda j: (0, 0)),
        ]
        operands += [parts, base.reshape(1, rows)]
        scratch = [pltpu.VMEM((rows, 1), jnp.float32)]
    in_specs.append(pl.BlockSpec((tile, width), lambda j: (j, 0)))
    operands.append(b)
    return pl.pallas_call(
        functools.partial(lse_kernel, scale=scale, shifted=shifted, copies=copies),
        out_shape=jax.ShapeDtypeStruct((copies, 1, cols), jnp.float32),
        grid=(cols // tile,),
        in_specs=in_specs,
        out_specs=pl.BlockSpec((copies, 1, tile), lambda j: (0, 0, j)),
        scratch_shapes=scratch,
        compiler_params=pltpu.CompilerParams(vmem_limit_bytes=vmem_limit),
        cost_estimate=pl.CostEstimate(
            flops=2 * rows * cols * width + 5 * rows * cols,
            transcendentals=rows * cols,
            bytes_accessed=2 * (rows + cols) * width + 4 * (rows + copies * cols),
        ),
    )(*operands)


def row_kernel(a_ref, parts_ref, base_ref, b_ref, out_ref, *, scale):
    demand = base_ref[...] - merged_lse(parts_ref[...])
    scores = lax.dot_general(
        a_ref[...], b_ref[...], (((1,), (1,)), ((), ())), preferred_element_type=jnp.float32
    )
    logits = scores * scale + demand
    top = jnp.max(logits, axis=1, keepdims=True)
    total = jnp.sum(jnp.exp(logits - top), axis=1, keepdims=True)
    result = top + jnp.log(total)
    wide = jnp.broadcast_to(result, (result.shape[0], 128))
    out_ref[...] = jnp.transpose(wide)[:1, :][None]


def row_lse(a, b, scale, tile, vmem_limit, parts, base):
    rows, width = a.shape
    cols = b.shape[0]
    tile = min(tile, rows)
    return pl.pallas_call(
        functools.partial(row_kernel, scale=scale),
        out_shape=jax.ShapeDtypeStruct((1, 1, rows), jnp.float32),
        grid=(rows // tile,),
        in_specs=[
            pl.BlockSpec((tile, width), lambda i: (i, 0)),
            pl.BlockSpec(parts.shape, lambda i: (0, 0, 0)),
            pl.BlockSpec((1, cols), lambda i: (0, 0)),
            pl.BlockSpec((cols, width), lambda i: (0, 0)),
        ],
        out_specs=pl.BlockSpec((1, 1, tile), lambda i: (0, 0, i)),
        compiler_params=pltpu.CompilerParams(vmem_limit_bytes=vmem_limit),
        cost_estimate=pl.CostEstimate(
            flops=2 * rows * cols * width + 5 * rows * cols,
            transcendentals=rows * cols,
            bytes_accessed=2 * (rows + cols) * width + 4 * (rows + 9 * cols),
        ),
    )(a, parts, base.reshape(1, cols), b)


def assign_kernel(
    rot_ref, v_ref, r_ref, parts_ref, base_ref, f_hbm, out_ref, f_ref, sem, *, scale
):
    fetch = pltpu.make_async_copy(f_hbm, f_ref, sem)
    fetch.start()
    demand = base_ref[...] - merged_lse(parts_ref[...])
    scores = lax.dot_general(
        v_ref[...], r_ref[...], (((1,), (1,)), ((), ())), preferred_element_type=jnp.float32
    )
    logits = scores * scale + demand
    top = jnp.max(logits, axis=1, keepdims=True)
    powers = jnp.exp(logits - top)
    mass = jnp.sum(powers, axis=1, keepdims=True)
    feat = f_ref.shape[1]
    fetch.wait()
    block_feat = jnp.dot(
        powers.astype(jnp.bfloat16), f_ref[...], preferred_element_type=jnp.float32
    )
    out_ref[:feat, :] = block_feat.T
    lane = lax.broadcasted_iota(jnp.int32, (top.shape[0], 128), 1)
    extra = jnp.where(lane == 0, mass, jnp.where(lane == 1, top, 0.0))
    out_ref[feat:, :] = extra.T[:8, :]


def assign_chunk(v, r, parts, base, f, scale, chunk, index):
    rows, width = v.shape
    cols, feat = f.shape
    grid_spec = pltpu.PrefetchScalarGridSpec(
        num_scalar_prefetch=1,
        grid=(1,),
        in_specs=[
            pl.BlockSpec((chunk, width), lambda i, at: (at[0], 0)),
            pl.BlockSpec((cols, width), lambda i, at: (0, 0)),
            pl.BlockSpec(parts.shape, lambda i, at: (0, 0, 0)),
            pl.BlockSpec((1, cols), lambda i, at: (0, 0)),
            pl.BlockSpec(memory_space=pl.ANY),
        ],
        out_specs=pl.BlockSpec((feat + 8, chunk), lambda i, at: (0, 0)),
        scratch_shapes=[pltpu.VMEM((cols, feat), f.dtype), pltpu.SemaphoreType.DMA(())],
    )
    return pl.pallas_call(
        functools.partial(assign_kernel, scale=scale),
        out_shape=jax.ShapeDtypeStruct((feat + 8, chunk), jnp.float32),
        grid_spec=grid_spec,
        compiler_params=pltpu.CompilerParams(vmem_limit_bytes=24 * 1024 * 1024),
        cost_estimate=pl.CostEstimate(
            flops=2 * chunk * cols * (width + feat) + 5 * chunk * cols,
            transcendentals=chunk * cols,
            bytes_accessed=2 * (chunk + cols) * width + 2 * cols * feat + 4 * chunk * (feat + 8),
        ),
    )(index, v, r, parts, base.reshape(1, cols), f)


def combine_kernel(*refs):
    count = len(refs) - 3
    piece_refs, out_ref, held, sem = refs[:count], refs[count], refs[count + 1], refs[count + 2]
    copies = [pltpu.make_async_copy(piece_refs[k], held.at[k], sem.at[k]) for k in range(count)]
    for copy in copies:
        copy.start()
    for copy in copies:
        copy.wait()
    feat = out_ref.shape[1]
    peaks = [held[k, feat + 1 : feat + 2, :] for k in range(count)]
    top = peaks[0]
    for peak in peaks[1:]:
        top = jnp.maximum(top, peak)
    numerator = None
    denominator = None
    for k, peak in enumerate(peaks):
        factor = jnp.exp(peak - top)
        term = held[k, :feat, :] * factor
        mass = held[k, feat : feat + 1, :] * factor
        numerator = term if numerator is None else numerator + term
        denominator = mass if denominator is None else denominator + mass
    out_ref[...] = (numerator / denominator).T


def combine(pieces, feat):
    rows, chunk = pieces[0].shape
    count = len(pieces)
    return pl.pallas_call(
        combine_kernel,
        out_shape=jax.ShapeDtypeStruct((chunk, feat), jnp.float32),
        in_specs=[pl.BlockSpec(memory_space=pl.ANY) for piece in pieces],
        out_specs=pl.BlockSpec((chunk, feat), lambda: (0, 0)),
        scratch_shapes=[
            pltpu.VMEM((count, rows, chunk), jnp.float32),
            pltpu.SemaphoreType.DMA((count,)),
        ],
        cost_estimate=pl.CostEstimate(
            flops=3 * count * chunk * feat,
            transcendentals=count * chunk,
            bytes_accessed=4 * chunk * (rows * count + feat),
        ),
    )(*pieces)


def local(vehicle_emb, request_emb, request_feat, log_supply, log_demand):
    own_rows = lax.all_gather(vehicle_emb, "req", axis=0, tiled=True)
    row_count = own_rows.shape[0]
    scale = 3.0 / math.sqrt(own_rows.shape[1])
    spread = lax.axis_size("veh")

    def exchange(block):
        return lax.all_to_all(block, "veh", 0, 0, tiled=True)

    first = exchange(lse_over_rows(own_rows, request_emb, scale, 4096, spread, 24 << 20))
    partial = row_lse(own_rows, request_emb, scale, 1024, 48 << 20, first, log_demand)
    row_parts = lax.all_gather(partial[0], "req", axis=0, tiled=False)
    second = exchange(
        lse_over_rows(own_rows, request_emb, scale, 4096, spread, 24 << 20, row_parts, log_supply)
    )

    owners = lax.axis_size("req")
    chunk = row_count // owners
    me = lax.axis_index("req")
    feat = request_feat.shape[1]
    if owners & (owners - 1) == 0:
        order = [(step, lambda i, m=step: i ^ m) for step in list(range(2, owners)) + [1]]
    else:
        order = [(step, lambda i, m=step: (i + m) % owners) for step in range(1, owners)]
    pieces = []
    for step, partner in order + [(0, None)]:
        index = jnp.reshape(partner(me) if step else me, (1,)).astype(jnp.int32)
        piece = assign_chunk(
            own_rows, request_emb, second, log_demand, request_feat, scale, chunk, index
        )
        if step:
            piece = lax.ppermute(piece, "req", [(i, partner(i)) for i in range(owners)])
        pieces.append(piece)
    return combine(pieces, feat)


def solution(mesh):
    in_specs = (P(("veh", "req"), None), P("req", None), P("req", None), P("veh"), P("req"))
    out_specs = P(("veh", "req"), None)
    return jax.shard_map(local, mesh=mesh, in_specs=in_specs, out_specs=out_specs, check_vma=False)
```

```python
import functools
import math

import jax
import jax.numpy as jnp
from jax import lax
from jax.experimental import pallas as pl
from jax.experimental.pallas import tpu as pltpu
from jax.sharding import PartitionSpec as P


def merged_lse(parts):
    top = jnp.max(parts, axis=0)
    return top + jnp.log(jnp.sum(jnp.exp(parts - top[None]), axis=0))


def lse_kernel(*refs, scale, shifted, copies):
    if shifted:
        a_ref, parts_ref, base_ref, b_ref, out_ref, column_ref = refs

        @pl.when(pl.program_id(0) == 0)
        def _():
            row = base_ref[...] - merged_lse(parts_ref[...])
            wide = jnp.broadcast_to(row, (128, row.shape[1]))
            column_ref[...] = jnp.transpose(wide)[:, :1]

    else:
        a_ref, b_ref, out_ref = refs
    scores = lax.dot_general(
        a_ref[...], b_ref[...], (((1,), (1,)), ((), ())), preferred_element_type=jnp.float32
    )
    logits = scores * scale
    if shifted:
        logits = logits + column_ref[...]
    top = jnp.max(logits, axis=0, keepdims=True)
    total = jnp.sum(jnp.exp(logits - top), axis=0, keepdims=True)
    result = top + jnp.log(total)
    out_ref[...] = jnp.broadcast_to(result[None], (copies,) + result.shape)


def lse_over_rows(a, b, scale, tile, copies, vmem_limit, parts=None, base=None):
    rows, width = a.shape
    cols = b.shape[0]
    tile = min(tile, cols)
    shifted = parts is not None
    in_specs = [pl.BlockSpec((rows, width), lambda j: (0, 0))]
    operands = [a]
    scratch = []
    if shifted:
        in_specs += [
            pl.BlockSpec(parts.shape, lambda j: (0, 0, 0)),
            pl.BlockSpec((1, rows), lambda j: (0, 0)),
        ]
        operands += [parts, base.reshape(1, rows)]
        scratch = [pltpu.VMEM((rows, 1), jnp.float32)]
    in_specs.append(pl.BlockSpec((tile, width), lambda j: (j, 0)))
    operands.append(b)
    return pl.pallas_call(
        functools.partial(lse_kernel, scale=scale, shifted=shifted, copies=copies),
        out_shape=jax.ShapeDtypeStruct((copies, 1, cols), jnp.float32),
        grid=(cols // tile,),
        in_specs=in_specs,
        out_specs=pl.BlockSpec((copies, 1, tile), lambda j: (0, 0, j)),
        scratch_shapes=scratch,
        compiler_params=pltpu.CompilerParams(vmem_limit_bytes=vmem_limit),
        cost_estimate=pl.CostEstimate(
            flops=2 * rows * cols * width + 5 * rows * cols,
            transcendentals=rows * cols,
            bytes_accessed=2 * (rows + cols) * width + 4 * (rows + copies * cols),
        ),
    )(*operands)


def row_kernel(a_ref, parts_ref, base_ref, b_ref, out_ref, *, scale):
    demand = base_ref[...] - merged_lse(parts_ref[...])
    scores = lax.dot_general(
        a_ref[...], b_ref[...], (((1,), (1,)), ((), ())), preferred_element_type=jnp.float32
    )
    logits = scores * scale + demand
    top = jnp.max(logits, axis=1, keepdims=True)
    total = jnp.sum(jnp.exp(logits - top), axis=1, keepdims=True)
    result = top + jnp.log(total)
    wide = jnp.broadcast_to(result, (result.shape[0], 128))
    out_ref[...] = jnp.transpose(wide)[:1, :][None]


def row_lse(a, b, scale, tile, vmem_limit, parts, base):
    rows, width = a.shape
    cols = b.shape[0]
    tile = min(tile, rows)
    return pl.pallas_call(
        functools.partial(row_kernel, scale=scale),
        out_shape=jax.ShapeDtypeStruct((1, 1, rows), jnp.float32),
        grid=(rows // tile,),
        in_specs=[
            pl.BlockSpec((tile, width), lambda i: (i, 0)),
            pl.BlockSpec(parts.shape, lambda i: (0, 0, 0)),
            pl.BlockSpec((1, cols), lambda i: (0, 0)),
            pl.BlockSpec((cols, width), lambda i: (0, 0)),
        ],
        out_specs=pl.BlockSpec((1, 1, tile), lambda i: (0, 0, i)),
        compiler_params=pltpu.CompilerParams(vmem_limit_bytes=vmem_limit),
        cost_estimate=pl.CostEstimate(
            flops=2 * rows * cols * width + 5 * rows * cols,
            transcendentals=rows * cols,
            bytes_accessed=2 * (rows + cols) * width + 4 * (rows + 9 * cols),
        ),
    )(a, parts, base.reshape(1, cols), b)


def assign_kernel(
    rot_ref, v_ref, r_ref, parts_ref, base_ref, f_hbm, out_ref, f_ref, sem, *, scale
):
    fetch = pltpu.make_async_copy(f_hbm, f_ref, sem)
    fetch.start()
    demand = base_ref[...] - merged_lse(parts_ref[...])
    scores = lax.dot_general(
        v_ref[...], r_ref[...], (((1,), (1,)), ((), ())), preferred_element_type=jnp.float32
    )
    logits = scores * scale + demand
    top = jnp.max(logits, axis=1, keepdims=True)
    powers = jnp.exp(logits - top)
    mass = jnp.sum(powers, axis=1, keepdims=True)
    feat = f_ref.shape[1]
    fetch.wait()
    block_feat = jnp.dot(
        powers.astype(jnp.bfloat16), f_ref[...], preferred_element_type=jnp.float32
    )
    out_ref[:feat, :] = block_feat.T
    lane = lax.broadcasted_iota(jnp.int32, (top.shape[0], 128), 1)
    extra = jnp.where(lane == 0, mass, jnp.where(lane == 1, top, 0.0))
    out_ref[feat:, :] = extra.T[:8, :]


def assign_chunk(v, r, parts, base, f, scale, chunk, index):
    rows, width = v.shape
    cols, feat = f.shape
    grid_spec = pltpu.PrefetchScalarGridSpec(
        num_scalar_prefetch=1,
        grid=(1,),
        in_specs=[
            pl.BlockSpec((chunk, width), lambda i, at: (at[0], 0)),
            pl.BlockSpec((cols, width), lambda i, at: (0, 0)),
            pl.BlockSpec(parts.shape, lambda i, at: (0, 0, 0)),
            pl.BlockSpec((1, cols), lambda i, at: (0, 0)),
            pl.BlockSpec(memory_space=pl.ANY),
        ],
        out_specs=pl.BlockSpec((feat + 8, chunk), lambda i, at: (0, 0)),
        scratch_shapes=[pltpu.VMEM((cols, feat), f.dtype), pltpu.SemaphoreType.DMA(())],
    )
    return pl.pallas_call(
        functools.partial(assign_kernel, scale=scale),
        out_shape=jax.ShapeDtypeStruct((feat + 8, chunk), jnp.float32),
        grid_spec=grid_spec,
        compiler_params=pltpu.CompilerParams(vmem_limit_bytes=24 * 1024 * 1024),
        cost_estimate=pl.CostEstimate(
            flops=2 * chunk * cols * (width + feat) + 5 * chunk * cols,
            transcendentals=chunk * cols,
            bytes_accessed=2 * (chunk + cols) * width + 2 * cols * feat + 4 * chunk * (feat + 8),
        ),
    )(index, v, r, parts, base.reshape(1, cols), f)


def combine_kernel(*refs):
    piece_refs, out_ref = refs[:-1], refs[-1]
    feat = out_ref.shape[1]
    peaks = [ref[feat + 1 : feat + 2, :] for ref in piece_refs]
    top = peaks[0]
    for peak in peaks[1:]:
        top = jnp.maximum(top, peak)
    numerator = None
    denominator = None
    for ref, peak in zip(piece_refs, peaks):
        factor = jnp.exp(peak - top)
        term = ref[:feat, :] * factor
        mass = ref[feat : feat + 1, :] * factor
        numerator = term if numerator is None else numerator + term
        denominator = mass if denominator is None else denominator + mass
    out_ref[...] = (numerator / denominator).T


def combine(pieces, feat):
    chunk = pieces[0].shape[1]
    width = min(128, chunk)
    return pl.pallas_call(
        combine_kernel,
        out_shape=jax.ShapeDtypeStruct((chunk, feat), jnp.float32),
        grid=(chunk // width,),
        in_specs=[pl.BlockSpec((feat + 8, width), lambda j: (0, j)) for piece in pieces],
        out_specs=pl.BlockSpec((width, feat), lambda j: (j, 0)),
        cost_estimate=pl.CostEstimate(
            flops=3 * len(pieces) * chunk * feat,
            transcendentals=len(pieces) * chunk,
            bytes_accessed=4 * chunk * ((feat + 8) * len(pieces) + feat),
        ),
    )(*pieces)


def local(vehicle_emb, request_emb, request_feat, log_supply, log_demand):
    own_rows = lax.all_gather(vehicle_emb, "req", axis=0, tiled=True)
    row_count = own_rows.shape[0]
    scale = 3.0 / math.sqrt(own_rows.shape[1])
    spread = lax.axis_size("veh")

    def exchange(block):
        return lax.all_to_all(block, "veh", 0, 0, tiled=True)

    first = exchange(lse_over_rows(own_rows, request_emb, scale, 4096, spread, 24 << 20))
    partial = row_lse(own_rows, request_emb, scale, 1024, 48 << 20, first, log_demand)
    row_parts = lax.all_gather(partial[0], "req", axis=0, tiled=False)
    second = exchange(
        lse_over_rows(own_rows, request_emb, scale, 4096, spread, 24 << 20, row_parts, log_supply)
    )

    owners = lax.axis_size("req")
    chunk = row_count // owners
    me = lax.axis_index("req")
    feat = request_feat.shape[1]
    if owners & (owners - 1) == 0:
        order = [(step, lambda i, m=step: i ^ m) for step in list(range(2, owners)) + [1]]
    else:
        order = [(step, lambda i, m=step: (i + m) % owners) for step in range(1, owners)]
    pieces = []
    for step, partner in order + [(0, None)]:
        index = jnp.reshape(partner(me) if step else me, (1,)).astype(jnp.int32)
        piece = assign_chunk(
            own_rows, request_emb, second, log_demand, request_feat, scale, chunk, index
        )
        if step:
            piece = lax.ppermute(piece, "req", [(i, partner(i)) for i in range(owners)])
        pieces.append(piece)
    arrived = jnp.stack(pieces)
    peaks = arrived[:, feat + 1, :]
    masses = arrived[:, feat, :]
    factor = jnp.exp(peaks - jnp.max(peaks, axis=0, keepdims=True))
    numerator = jnp.sum(arrived[:, :feat, :] * factor[:, None, :], axis=0)
    denominator = jnp.sum(masses * factor, axis=0)
    return (numerator / denominator[None, :]).T


def solution(mesh):
    in_specs = (P(("veh", "req"), None), P("req", None), P("req", None), P("veh"), P("req"))
    out_specs = P(("veh", "req"), None)
    return jax.shard_map(local, mesh=mesh, in_specs=in_specs, out_specs=out_specs, check_vma=False)
```

```python
import functools
import math

import jax
import jax.numpy as jnp
from jax import lax
from jax.experimental import pallas as pl
from jax.experimental.pallas import tpu as pltpu
from jax.sharding import PartitionSpec as P


def merged_lse(parts):
    top = jnp.max(parts, axis=0)
    return top + jnp.log(jnp.sum(jnp.exp(parts - top[None]), axis=0))


def lse_kernel(*refs, scale, shifted, copies):
    if shifted:
        a_ref, parts_ref, base_ref, b_ref, out_ref, column_ref = refs

        @pl.when(pl.program_id(0) == 0)
        def _():
            row = base_ref[...] - merged_lse(parts_ref[...])
            wide = jnp.broadcast_to(row, (128, row.shape[1]))
            column_ref[...] = jnp.transpose(wide)[:, :1]

    else:
        a_ref, b_ref, out_ref = refs
    scores = lax.dot_general(
        a_ref[...], b_ref[...], (((1,), (1,)), ((), ())), preferred_element_type=jnp.float32
    )
    logits = scores * scale
    if shifted:
        logits = logits + column_ref[...]
    top = jnp.max(logits, axis=0, keepdims=True)
    total = jnp.sum(jnp.exp(logits - top), axis=0, keepdims=True)
    result = top + jnp.log(total)
    out_ref[...] = jnp.broadcast_to(result[None], (copies,) + result.shape)


def lse_over_rows(a, b, scale, tile, copies, vmem_limit, parts=None, base=None):
    rows, width = a.shape
    cols = b.shape[0]
    tile = min(tile, cols)
    shifted = parts is not None
    in_specs = [pl.BlockSpec((rows, width), lambda j: (0, 0))]
    operands = [a]
    scratch = []
    if shifted:
        in_specs += [
            pl.BlockSpec(parts.shape, lambda j: (0, 0, 0)),
            pl.BlockSpec((1, rows), lambda j: (0, 0)),
        ]
        operands += [parts, base.reshape(1, rows)]
        scratch = [pltpu.VMEM((rows, 1), jnp.float32)]
    in_specs.append(pl.BlockSpec((tile, width), lambda j: (j, 0)))
    operands.append(b)
    return pl.pallas_call(
        functools.partial(lse_kernel, scale=scale, shifted=shifted, copies=copies),
        out_shape=jax.ShapeDtypeStruct((copies, 1, cols), jnp.float32),
        grid=(cols // tile,),
        in_specs=in_specs,
        out_specs=pl.BlockSpec((copies, 1, tile), lambda j: (0, 0, j)),
        scratch_shapes=scratch,
        compiler_params=pltpu.CompilerParams(vmem_limit_bytes=vmem_limit),
        cost_estimate=pl.CostEstimate(
            flops=2 * rows * cols * width + 5 * rows * cols,
            transcendentals=rows * cols,
            bytes_accessed=2 * (rows + cols) * width + 4 * (rows + copies * cols),
        ),
    )(*operands)


def row_kernel(a_ref, parts_ref, base_ref, b_ref, out_ref, *, scale):
    demand = base_ref[...] - merged_lse(parts_ref[...])
    scores = lax.dot_general(
        a_ref[...], b_ref[...], (((1,), (1,)), ((), ())), preferred_element_type=jnp.float32
    )
    logits = scores * scale + demand
    top = jnp.max(logits, axis=1, keepdims=True)
    total = jnp.sum(jnp.exp(logits - top), axis=1, keepdims=True)
    result = top + jnp.log(total)
    wide = jnp.broadcast_to(result, (result.shape[0], 128))
    out_ref[...] = jnp.transpose(wide)[:1, :][None]


def row_lse(a, b, scale, tile, vmem_limit, parts, base):
    rows, width = a.shape
    cols = b.shape[0]
    tile = min(tile, rows)
    return pl.pallas_call(
        functools.partial(row_kernel, scale=scale),
        out_shape=jax.ShapeDtypeStruct((1, 1, rows), jnp.float32),
        grid=(rows // tile,),
        in_specs=[
            pl.BlockSpec((tile, width), lambda i: (i, 0)),
            pl.BlockSpec(parts.shape, lambda i: (0, 0, 0)),
            pl.BlockSpec((1, cols), lambda i: (0, 0)),
            pl.BlockSpec((cols, width), lambda i: (0, 0)),
        ],
        out_specs=pl.BlockSpec((1, 1, tile), lambda i: (0, 0, i)),
        compiler_params=pltpu.CompilerParams(vmem_limit_bytes=vmem_limit),
        cost_estimate=pl.CostEstimate(
            flops=2 * rows * cols * width + 5 * rows * cols,
            transcendentals=rows * cols,
            bytes_accessed=2 * (rows + cols) * width + 4 * (rows + 9 * cols),
        ),
    )(a, parts, base.reshape(1, cols), b)


def assign_kernel(
    rot_ref, v_ref, r_ref, parts_ref, base_ref, f_hbm, out_ref, f_ref, sem, *, scale
):
    fetch = pltpu.make_async_copy(f_hbm, f_ref, sem)
    fetch.start()
    demand = base_ref[...] - merged_lse(parts_ref[...])
    scores = lax.dot_general(
        v_ref[...], r_ref[...], (((1,), (1,)), ((), ())), preferred_element_type=jnp.float32
    )
    logits = scores * scale + demand
    top = jnp.max(logits, axis=1, keepdims=True)
    powers = jnp.exp(logits - top)
    mass = jnp.sum(powers, axis=1, keepdims=True)
    feat = f_ref.shape[1]
    fetch.wait()
    block_feat = jnp.dot(
        powers.astype(jnp.bfloat16), f_ref[...], preferred_element_type=jnp.float32
    )
    out_ref[:, :feat] = block_feat
    lane = lax.broadcasted_iota(jnp.int32, (top.shape[0], 128), 1)
    out_ref[:, feat:] = jnp.where(lane == 0, mass, jnp.where(lane == 1, top, 0.0))


def assign_chunk(v, r, parts, base, f, scale, chunk, index):
    rows, width = v.shape
    cols, feat = f.shape
    grid_spec = pltpu.PrefetchScalarGridSpec(
        num_scalar_prefetch=1,
        grid=(1,),
        in_specs=[
            pl.BlockSpec((chunk, width), lambda i, at: (at[0], 0)),
            pl.BlockSpec((cols, width), lambda i, at: (0, 0)),
            pl.BlockSpec(parts.shape, lambda i, at: (0, 0, 0)),
            pl.BlockSpec((1, cols), lambda i, at: (0, 0)),
            pl.BlockSpec(memory_space=pl.ANY),
        ],
        out_specs=pl.BlockSpec((chunk, feat + 128), lambda i, at: (0, 0)),
        scratch_shapes=[pltpu.VMEM((cols, feat), f.dtype), pltpu.SemaphoreType.DMA(())],
    )
    return pl.pallas_call(
        functools.partial(assign_kernel, scale=scale),
        out_shape=jax.ShapeDtypeStruct((chunk, feat + 128), jnp.float32),
        grid_spec=grid_spec,
        compiler_params=pltpu.CompilerParams(vmem_limit_bytes=24 * 1024 * 1024),
        cost_estimate=pl.CostEstimate(
            flops=2 * chunk * cols * (width + feat) + 5 * chunk * cols,
            transcendentals=chunk * cols,
            bytes_accessed=2 * (chunk + cols) * width + 2 * cols * feat + 4 * chunk * (feat + 128),
        ),
    )(index, v, r, parts, base.reshape(1, cols), f)


def combine_kernel(*refs):
    piece_refs, out_ref = refs[:-1], refs[-1]
    feat = out_ref.shape[1]
    peaks = [ref[feat + 1 : feat + 2, :] for ref in piece_refs]
    top = peaks[0]
    for peak in peaks[1:]:
        top = jnp.maximum(top, peak)
    numerator = None
    denominator = None
    for ref, peak in zip(piece_refs, peaks):
        factor = jnp.exp(peak - top)
        term = ref[:feat, :] * factor
        mass = ref[feat : feat + 1, :] * factor
        numerator = term if numerator is None else numerator + term
        denominator = mass if denominator is None else denominator + mass
    out_ref[...] = (numerator / denominator).T


def combine(pieces, feat):
    chunk = pieces[0].shape[1]
    width = min(128, chunk)
    return pl.pallas_call(
        combine_kernel,
        out_shape=jax.ShapeDtypeStruct((chunk, feat), jnp.float32),
        grid=(chunk // width,),
        in_specs=[pl.BlockSpec((feat + 8, width), lambda j: (0, j)) for piece in pieces],
        out_specs=pl.BlockSpec((width, feat), lambda j: (j, 0)),
        cost_estimate=pl.CostEstimate(
            flops=3 * len(pieces) * chunk * feat,
            transcendentals=len(pieces) * chunk,
            bytes_accessed=4 * chunk * ((feat + 8) * len(pieces) + feat),
        ),
    )(*pieces)


def local(vehicle_emb, request_emb, request_feat, log_supply, log_demand):
    own_rows = lax.all_gather(vehicle_emb, "req", axis=0, tiled=True)
    row_count = own_rows.shape[0]
    scale = 3.0 / math.sqrt(own_rows.shape[1])
    spread = lax.axis_size("veh")

    def exchange(block):
        return lax.all_to_all(block, "veh", 0, 0, tiled=True)

    first = exchange(lse_over_rows(own_rows, request_emb, scale, 4096, spread, 24 << 20))
    partial = row_lse(own_rows, request_emb, scale, 1024, 48 << 20, first, log_demand)
    row_parts = lax.all_gather(partial[0], "req", axis=0, tiled=False)
    second = exchange(
        lse_over_rows(own_rows, request_emb, scale, 4096, spread, 24 << 20, row_parts, log_supply)
    )

    owners = lax.axis_size("req")
    chunk = row_count // owners
    me = lax.axis_index("req")
    feat = request_feat.shape[1]
    if owners & (owners - 1) == 0:
        order = [(step, lambda i, m=step: i ^ m) for step in list(range(2, owners)) + [1]]
    else:
        order = [(step, lambda i, m=step: (i + m) % owners) for step in range(1, owners)]
    pieces = []
    for step, partner in order + [(0, None)]:
        index = jnp.reshape(partner(me) if step else me, (1,)).astype(jnp.int32)
        piece = assign_chunk(
            own_rows, request_emb, second, log_demand, request_feat, scale, chunk, index
        )
        if step:
            piece = lax.ppermute(piece, "req", [(i, partner(i)) for i in range(owners)])
        pieces.append(piece)
    arrived = jnp.stack(pieces)
    peaks = arrived[:, :, feat + 1]
    masses = arrived[:, :, feat]
    factor = jnp.exp(peaks - jnp.max(peaks, axis=0, keepdims=True))
    numerator = jnp.sum(arrived[:, :, :feat] * factor[:, :, None], axis=0)
    denominator = jnp.sum(masses * factor, axis=0)
    return numerator / denominator[:, None]


def solution(mesh):
    in_specs = (P(("veh", "req"), None), P("req", None), P("req", None), P("veh"), P("req"))
    out_specs = P(("veh", "req"), None)
    return jax.shard_map(local, mesh=mesh, in_specs=in_specs, out_specs=out_specs, check_vma=False)
```

```python
import functools
import math

import jax
import jax.numpy as jnp
from jax import lax
from jax.experimental import pallas as pl
from jax.experimental.pallas import tpu as pltpu
from jax.sharding import PartitionSpec as P


def merged_lse(parts):
    top = jnp.max(parts, axis=0)
    return top + jnp.log(jnp.sum(jnp.exp(parts - top[None]), axis=0))


def lse_kernel(*refs, scale, shifted, copies):
    if shifted:
        a_ref, parts_ref, base_ref, b_ref, out_ref, column_ref = refs

        @pl.when(pl.program_id(0) == 0)
        def _():
            row = base_ref[...] - merged_lse(parts_ref[...])
            wide = jnp.broadcast_to(row, (128, row.shape[1]))
            column_ref[...] = jnp.transpose(wide)[:, :1]

    else:
        a_ref, b_ref, out_ref = refs
    scores = lax.dot_general(
        a_ref[...], b_ref[...], (((1,), (1,)), ((), ())), preferred_element_type=jnp.float32
    )
    logits = scores * scale
    if shifted:
        logits = logits + column_ref[...]
    top = jnp.max(logits, axis=0, keepdims=True)
    total = jnp.sum(jnp.exp(logits - top), axis=0, keepdims=True)
    result = top + jnp.log(total)
    out_ref[...] = jnp.broadcast_to(result[None], (copies,) + result.shape)


def lse_over_rows(a, b, scale, tile, copies, vmem_limit, parts=None, base=None):
    rows, width = a.shape
    cols = b.shape[0]
    tile = min(tile, cols)
    shifted = parts is not None
    in_specs = [pl.BlockSpec((rows, width), lambda j: (0, 0))]
    operands = [a]
    scratch = []
    if shifted:
        in_specs += [
            pl.BlockSpec(parts.shape, lambda j: (0, 0, 0)),
            pl.BlockSpec((1, rows), lambda j: (0, 0)),
        ]
        operands += [parts, base.reshape(1, rows)]
        scratch = [pltpu.VMEM((rows, 1), jnp.float32)]
    in_specs.append(pl.BlockSpec((tile, width), lambda j: (j, 0)))
    operands.append(b)
    return pl.pallas_call(
        functools.partial(lse_kernel, scale=scale, shifted=shifted, copies=copies),
        out_shape=jax.ShapeDtypeStruct((copies, 1, cols), jnp.float32),
        grid=(cols // tile,),
        in_specs=in_specs,
        out_specs=pl.BlockSpec((copies, 1, tile), lambda j: (0, 0, j)),
        scratch_shapes=scratch,
        compiler_params=pltpu.CompilerParams(vmem_limit_bytes=vmem_limit),
        cost_estimate=pl.CostEstimate(
            flops=2 * rows * cols * width + 5 * rows * cols,
            transcendentals=rows * cols,
            bytes_accessed=2 * (rows + cols) * width + 4 * (rows + copies * cols),
        ),
    )(*operands)


def row_kernel(a_ref, parts_ref, base_ref, b_ref, out_ref, *, scale):
    demand = base_ref[...] - merged_lse(parts_ref[...])
    scores = lax.dot_general(
        a_ref[...], b_ref[...], (((1,), (1,)), ((), ())), preferred_element_type=jnp.float32
    )
    logits = scores * scale + demand
    top = jnp.max(logits, axis=1, keepdims=True)
    total = jnp.sum(jnp.exp(logits - top), axis=1, keepdims=True)
    result = top + jnp.log(total)
    wide = jnp.broadcast_to(result, (result.shape[0], 128))
    out_ref[...] = jnp.transpose(wide)[:1, :][None]


def row_lse(a, b, scale, tile, vmem_limit, parts, base):
    rows, width = a.shape
    cols = b.shape[0]
    tile = min(tile, rows)
    return pl.pallas_call(
        functools.partial(row_kernel, scale=scale),
        out_shape=jax.ShapeDtypeStruct((1, 1, rows), jnp.float32),
        grid=(rows // tile,),
        in_specs=[
            pl.BlockSpec((tile, width), lambda i: (i, 0)),
            pl.BlockSpec(parts.shape, lambda i: (0, 0, 0)),
            pl.BlockSpec((1, cols), lambda i: (0, 0)),
            pl.BlockSpec((cols, width), lambda i: (0, 0)),
        ],
        out_specs=pl.BlockSpec((1, 1, tile), lambda i: (0, 0, i)),
        compiler_params=pltpu.CompilerParams(vmem_limit_bytes=vmem_limit),
        cost_estimate=pl.CostEstimate(
            flops=2 * rows * cols * width + 5 * rows * cols,
            transcendentals=rows * cols,
            bytes_accessed=2 * (rows + cols) * width + 4 * (rows + 9 * cols),
        ),
    )(a, parts, base.reshape(1, cols), b)


def assign_kernel(
    rot_ref, v_ref, r_ref, parts_ref, base_ref, f_hbm, out_ref, f_ref, sem, *, scale
):
    fetch = pltpu.make_async_copy(f_hbm, f_ref, sem)
    fetch.start()
    demand = base_ref[...] - merged_lse(parts_ref[...])
    scores = lax.dot_general(
        v_ref[...], r_ref[...], (((1,), (1,)), ((), ())), preferred_element_type=jnp.float32
    )
    logits = scores * scale + demand
    top = jnp.max(logits, axis=1, keepdims=True)
    powers = jnp.exp(logits - top)
    mass = jnp.sum(powers, axis=1, keepdims=True)
    feat = f_ref.shape[1]
    fetch.wait()
    block_feat = jnp.dot(
        powers.astype(jnp.bfloat16), f_ref[...], preferred_element_type=jnp.float32
    )
    out_ref[:feat, :] = block_feat.T
    lane = lax.broadcasted_iota(jnp.int32, (top.shape[0], 128), 1)
    extra = jnp.where(lane == 0, mass, jnp.where(lane == 1, top, 0.0))
    out_ref[feat:, :] = extra.T[:8, :]


def assign_chunk(v, r, parts, base, f, scale, chunk, index):
    rows, width = v.shape
    cols, feat = f.shape
    grid_spec = pltpu.PrefetchScalarGridSpec(
        num_scalar_prefetch=1,
        grid=(1,),
        in_specs=[
            pl.BlockSpec((chunk, width), lambda i, at: (at[0], 0)),
            pl.BlockSpec((cols, width), lambda i, at: (0, 0)),
            pl.BlockSpec(parts.shape, lambda i, at: (0, 0, 0)),
            pl.BlockSpec((1, cols), lambda i, at: (0, 0)),
            pl.BlockSpec(memory_space=pl.ANY),
        ],
        out_specs=pl.BlockSpec((feat + 8, chunk), lambda i, at: (0, 0)),
        scratch_shapes=[pltpu.VMEM((cols, feat), f.dtype), pltpu.SemaphoreType.DMA(())],
    )
    return pl.pallas_call(
        functools.partial(assign_kernel, scale=scale),
        out_shape=jax.ShapeDtypeStruct((feat + 8, chunk), jnp.float32),
        grid_spec=grid_spec,
        compiler_params=pltpu.CompilerParams(vmem_limit_bytes=16 * 1024 * 1024),
        cost_estimate=pl.CostEstimate(
            flops=2 * chunk * cols * (width + feat) + 5 * chunk * cols,
            transcendentals=chunk * cols,
            bytes_accessed=2 * (chunk + cols) * width + 2 * cols * feat + 4 * chunk * (feat + 8),
        ),
    )(index, v, r, parts, base.reshape(1, cols), f)


def combine_kernel(*refs):
    piece_refs, out_ref = refs[:-1], refs[-1]
    feat = out_ref.shape[1]
    peaks = [ref[feat + 1 : feat + 2, :] for ref in piece_refs]
    top = peaks[0]
    for peak in peaks[1:]:
        top = jnp.maximum(top, peak)
    numerator = None
    denominator = None
    for ref, peak in zip(piece_refs, peaks):
        factor = jnp.exp(peak - top)
        term = ref[:feat, :] * factor
        mass = ref[feat : feat + 1, :] * factor
        numerator = term if numerator is None else numerator + term
        denominator = mass if denominator is None else denominator + mass
    out_ref[...] = (numerator / denominator).T


def combine(pieces, feat):
    chunk = pieces[0].shape[1]
    width = min(128, chunk)
    return pl.pallas_call(
        combine_kernel,
        out_shape=jax.ShapeDtypeStruct((chunk, feat), jnp.float32),
        grid=(chunk // width,),
        in_specs=[pl.BlockSpec((feat + 8, width), lambda j: (0, j)) for piece in pieces],
        out_specs=pl.BlockSpec((width, feat), lambda j: (j, 0)),
        cost_estimate=pl.CostEstimate(
            flops=3 * len(pieces) * chunk * feat,
            transcendentals=len(pieces) * chunk,
            bytes_accessed=4 * chunk * ((feat + 8) * len(pieces) + feat),
        ),
    )(*pieces)


def local(vehicle_emb, request_emb, request_feat, log_supply, log_demand):
    own_rows = lax.all_gather(vehicle_emb, "req", axis=0, tiled=True)
    row_count = own_rows.shape[0]
    scale = 3.0 / math.sqrt(own_rows.shape[1])
    spread = lax.axis_size("veh")

    def exchange(block):
        return lax.all_to_all(block, "veh", 0, 0, tiled=True)

    first = exchange(lse_over_rows(own_rows, request_emb, scale, 4096, spread, 24 << 20))
    partial = row_lse(own_rows, request_emb, scale, 1024, 24 << 20, first, log_demand)
    row_parts = lax.all_gather(partial[0], "req", axis=0, tiled=False)
    second = exchange(
        lse_over_rows(own_rows, request_emb, scale, 4096, spread, 24 << 20, row_parts, log_supply)
    )

    owners = lax.axis_size("req")
    chunk = row_count // owners
    me = lax.axis_index("req")
    feat = request_feat.shape[1]
    if owners & (owners - 1) == 0:
        order = [(step, lambda i, m=step: i ^ m) for step in list(range(2, owners)) + [1]]
    else:
        order = [(step, lambda i, m=step: (i + m) % owners) for step in range(1, owners)]
    pieces = []
    for step, partner in order + [(0, None)]:
        index = jnp.reshape(partner(me) if step else me, (1,)).astype(jnp.int32)
        piece = assign_chunk(
            own_rows, request_emb, second, log_demand, request_feat, scale, chunk, index
        )
        if step:
            piece = lax.ppermute(piece, "req", [(i, partner(i)) for i in range(owners)])
        pieces.append(piece)
    arrived = jnp.stack(pieces)
    peaks = arrived[:, feat + 1, :]
    masses = arrived[:, feat, :]
    factor = jnp.exp(peaks - jnp.max(peaks, axis=0, keepdims=True))
    numerator = jnp.sum(arrived[:, :feat, :] * factor[:, None, :], axis=0)
    denominator = jnp.sum(masses * factor, axis=0)
    return (numerator / denominator[None, :]).T


def solution(mesh):
    in_specs = (P(("veh", "req"), None), P("req", None), P("req", None), P("veh"), P("req"))
    out_specs = P(("veh", "req"), None)
    return jax.shard_map(local, mesh=mesh, in_specs=in_specs, out_specs=out_specs, check_vma=False)
```

```python
import functools
import math

import jax
import jax.numpy as jnp
from jax import lax
from jax.experimental import pallas as pl
from jax.experimental.pallas import tpu as pltpu
from jax.sharding import PartitionSpec as P


def merged_lse(parts):
    top = jnp.max(parts, axis=0)
    return top + jnp.log(jnp.sum(jnp.exp(parts - top[None]), axis=0))


def lse_kernel(*refs, scale, shifted, copies):
    if shifted:
        a_ref, parts_ref, base_ref, b_ref, out_ref, column_ref = refs

        @pl.when(pl.program_id(0) == 0)
        def _():
            row = base_ref[...] - merged_lse(parts_ref[...])
            wide = jnp.broadcast_to(row, (128, row.shape[1]))
            column_ref[...] = jnp.transpose(wide)[:, :1]

    else:
        a_ref, b_ref, out_ref = refs
    scores = lax.dot_general(
        a_ref[...], b_ref[...], (((1,), (1,)), ((), ())), preferred_element_type=jnp.float32
    )
    logits = scores * scale
    if shifted:
        logits = logits + column_ref[...]
    top = jnp.max(logits, axis=0, keepdims=True)
    total = jnp.sum(jnp.exp(logits - top), axis=0, keepdims=True)
    result = top + jnp.log(total)
    out_ref[...] = jnp.broadcast_to(result[None], (copies,) + result.shape)


def lse_over_rows(a, b, scale, tile, copies, vmem_limit, parts=None, base=None):
    rows, width = a.shape
    cols = b.shape[0]
    tile = min(tile, cols)
    shifted = parts is not None
    in_specs = [pl.BlockSpec((rows, width), lambda j: (0, 0))]
    operands = [a]
    scratch = []
    if shifted:
        in_specs += [
            pl.BlockSpec(parts.shape, lambda j: (0, 0, 0)),
            pl.BlockSpec((1, rows), lambda j: (0, 0)),
        ]
        operands += [parts, base.reshape(1, rows)]
        scratch = [pltpu.VMEM((rows, 1), jnp.float32)]
    in_specs.append(pl.BlockSpec((tile, width), lambda j: (j, 0)))
    operands.append(b)
    return pl.pallas_call(
        functools.partial(lse_kernel, scale=scale, shifted=shifted, copies=copies),
        out_shape=jax.ShapeDtypeStruct((copies, 1, cols), jnp.float32),
        grid=(cols // tile,),
        in_specs=in_specs,
        out_specs=pl.BlockSpec((copies, 1, tile), lambda j: (0, 0, j)),
        scratch_shapes=scratch,
        compiler_params=pltpu.CompilerParams(vmem_limit_bytes=vmem_limit),
        cost_estimate=pl.CostEstimate(
            flops=2 * rows * cols * width + 5 * rows * cols,
            transcendentals=rows * cols,
            bytes_accessed=2 * (rows + cols) * width + 4 * (rows + copies * cols),
        ),
    )(*operands)


def row_kernel(a_ref, parts_ref, base_ref, b_ref, out_ref, *, scale):
    demand = base_ref[...] - merged_lse(parts_ref[...])
    scores = lax.dot_general(
        a_ref[...], b_ref[...], (((1,), (1,)), ((), ())), preferred_element_type=jnp.float32
    )
    logits = scores * scale + demand
    top = jnp.max(logits, axis=1, keepdims=True)
    total = jnp.sum(jnp.exp(logits - top), axis=1, keepdims=True)
    result = top + jnp.log(total)
    wide = jnp.broadcast_to(result, (result.shape[0], 128))
    out_ref[...] = jnp.transpose(wide)[:1, :][None]


def row_lse(a, b, scale, tile, vmem_limit, parts, base):
    rows, width = a.shape
    cols = b.shape[0]
    tile = min(tile, rows)
    return pl.pallas_call(
        functools.partial(row_kernel, scale=scale),
        out_shape=jax.ShapeDtypeStruct((1, 1, rows), jnp.float32),
        grid=(rows // tile,),
        in_specs=[
            pl.BlockSpec((tile, width), lambda i: (i, 0)),
            pl.BlockSpec(parts.shape, lambda i: (0, 0, 0)),
            pl.BlockSpec((1, cols), lambda i: (0, 0)),
            pl.BlockSpec((cols, width), lambda i: (0, 0)),
        ],
        out_specs=pl.BlockSpec((1, 1, tile), lambda i: (0, 0, i)),
        compiler_params=pltpu.CompilerParams(vmem_limit_bytes=vmem_limit),
        cost_estimate=pl.CostEstimate(
            flops=2 * rows * cols * width + 5 * rows * cols,
            transcendentals=rows * cols,
            bytes_accessed=2 * (rows + cols) * width + 4 * (rows + 9 * cols),
        ),
    )(a, parts, base.reshape(1, cols), b)


def assign_kernel(
    rot_ref, v_ref, r_ref, parts_ref, base_ref, f_hbm, out_ref, f_ref, sem, *, scale
):
    fetch = pltpu.make_async_copy(f_hbm, f_ref, sem)
    fetch.start()
    demand = base_ref[...] - merged_lse(parts_ref[...])
    scores = lax.dot_general(
        v_ref[...], r_ref[...], (((1,), (1,)), ((), ())), preferred_element_type=jnp.float32
    )
    logits = scores * scale + demand
    top = jnp.max(logits, axis=1, keepdims=True)
    powers = jnp.exp(logits - top)
    mass = jnp.sum(powers, axis=1, keepdims=True)
    feat = f_ref.shape[1]
    fetch.wait()
    block_feat = jnp.dot(
        powers.astype(jnp.bfloat16), f_ref[...], preferred_element_type=jnp.float32
    )
    out_ref[:feat, :] = block_feat.T
    lane = lax.broadcasted_iota(jnp.int32, (top.shape[0], 128), 1)
    extra = jnp.where(lane == 0, mass, jnp.where(lane == 1, top, 0.0))
    out_ref[feat:, :] = extra.T[:8, :]


def assign_chunk(v, r, parts, base, f, scale, chunk, index):
    rows, width = v.shape
    cols, feat = f.shape
    grid_spec = pltpu.PrefetchScalarGridSpec(
        num_scalar_prefetch=1,
        grid=(1,),
        in_specs=[
            pl.BlockSpec((chunk, width), lambda i, at: (at[0], 0)),
            pl.BlockSpec((cols, width), lambda i, at: (0, 0)),
            pl.BlockSpec(parts.shape, lambda i, at: (0, 0, 0)),
            pl.BlockSpec((1, cols), lambda i, at: (0, 0)),
            pl.BlockSpec(memory_space=pl.ANY),
        ],
        out_specs=pl.BlockSpec((feat + 8, chunk), lambda i, at: (0, 0)),
        scratch_shapes=[pltpu.VMEM((cols, feat), f.dtype), pltpu.SemaphoreType.DMA(())],
    )
    return pl.pallas_call(
        functools.partial(assign_kernel, scale=scale),
        out_shape=jax.ShapeDtypeStruct((feat + 8, chunk), jnp.float32),
        grid_spec=grid_spec,
        compiler_params=pltpu.CompilerParams(vmem_limit_bytes=24 * 1024 * 1024),
        cost_estimate=pl.CostEstimate(
            flops=2 * chunk * cols * (width + feat) + 5 * chunk * cols,
            transcendentals=chunk * cols,
            bytes_accessed=2 * (chunk + cols) * width + 2 * cols * feat + 4 * chunk * (feat + 8),
        ),
    )(index, v, r, parts, base.reshape(1, cols), f)


def combine_kernel(*refs):
    piece_refs, out_ref = refs[:-1], refs[-1]
    feat = out_ref.shape[1]
    peaks = [ref[feat + 1 : feat + 2, :] for ref in piece_refs]
    top = peaks[0]
    for peak in peaks[1:]:
        top = jnp.maximum(top, peak)
    numerator = None
    denominator = None
    for ref, peak in zip(piece_refs, peaks):
        factor = jnp.exp(peak - top)
        term = ref[:feat, :] * factor
        mass = ref[feat : feat + 1, :] * factor
        numerator = term if numerator is None else numerator + term
        denominator = mass if denominator is None else denominator + mass
    out_ref[...] = (numerator / denominator).T


def combine(pieces, feat):
    chunk = pieces[0].shape[1]
    width = min(128, chunk)
    return pl.pallas_call(
        combine_kernel,
        out_shape=jax.ShapeDtypeStruct((chunk, feat), jnp.float32),
        grid=(chunk // width,),
        in_specs=[pl.BlockSpec((feat + 8, width), lambda j: (0, j)) for piece in pieces],
        out_specs=pl.BlockSpec((width, feat), lambda j: (j, 0)),
        cost_estimate=pl.CostEstimate(
            flops=3 * len(pieces) * chunk * feat,
            transcendentals=len(pieces) * chunk,
            bytes_accessed=4 * chunk * ((feat + 8) * len(pieces) + feat),
        ),
    )(*pieces)


def local(vehicle_emb, request_emb, request_feat, log_supply, log_demand):
    own_rows = lax.all_gather(vehicle_emb, "req", axis=0, tiled=True)
    row_count = own_rows.shape[0]
    scale = 3.0 / math.sqrt(own_rows.shape[1])
    spread = lax.axis_size("veh")

    def exchange(block):
        return lax.all_to_all(block, "veh", 0, 0, tiled=True)

    first = exchange(lse_over_rows(own_rows, request_emb, scale, 4096, spread, 24 << 20))
    partial = row_lse(own_rows, request_emb, scale, 1024, 48 << 20, first, log_demand)
    row_parts = lax.all_gather(partial[0], "req", axis=0, tiled=False)
    second = exchange(
        lse_over_rows(own_rows, request_emb, scale, 4096, spread, 24 << 20, row_parts, log_supply)
    )

    owners = lax.axis_size("req")
    chunk = row_count // owners
    me = lax.axis_index("req")
    feat = request_feat.shape[1]
    if owners & (owners - 1) == 0:
        order = [(step, lambda i, m=step: i ^ m) for step in list(range(owners - 1, 1, -1)) + [1]]
    else:
        order = [(step, lambda i, m=step: (i + m) % owners) for step in range(1, owners)]
    pieces = []
    for step, partner in order + [(0, None)]:
        index = jnp.reshape(partner(me) if step else me, (1,)).astype(jnp.int32)
        piece = assign_chunk(
            own_rows, request_emb, second, log_demand, request_feat, scale, chunk, index
        )
        if step:
            piece = lax.ppermute(piece, "req", [(i, partner(i)) for i in range(owners)])
        pieces.append(piece)
    arrived = jnp.stack(pieces)
    peaks = arrived[:, feat + 1, :]
    masses = arrived[:, feat, :]
    factor = jnp.exp(peaks - jnp.max(peaks, axis=0, keepdims=True))
    numerator = jnp.sum(arrived[:, :feat, :] * factor[:, None, :], axis=0)
    denominator = jnp.sum(masses * factor, axis=0)
    return (numerator / denominator[None, :]).T


def solution(mesh):
    in_specs = (P(("veh", "req"), None), P("req", None), P("req", None), P("veh"), P("req"))
    out_specs = P(("veh", "req"), None)
    return jax.shard_map(local, mesh=mesh, in_specs=in_specs, out_specs=out_specs, check_vma=False)
```

```python
import functools
import math

import jax
import jax.numpy as jnp
from jax import lax
from jax.experimental import pallas as pl
from jax.experimental.pallas import tpu as pltpu
from jax.sharding import PartitionSpec as P


def merged_lse(parts):
    top = jnp.max(parts, axis=0)
    return top + jnp.log(jnp.sum(jnp.exp(parts - top[None]), axis=0))


def lse_kernel(*refs, scale, shifted, copies):
    if shifted:
        a_ref, parts_ref, base_ref, b_ref, out_ref, column_ref = refs

        @pl.when(pl.program_id(0) == 0)
        def _():
            row = base_ref[...] - merged_lse(parts_ref[...])
            wide = jnp.broadcast_to(row, (128, row.shape[1]))
            column_ref[...] = jnp.transpose(wide)[:, :1]

    else:
        a_ref, b_ref, out_ref = refs
    scores = lax.dot_general(
        a_ref[...], b_ref[...], (((1,), (1,)), ((), ())), preferred_element_type=jnp.float32
    )
    logits = scores * scale
    if shifted:
        logits = logits + column_ref[...]
    top = jnp.max(logits, axis=0, keepdims=True)
    total = jnp.sum(jnp.exp(logits - top), axis=0, keepdims=True)
    result = top + jnp.log(total)
    out_ref[...] = jnp.broadcast_to(result[None], (copies,) + result.shape)


def lse_over_rows(a, b, scale, tile, copies, vmem_limit, parts=None, base=None):
    rows, width = a.shape
    cols = b.shape[0]
    tile = min(tile, cols)
    shifted = parts is not None
    in_specs = [pl.BlockSpec((rows, width), lambda j: (0, 0))]
    operands = [a]
    scratch = []
    if shifted:
        in_specs += [
            pl.BlockSpec(parts.shape, lambda j: (0, 0, 0)),
            pl.BlockSpec((1, rows), lambda j: (0, 0)),
        ]
        operands += [parts, base.reshape(1, rows)]
        scratch = [pltpu.VMEM((rows, 1), jnp.float32)]
    in_specs.append(pl.BlockSpec((tile, width), lambda j: (j, 0)))
    operands.append(b)
    return pl.pallas_call(
        functools.partial(lse_kernel, scale=scale, shifted=shifted, copies=copies),
        out_shape=jax.ShapeDtypeStruct((copies, 1, cols), jnp.float32),
        grid=(cols // tile,),
        in_specs=in_specs,
        out_specs=pl.BlockSpec((copies, 1, tile), lambda j: (0, 0, j)),
        scratch_shapes=scratch,
        compiler_params=pltpu.CompilerParams(vmem_limit_bytes=vmem_limit),
        cost_estimate=pl.CostEstimate(
            flops=2 * rows * cols * width + 5 * rows * cols,
            transcendentals=rows * cols,
            bytes_accessed=2 * (rows + cols) * width + 4 * (rows + copies * cols),
        ),
    )(*operands)


def row_kernel(a_ref, parts_ref, base_ref, b_ref, out_ref, *, scale, copies):
    demand = base_ref[...] - merged_lse(parts_ref[...])
    scores = lax.dot_general(
        a_ref[...], b_ref[...], (((1,), (1,)), ((), ())), preferred_element_type=jnp.float32
    )
    logits = scores * scale + demand
    top = jnp.max(logits, axis=1, keepdims=True)
    total = jnp.sum(jnp.exp(logits - top), axis=1, keepdims=True)
    result = top + jnp.log(total)
    wide = jnp.broadcast_to(result, (result.shape[0], 128))
    row = jnp.transpose(wide)[:1, :]
    out_ref[...] = jnp.broadcast_to(row[None], (copies,) + row.shape)


def row_lse(a, b, scale, tile, vmem_limit, parts, base, copies):
    rows, width = a.shape
    cols = b.shape[0]
    tile = min(tile, rows)
    return pl.pallas_call(
        functools.partial(row_kernel, scale=scale, copies=copies),
        out_shape=jax.ShapeDtypeStruct((copies, 1, rows), jnp.float32),
        grid=(rows // tile,),
        in_specs=[
            pl.BlockSpec((tile, width), lambda i: (i, 0)),
            pl.BlockSpec(parts.shape, lambda i: (0, 0, 0)),
            pl.BlockSpec((1, cols), lambda i: (0, 0)),
            pl.BlockSpec((cols, width), lambda i: (0, 0)),
        ],
        out_specs=pl.BlockSpec((copies, 1, tile), lambda i: (0, 0, i)),
        compiler_params=pltpu.CompilerParams(vmem_limit_bytes=vmem_limit),
        cost_estimate=pl.CostEstimate(
            flops=2 * rows * cols * width + 5 * rows * cols,
            transcendentals=rows * cols,
            bytes_accessed=2 * (rows + cols) * width + 4 * (rows + 9 * cols),
        ),
    )(a, parts, base.reshape(1, cols), b)


def assign_kernel(
    rot_ref, v_ref, r_ref, parts_ref, base_ref, f_hbm, out_ref, f_ref, sem, *, scale
):
    fetch = pltpu.make_async_copy(f_hbm, f_ref, sem)
    fetch.start()
    demand = base_ref[...] - merged_lse(parts_ref[...])
    scores = lax.dot_general(
        v_ref[...], r_ref[...], (((1,), (1,)), ((), ())), preferred_element_type=jnp.float32
    )
    logits = scores * scale + demand
    top = jnp.max(logits, axis=1, keepdims=True)
    powers = jnp.exp(logits - top)
    mass = jnp.sum(powers, axis=1, keepdims=True)
    feat = f_ref.shape[1]
    fetch.wait()
    block_feat = jnp.dot(
        powers.astype(jnp.bfloat16), f_ref[...], preferred_element_type=jnp.float32
    )
    out_ref[:feat, :] = block_feat.T
    lane = lax.broadcasted_iota(jnp.int32, (top.shape[0], 128), 1)
    extra = jnp.where(lane == 0, mass, jnp.where(lane == 1, top, 0.0))
    out_ref[feat:, :] = extra.T[:8, :]


def assign_chunk(v, r, parts, base, f, scale, chunk, index):
    rows, width = v.shape
    cols, feat = f.shape
    grid_spec = pltpu.PrefetchScalarGridSpec(
        num_scalar_prefetch=1,
        grid=(1,),
        in_specs=[
            pl.BlockSpec((chunk, width), lambda i, at: (at[0], 0)),
            pl.BlockSpec((cols, width), lambda i, at: (0, 0)),
            pl.BlockSpec(parts.shape, lambda i, at: (0, 0, 0)),
            pl.BlockSpec((1, cols), lambda i, at: (0, 0)),
            pl.BlockSpec(memory_space=pl.ANY),
        ],
        out_specs=pl.BlockSpec((feat + 8, chunk), lambda i, at: (0, 0)),
        scratch_shapes=[pltpu.VMEM((cols, feat), f.dtype), pltpu.SemaphoreType.DMA(())],
    )
    return pl.pallas_call(
        functools.partial(assign_kernel, scale=scale),
        out_shape=jax.ShapeDtypeStruct((feat + 8, chunk), jnp.float32),
        grid_spec=grid_spec,
        compiler_params=pltpu.CompilerParams(vmem_limit_bytes=24 * 1024 * 1024),
        cost_estimate=pl.CostEstimate(
            flops=2 * chunk * cols * (width + feat) + 5 * chunk * cols,
            transcendentals=chunk * cols,
            bytes_accessed=2 * (chunk + cols) * width + 2 * cols * feat + 4 * chunk * (feat + 8),
        ),
    )(index, v, r, parts, base.reshape(1, cols), f)


def combine_kernel(*refs):
    piece_refs, out_ref = refs[:-1], refs[-1]
    feat = out_ref.shape[1]
    peaks = [ref[feat + 1 : feat + 2, :] for ref in piece_refs]
    top = peaks[0]
    for peak in peaks[1:]:
        top = jnp.maximum(top, peak)
    numerator = None
    denominator = None
    for ref, peak in zip(piece_refs, peaks):
        factor = jnp.exp(peak - top)
        term = ref[:feat, :] * factor
        mass = ref[feat : feat + 1, :] * factor
        numerator = term if numerator is None else numerator + term
        denominator = mass if denominator is None else denominator + mass
    out_ref[...] = (numerator / denominator).T


def combine(pieces, feat):
    chunk = pieces[0].shape[1]
    width = min(128, chunk)
    return pl.pallas_call(
        combine_kernel,
        out_shape=jax.ShapeDtypeStruct((chunk, feat), jnp.float32),
        grid=(chunk // width,),
        in_specs=[pl.BlockSpec((feat + 8, width), lambda j: (0, j)) for piece in pieces],
        out_specs=pl.BlockSpec((width, feat), lambda j: (j, 0)),
        cost_estimate=pl.CostEstimate(
            flops=3 * len(pieces) * chunk * feat,
            transcendentals=len(pieces) * chunk,
            bytes_accessed=4 * chunk * ((feat + 8) * len(pieces) + feat),
        ),
    )(*pieces)


def local(vehicle_emb, request_emb, request_feat, log_supply, log_demand):
    own_rows = lax.all_gather(vehicle_emb, "req", axis=0, tiled=True)
    row_count = own_rows.shape[0]
    scale = 3.0 / math.sqrt(own_rows.shape[1])
    spread = lax.axis_size("veh")

    def exchange(block):
        return lax.all_to_all(block, "veh", 0, 0, tiled=True)

    first = exchange(lse_over_rows(own_rows, request_emb, scale, 4096, spread, 24 << 20))
    partial = row_lse(
        own_rows, request_emb, scale, 1024, 48 << 20, first, log_demand, lax.axis_size("req")
    )
    row_parts = lax.all_to_all(partial, "req", 0, 0, tiled=True)
    second = exchange(
        lse_over_rows(own_rows, request_emb, scale, 4096, spread, 24 << 20, row_parts, log_supply)
    )

    owners = lax.axis_size("req")
    chunk = row_count // owners
    me = lax.axis_index("req")
    feat = request_feat.shape[1]
    if owners & (owners - 1) == 0:
        order = [(step, lambda i, m=step: i ^ m) for step in list(range(2, owners)) + [1]]
    else:
        order = [(step, lambda i, m=step: (i + m) % owners) for step in range(1, owners)]
    pieces = []
    for step, partner in order + [(0, None)]:
        index = jnp.reshape(partner(me) if step else me, (1,)).astype(jnp.int32)
        piece = assign_chunk(
            own_rows, request_emb, second, log_demand, request_feat, scale, chunk, index
        )
        if step:
            piece = lax.ppermute(piece, "req", [(i, partner(i)) for i in range(owners)])
        pieces.append(piece)
    arrived = jnp.stack(pieces)
    peaks = arrived[:, feat + 1, :]
    masses = arrived[:, feat, :]
    factor = jnp.exp(peaks - jnp.max(peaks, axis=0, keepdims=True))
    numerator = jnp.sum(arrived[:, :feat, :] * factor[:, None, :], axis=0)
    denominator = jnp.sum(masses * factor, axis=0)
    return (numerator / denominator[None, :]).T


def solution(mesh):
    in_specs = (P(("veh", "req"), None), P("req", None), P("req", None), P("veh"), P("req"))
    out_specs = P(("veh", "req"), None)
    return jax.shard_map(local, mesh=mesh, in_specs=in_specs, out_specs=out_specs, check_vma=False)
```

```python
import functools
import math

import jax
import jax.numpy as jnp
from jax import lax
from jax.experimental import pallas as pl
from jax.experimental.pallas import tpu as pltpu
from jax.sharding import PartitionSpec as P


def merged_lse(parts):
    top = jnp.max(parts, axis=0)
    return top + jnp.log(jnp.sum(jnp.exp(parts - top[None]), axis=0))


def lse_kernel(*refs, scale, shifted, copies):
    if shifted:
        a_ref, parts_ref, base_ref, b_ref, out_ref, column_ref = refs

        @pl.when(pl.program_id(0) == 0)
        def _():
            row = base_ref[...] - merged_lse(parts_ref[...])
            wide = jnp.broadcast_to(row, (128, row.shape[1]))
            column_ref[...] = jnp.transpose(wide)[:, :1]

    else:
        a_ref, b_ref, out_ref = refs
    scores = lax.dot_general(
        a_ref[...], b_ref[...], (((1,), (1,)), ((), ())), preferred_element_type=jnp.float32
    )
    logits = scores * scale
    if shifted:
        logits = logits + column_ref[...]
    top = jnp.max(logits, axis=0, keepdims=True)
    total = jnp.sum(jnp.exp(logits - top), axis=0, keepdims=True)
    result = top + jnp.log(total)
    out_ref[...] = jnp.broadcast_to(result[None], (copies,) + result.shape)


def lse_over_rows(a, b, scale, tile, copies, vmem_limit, parts=None, base=None):
    rows, width = a.shape
    cols = b.shape[0]
    tile = min(tile, cols)
    shifted = parts is not None
    in_specs = [pl.BlockSpec((rows, width), lambda j: (0, 0))]
    operands = [a]
    scratch = []
    if shifted:
        in_specs += [
            pl.BlockSpec(parts.shape, lambda j: (0, 0, 0)),
            pl.BlockSpec((1, rows), lambda j: (0, 0)),
        ]
        operands += [parts, base.reshape(1, rows)]
        scratch = [pltpu.VMEM((rows, 1), jnp.float32)]
    in_specs.append(pl.BlockSpec((tile, width), lambda j: (j, 0)))
    operands.append(b)
    return pl.pallas_call(
        functools.partial(lse_kernel, scale=scale, shifted=shifted, copies=copies),
        out_shape=jax.ShapeDtypeStruct((copies, 1, cols), jnp.float32),
        grid=(cols // tile,),
        in_specs=in_specs,
        out_specs=pl.BlockSpec((copies, 1, tile), lambda j: (0, 0, j)),
        scratch_shapes=scratch,
        compiler_params=pltpu.CompilerParams(vmem_limit_bytes=vmem_limit),
        cost_estimate=pl.CostEstimate(
            flops=2 * rows * cols * width + 5 * rows * cols,
            transcendentals=rows * cols,
            bytes_accessed=2 * (rows + cols) * width + 4 * (rows + copies * cols),
        ),
    )(*operands)


def row_kernel(a_ref, parts_ref, base_ref, b_ref, out_ref, *, scale):
    demand = base_ref[...] - merged_lse(parts_ref[...])
    scores = lax.dot_general(
        a_ref[...], b_ref[...], (((1,), (1,)), ((), ())), preferred_element_type=jnp.float32
    )
    logits = scores * scale + demand
    top = jnp.max(logits, axis=1, keepdims=True)
    total = jnp.sum(jnp.exp(logits - top), axis=1, keepdims=True)
    result = top + jnp.log(total)
    wide = jnp.broadcast_to(result, (result.shape[0], 128))
    out_ref[...] = jnp.transpose(wide)[:1, :][None]


def row_lse(a, b, scale, tile, vmem_limit, parts, base):
    rows, width = a.shape
    cols = b.shape[0]
    tile = min(tile, rows)
    return pl.pallas_call(
        functools.partial(row_kernel, scale=scale),
        out_shape=jax.ShapeDtypeStruct((1, 1, rows), jnp.float32),
        grid=(rows // tile,),
        in_specs=[
            pl.BlockSpec((tile, width), lambda i: (i, 0)),
            pl.BlockSpec(parts.shape, lambda i: (0, 0, 0)),
            pl.BlockSpec((1, cols), lambda i: (0, 0)),
            pl.BlockSpec((cols, width), lambda i: (0, 0)),
        ],
        out_specs=pl.BlockSpec((1, 1, tile), lambda i: (0, 0, i)),
        compiler_params=pltpu.CompilerParams(vmem_limit_bytes=vmem_limit),
        cost_estimate=pl.CostEstimate(
            flops=2 * rows * cols * width + 5 * rows * cols,
            transcendentals=rows * cols,
            bytes_accessed=2 * (rows + cols) * width + 4 * (rows + 9 * cols),
        ),
    )(a, parts, base.reshape(1, cols), b)


def assign_kernel(rot_ref, v_ref, r_ref, demand_ref, f_hbm, out_ref, f_ref, sem, *, scale):
    fetch = pltpu.make_async_copy(f_hbm, f_ref, sem)
    fetch.start()
    scores = lax.dot_general(
        v_ref[...], r_ref[...], (((1,), (1,)), ((), ())), preferred_element_type=jnp.float32
    )
    logits = scores * scale + demand_ref[...]
    top = jnp.max(logits, axis=1, keepdims=True)
    powers = jnp.exp(logits - top)
    mass = jnp.sum(powers, axis=1, keepdims=True)
    feat = f_ref.shape[1]
    fetch.wait()
    block_feat = jnp.dot(
        powers.astype(jnp.bfloat16), f_ref[...], preferred_element_type=jnp.float32
    )
    out_ref[:feat, :] = block_feat.T
    lane = lax.broadcasted_iota(jnp.int32, (top.shape[0], 128), 1)
    extra = jnp.where(lane == 0, mass, jnp.where(lane == 1, top, 0.0))
    out_ref[feat:, :] = extra.T[:8, :]


def assign_chunk(v, r, demand, f, scale, chunk, index):
    rows, width = v.shape
    cols, feat = f.shape
    grid_spec = pltpu.PrefetchScalarGridSpec(
        num_scalar_prefetch=1,
        grid=(1,),
        in_specs=[
            pl.BlockSpec((chunk, width), lambda i, at: (at[0], 0)),
            pl.BlockSpec((cols, width), lambda i, at: (0, 0)),
            pl.BlockSpec((1, cols), lambda i, at: (0, 0)),
            pl.BlockSpec(memory_space=pl.ANY),
        ],
        out_specs=pl.BlockSpec((feat + 8, chunk), lambda i, at: (0, 0)),
        scratch_shapes=[pltpu.VMEM((cols, feat), f.dtype), pltpu.SemaphoreType.DMA(())],
    )
    return pl.pallas_call(
        functools.partial(assign_kernel, scale=scale),
        out_shape=jax.ShapeDtypeStruct((feat + 8, chunk), jnp.float32),
        grid_spec=grid_spec,
        compiler_params=pltpu.CompilerParams(vmem_limit_bytes=24 * 1024 * 1024),
        cost_estimate=pl.CostEstimate(
            flops=2 * chunk * cols * (width + feat) + 5 * chunk * cols,
            transcendentals=chunk * cols,
            bytes_accessed=2 * (chunk + cols) * width + 2 * cols * feat + 4 * chunk * (feat + 8),
        ),
    )(index, v, r, demand, f)


def combine_kernel(*refs):
    piece_refs, out_ref = refs[:-1], refs[-1]
    feat = out_ref.shape[1]
    peaks = [ref[feat + 1 : feat + 2, :] for ref in piece_refs]
    top = peaks[0]
    for peak in peaks[1:]:
        top = jnp.maximum(top, peak)
    numerator = None
    denominator = None
    for ref, peak in zip(piece_refs, peaks):
        factor = jnp.exp(peak - top)
        term = ref[:feat, :] * factor
        mass = ref[feat : feat + 1, :] * factor
        numerator = term if numerator is None else numerator + term
        denominator = mass if denominator is None else denominator + mass
    out_ref[...] = (numerator / denominator).T


def combine(pieces, feat):
    chunk = pieces[0].shape[1]
    width = min(128, chunk)
    return pl.pallas_call(
        combine_kernel,
        out_shape=jax.ShapeDtypeStruct((chunk, feat), jnp.float32),
        grid=(chunk // width,),
        in_specs=[pl.BlockSpec((feat + 8, width), lambda j: (0, j)) for piece in pieces],
        out_specs=pl.BlockSpec((width, feat), lambda j: (j, 0)),
        cost_estimate=pl.CostEstimate(
            flops=3 * len(pieces) * chunk * feat,
            transcendentals=len(pieces) * chunk,
            bytes_accessed=4 * chunk * ((feat + 8) * len(pieces) + feat),
        ),
    )(*pieces)


def local(vehicle_emb, request_emb, request_feat, log_supply, log_demand):
    own_rows = lax.all_gather(vehicle_emb, "req", axis=0, tiled=True)
    row_count = own_rows.shape[0]
    scale = 3.0 / math.sqrt(own_rows.shape[1])
    spread = lax.axis_size("veh")

    def exchange(block):
        return lax.all_to_all(block, "veh", 0, 0, tiled=True)

    first = exchange(lse_over_rows(own_rows, request_emb, scale, 4096, spread, 24 << 20))
    partial = row_lse(own_rows, request_emb, scale, 1024, 48 << 20, first, log_demand)
    row_parts = lax.all_gather(partial[0], "req", axis=0, tiled=False)
    second = exchange(
        lse_over_rows(own_rows, request_emb, scale, 4096, spread, 24 << 20, row_parts, log_supply)
    )

    owners = lax.axis_size("req")
    chunk = row_count // owners
    me = lax.axis_index("req")
    feat = request_feat.shape[1]
    if owners & (owners - 1) == 0:
        order = [(step, lambda i, m=step: i ^ m) for step in list(range(2, owners)) + [1]]
    else:
        order = [(step, lambda i, m=step: (i + m) % owners) for step in range(1, owners)]
    demand = log_demand.reshape(1, -1) - merged_lse(second)
    pieces = []
    for step, partner in order + [(0, None)]:
        index = jnp.reshape(partner(me) if step else me, (1,)).astype(jnp.int32)
        piece = assign_chunk(own_rows, request_emb, demand, request_feat, scale, chunk, index)
        if step:
            piece = lax.ppermute(piece, "req", [(i, partner(i)) for i in range(owners)])
        pieces.append(piece)
    arrived = jnp.stack(pieces)
    peaks = arrived[:, feat + 1, :]
    masses = arrived[:, feat, :]
    factor = jnp.exp(peaks - jnp.max(peaks, axis=0, keepdims=True))
    numerator = jnp.sum(arrived[:, :feat, :] * factor[:, None, :], axis=0)
    denominator = jnp.sum(masses * factor, axis=0)
    return (numerator / denominator[None, :]).T


def solution(mesh):
    in_specs = (P(("veh", "req"), None), P("req", None), P("req", None), P("veh"), P("req"))
    out_specs = P(("veh", "req"), None)
    return jax.shard_map(local, mesh=mesh, in_specs=in_specs, out_specs=out_specs, check_vma=False)
```
